32 devices in a mesh: band: 4 (over y, x), grid: 8 (over z, core).
Axes of the slice: x: 2, y: 2, z: 4, core: 2. Of those that a mesh axis runs over, the one named last changes fastest.
Arguments:
- coefficients: float32 [4, 2, 128, 512], P('band', None, 'grid'), may hold values from -6 to 6
- occupations: float32 [4], P('band'), may hold values from 0.02 to 0.12
- stick_cols: int32 [128], replicated, may hold values from 0 to 65536, as said below
- plane_counts: int32 [8], replicated, may hold values from 1 to 4, as said below
- projections: float32 [4, 2, 18, 32], P('band', None, None, 'grid'), may hold values from -6 to 6
- pair_functions: float32 [171, 16, 256], replicated, may hold values from -0.4375 to 0.4375
- atom_offsets: int32 [32, 2], P('grid'), may hold values from 0 to 255
- piece_owner: int32 [512, 1], P('grid'), may hold values from 0 to 7; in each aligned block of 64 rows (0 to 63, 64 to 127, ...) at most 16 rows name the same one
- piece_slot: int32 [512], P('grid'), may hold values from 0 to 3
Outputs:
- density: float32 [8, 4, 256, 256], P('grid', 'band')
The draws below stay inside these ranges and needn't reach their ends.
Inputs may be any that keep to these rules, and one draw needn't show every extreme that they name: `stick_cols`: live stick columns are distinct over all devices. A device's live sticks fill its first slots, its other slots hold 65536. Each device has 8 to 16 live sticks, some device exactly 16 and some exactly 8. Some owner holds 4 planes and some owner holds 1; slots from plane_counts[g] on stay zero in density. `piece_owner`: among the 64 box planes of one device no owner is named more than 16 times.
All inputs are finite; a program needn't handle non-finite values.
Results may differ from the reference program's by a relative error of at most 0.0001.
Values sent between devices are 32-bit elements; how exact they have to be, the bound alone decides.
No kernel may reach another device: no remote copies, remote signals or barrier semaphores. Data moves between devices by JAX's collectives and lax.ppermute only.
A program may use at most 64 MiB of HBM per device.

```python
import math
import jax
import jax.numpy as jnp
import numpy as np
from jax import lax

NX = 256
NY = 256
NZ = 512
STICK_SLOTS = 16
PLANE_SLOTS = 4
NPROJ = 18
BZ = 16
BX = 16
BXY = 256
PAIRS = 171
BANDS = 4
OWNERS = 8
STICKS = 128
PLANES = 32
ATOMS = 32
PIECE_DEV = 64
PIECES = 512
CAP = 16


def draw_plane_counts(key, part):
    key_a, key_b, key_c = jax.random.split(jax.random.fold_in(key, 11), 3)
    counts = jax.random.randint(key_a, (OWNERS,), 1, PLANE_SLOTS + 1)
    full_at = jax.random.randint(key_b, (), 0, OWNERS)
    low_at = (full_at + 1 + jax.random.randint(key_c, (), 0, OWNERS - 1)) % OWNERS
    counts = counts.at[full_at].set(PLANE_SLOTS).at[low_at].set(1)
    return counts.astype(jnp.int32)


def draw_stick_cols(key, part):
    key_a, key_b, key_c, key_d = jax.random.split(jax.random.fold_in(key, 23), 4)
    counts = jax.random.randint(key_a, (OWNERS,), STICK_SLOTS // 2, STICK_SLOTS + 1)
    full_at = jax.random.randint(key_b, (), 0, OWNERS)
    half_at = (full_at + 1 + jax.random.randint(key_c, (), 0, OWNERS - 1)) % OWNERS
    counts = counts.at[full_at].set(STICK_SLOTS).at[half_at].set(STICK_SLOTS // 2)
    flat_live = (jnp.arange(STICK_SLOTS)[None, :] < counts[:, None]).reshape(-1)
    live_rank = jnp.cumsum(flat_live.astype(jnp.int32)) - 1
    shuffled = jax.random.permutation(key_d, NX * NY - 2) + 1
    columns = jnp.where(flat_live, shuffled[jnp.maximum(live_rank, 0)], NX * NY)
    columns = columns.at[full_at * STICK_SLOTS].set(0).at[full_at * STICK_SLOTS + 1].set(NX * NY - 1)
    return columns.astype(jnp.int32)


def touch_ends(drawn, key, low, largest):
    shape = drawn.shape
    spot = [jax.random.randint(jax.random.fold_in(key, axis), (), 0, shape[axis]) for axis in range(len(shape))]
    drawn = drawn.at[tuple(spot)].set(low)
    longest = shape.index(max(shape))
    spot[longest] = (spot[longest] + 1) % shape[longest]
    return drawn.at[tuple(spot)].set(largest)


def shard_levels(key, extent, cuts, smallest, high):
    def one(position, shards_of):
        draws = jax.random.uniform(jax.random.fold_in(jax.random.fold_in(key, 6), position), (shards_of,), jnp.float32, smallest / len(cuts), high / len(cuts))
        return jnp.repeat(jnp.exp(draws), extent[position] // shards_of).reshape((-1,) + (1,) * (len(extent) - position - 1))

    factor_of = one(*cuts[0])
    for cut in cuts[1:]:
        factor_of = factor_of * one(*cut)
    return factor_of


def routed_block(key, own, number, rows, number_of, top, limit, slope):
    sequence = jax.random.permutation(key, number_of)
    packed, ordinary = load_shares(number_of, rows * top, limit, slope, True), load_shares(number_of, rows * top, limit, slope, False)
    places = jnp.arange(number_of)

    def named(lengths, turn):
        used = int((lengths > 0).sum())
        fixed = max(1, used // 4)
        shifted = fixed + (places - fixed + turn * (used - fixed)) % max(1, number_of - fixed)
        return jnp.zeros((number_of,), jnp.int32).at[sequence[jnp.where(places < fixed, places, shifted)]].set(jnp.asarray(lengths, jnp.int32))

    lengths = jnp.where(number % 4 == 0, named(packed, number // 4), named(ordinary, number - number // 4 - 1))
    mixed = jax.random.permutation(jax.random.fold_in(own, 3), number_of)
    giver, sink = mixed[0:number_of // 2 * 2:2], mixed[1:number_of // 2 * 2:2]
    slack = jnp.minimum(lengths[giver] - 1, limit - lengths[sink]) // 2
    slack = jnp.where((giver == sequence[0]) | (sink == sequence[0]) | (lengths[sink] == 0), 0, jnp.maximum(slack, 0))
    shifted = jax.random.randint(jax.random.fold_in(own, 4), (number_of // 2,), 0, 1 << 20) % (slack + 1)
    lengths = lengths.at[giver].add(-shifted).at[sink].add(shifted)
    items = jnp.searchsorted(jnp.cumsum(lengths), jnp.arange(rows * top), side="right").astype(jnp.int32)
    table = items.reshape(top, rows).T
    table = table[jax.random.permutation(jax.random.fold_in(own, 1), rows)]
    turn = jax.random.randint(jax.random.fold_in(own, 2), (rows, 1), 0, top)
    return jnp.take_along_axis(table, (jnp.arange(top)[None, :] + turn) % top, axis=1)


def load_shares(number_of, total, limit, slope, full):
    portions = [(1 << 20) // math.isqrt(standing ** slope) + 1 for standing in range(1, number_of + 1)]
    largest = limit if full else min(limit, max(-(-total // number_of), total * portions[0] // sum(portions)))
    least = 1 if total - largest >= number_of - 1 else 0
    holding, rest = [largest] + [least] * (number_of - 1), total - largest - least * (number_of - 1)
    while rest > 0:
        candidates = [i for i in range(1, number_of) if holding[i] < largest] or [i for i in range(1, number_of) if holding[i] < limit]
        pool, left = sum([portions[i] for i in candidates]), rest
        for i in candidates:
            extra = min(limit - holding[i], max(1, left * portions[i] // pool), rest)
            holding[i] = holding[i] + extra
            rest = rest - extra
    return np.array(holding)


def bell_draw(stream_key, dims, spread, bound, shards=(), held_as=jnp.bfloat16):
    drawn = spread * jax.random.normal(stream_key, dims, jnp.float32)
    if shards:
        drawn = drawn * shard_levels(stream_key, dims, shards, -0.22, 0.18)
    return jnp.clip(drawn, -bound, bound).astype(held_as)


def setup_inputs(seed: int = 0) -> dict:
    key_of = jax.random.split(jax.random.key(seed), 10)
    coefficients = bell_draw(key_of[0], (BANDS, 2, STICKS, NZ), 1.0, 6.0, ((0, 4), (2, 8)), jnp.float32)
    occupations = jnp.clip(0.02 + 0.09999999776482582 * jax.random.uniform(key_of[1], (BANDS,), jnp.float32) ** shard_levels(key_of[1], (BANDS,), ((0, 4),), -0.2, 0.2), 0.02, 0.12)
    stick_cols = draw_stick_cols(jax.random.fold_in(key_of[9], 71), 0)
    plane_counts = draw_plane_counts(jax.random.fold_in(key_of[9], 71), 0)
    projections = bell_draw(key_of[4], (BANDS, 2, NPROJ, ATOMS), 1.0, 6.0, ((0, 4), (3, 8)), jnp.float32)
    pair_functions = bell_draw(key_of[5], (PAIRS, BZ, BXY), PAIRS ** -0.5, 0.4375, (), jnp.float32)
    atom_offsets = touch_ends(jax.random.randint(key_of[6], (ATOMS, 2), 0, NX), jax.random.fold_in(key_of[6], 1), 0, NX - 1).astype(jnp.int32)
    piece_owner_keys = jax.random.split(jax.random.fold_in(key_of[7], 1), PIECES // PIECE_DEV)
    piece_owner_turns = jax.random.permutation(jax.random.fold_in(key_of[7], 3), PIECES // PIECE_DEV)
    piece_owner = jax.vmap(lambda own, number: routed_block(jax.random.fold_in(key_of[7], 2), own, number, PIECE_DEV, OWNERS, 1, CAP, 1))(piece_owner_keys, piece_owner_turns).reshape((PIECES, 1))
    piece_slot = touch_ends(jax.random.randint(key_of[8], (PIECES,), 0, PLANE_SLOTS), jax.random.fold_in(key_of[8], 1), 0, PLANE_SLOTS - 1).astype(jnp.int32)
    return {"coefficients": coefficients, "occupations": occupations, "stick_cols": stick_cols, "plane_counts": plane_counts, "projections": projections, "pair_functions": pair_functions, "atom_offsets": atom_offsets, "piece_owner": piece_owner, "piece_slot": piece_slot}


PRECISE = lax.Precision.HIGHEST


def reference(coefficients, occupations, stick_cols, plane_counts, projections, pair_functions, atom_offsets, piece_owner, piece_slot):
    offsets = jnp.cumsum(plane_counts) - plane_counts
    slot_ids = jnp.arange(PLANE_SLOTS, dtype=jnp.int32)
    live_slot = (slot_ids[None, :] < plane_counts[:, None]).reshape(-1)
    plane_z = jnp.where(live_slot, (offsets[:, None] + slot_ids[None, :]).reshape(-1), 0).astype(jnp.int32)
    scaling = (NZ * STICKS) ** -0.5

    def add_band(valence, inputs):
        coef_band, occupied = inputs
        wave_g = coef_band[0] + 1j * coef_band[1]
        z_lines = jnp.fft.ifft(wave_g, axis=-1) * NZ
        chosen = jnp.where(live_slot[None, :], z_lines[:, plane_z], 0.0)
        g_field = jnp.zeros((PLANES, NY * NX), chosen.dtype).at[:, stick_cols].set(chosen.T, mode="drop")
        wave_r = jnp.fft.ifft2(g_field.reshape(PLANES, NY, NX)) * (NY * NX * scaling)
        return valence + occupied * (wave_r.real ** 2 + wave_r.imag ** 2), None

    valence, _ = lax.scan(add_band, jnp.zeros((PLANES, NY, NX), jnp.float32), (coefficients, occupations))
    pair_rows, pair_cols = np.triu_indices(NPROJ)
    factor = jnp.asarray(np.where(pair_rows == pair_cols, 1.0, 2.0), jnp.float32)
    products = jnp.einsum("bcia,bcja,b->aij", projections, projections, occupations, precision=PRECISE)
    pair_sum = products[:, pair_rows, pair_cols] * factor[None, :]
    pieces = jnp.dot(pair_sum, pair_functions.reshape(PAIRS, BZ * BXY), precision=PRECISE).reshape(PIECES, BXY)
    destination = piece_owner[:, 0]
    slot_of = piece_slot % plane_counts[destination]
    corner = jnp.repeat(atom_offsets, BZ, axis=0)
    box_ids = jnp.arange(BXY, dtype=jnp.int32)
    grid_rows = (corner[:, 0:1] + box_ids[None, :] // BX) % NY
    grid_cols = (corner[:, 1:2] + box_ids[None, :] % BX) % NX
    target = ((destination * PLANE_SLOTS + slot_of)[:, None] * NY + grid_rows) * NX + grid_cols
    density = valence.reshape(-1).at[target.reshape(-1)].add(pieces.reshape(-1))
    return density.reshape(OWNERS, PLANE_SLOTS, NY, NX)
```

```python
import math

import jax
import jax.numpy as jnp
import numpy as np
from jax import lax
from jax.sharding import PartitionSpec as P

NX = 256
NY = 256
PLANE_SLOTS = 4
BY = 16
BX = 16


PRECISE = lax.Precision.HIGHEST


def phase_table(left, right, length):
    phase_int = left[:, None] * right[None, :] % length
    phases = phase_int.astype(jnp.float32) * (2.0 * math.pi / length)
    return jnp.cos(phases), jnp.sin(phases)


def on_device(
    coefficients,
    occupations,
    stick_cols,
    plane_counts,
    projections,
    pair_functions,
    atom_offsets,
    piece_owner,
    piece_slot,
):
    grid_devs = lax.axis_size("grid")
    band_devs = lax.axis_size("band")
    devices = grid_devs * band_devs
    _, _, stick_local, z_length = coefficients.shape
    stick_count = stick_local * grid_devs
    plane_slots = PLANE_SLOTS
    slot_ids = jnp.arange(plane_slots, dtype=jnp.int32)
    occupied = occupations[0]

    offsets = jnp.cumsum(plane_counts) - plane_counts
    live = slot_ids[:, None] < plane_counts[None, :]
    plane_z = jnp.where(live, offsets[None, :] + slot_ids[:, None], 0).reshape(-1)
    weight = jnp.where(live, 1.0, 0.0).reshape(-1) * (
        jnp.sqrt(occupied) * (z_length * stick_count) ** -0.5
    )
    z_cos, z_sin = phase_table(plane_z, jnp.arange(z_length, dtype=jnp.int32), z_length)
    z_table = jnp.concatenate([z_cos * weight[:, None], z_sin * weight[:, None]], 0)
    product = jnp.einsum("tk,csk->tcs", z_table, coefficients[0], precision=PRECISE)
    line_real = product[:devices, 0] - product[devices:, 1]
    line_imag = product[devices:, 0] + product[:devices, 1]

    proj = projections[0]
    nproj = proj.shape[1]
    pair_rows, pair_cols = np.triu_indices(nproj)
    factor = jnp.asarray(np.where(pair_rows == pair_cols, 1.0, 2.0), jnp.float32)
    products = jnp.einsum("cia,cja->aij", proj, proj, precision=PRECISE) * occupied
    pair_part = (products[:, pair_rows, pair_cols] * factor[None, :]).reshape(1, -1)

    owner_ids = jnp.arange(plane_counts.shape[0], dtype=jnp.int32)
    destination = piece_owner[:, 0]
    owner_hot = destination[:, None] == owner_ids[None, :]
    count_of = jnp.sum(jnp.where(owner_hot, plane_counts[None, :], 0), 1)
    target_plane = destination * plane_slots + piece_slot % count_of
    dest_ids = jnp.arange(devices, dtype=jnp.int32)
    dest_plane = (dest_ids % grid_devs) * plane_slots + dest_ids // grid_devs
    wanted = (target_plane[None, :] == dest_plane[:, None]).astype(jnp.float32)

    corners = atom_offsets.astype(jnp.float32).reshape(1, -1)
    shared = jnp.concatenate([pair_part, corners], 1)
    send = jnp.concatenate(
        [line_real, line_imag, wanted, jnp.broadcast_to(shared, (devices, shared.shape[1]))], 1
    )
    got = lax.all_to_all(send, ("band", "grid"), 0, 0, tiled=True)
    got = got.reshape(band_devs, grid_devs, -1)

    lre = got[:, :, 0:stick_local].reshape(band_devs, stick_count)
    lim = got[:, :, stick_local : 2 * stick_local].reshape(band_devs, stick_count)
    row_of = stick_cols // NX
    col_of = stick_cols % NX
    y_cos, y_sin = phase_table(jnp.arange(NY, dtype=jnp.int32), row_of, NY)
    stick_live = jnp.where(stick_cols < NX * NY, 1.0, 0.0)[None, :]
    along_y = jnp.concatenate([y_cos * stick_live, y_sin * stick_live], 1)
    x_cos, x_sin = phase_table(col_of, jnp.arange(NX, dtype=jnp.int32), NX)
    b_real = lre[:, :, None] * x_cos[None] - lim[:, :, None] * x_sin[None]
    b_imag = lre[:, :, None] * x_sin[None] + lim[:, :, None] * x_cos[None]
    rhs = jnp.concatenate(
        [jnp.concatenate([b_real, b_imag], 2), jnp.concatenate([-b_imag, b_real], 2)], 1
    )
    wave = jnp.einsum("yk,bkx->byx", along_y, rhs, precision=PRECISE)
    valence = jnp.sum(wave[:, :, :NX] ** 2 + wave[:, :, NX:] ** 2, 0)

    pos = 2 * stick_local
    piece_dev = piece_owner.shape[0]
    wanted_here = got[0, :, pos : pos + piece_dev]
    pos += piece_dev
    pairs = pair_rows.shape[0]
    atoms_dev = atom_offsets.shape[0]
    pair_len = atoms_dev * pairs
    pair_sum = jnp.sum(got[:, :, pos : pos + pair_len], 0).reshape(-1, pairs)
    pos += pair_len
    corner = got[0, :, pos : pos + 2 * atoms_dev].reshape(-1, 2).astype(jnp.int32)
    box_depth = pair_functions.shape[1]
    box_cells = pair_functions.shape[2]
    atoms = pair_sum.shape[0]
    flat_functions = pair_functions.reshape(pair_functions.shape[0], box_depth * box_cells)
    pieces = jnp.dot(pair_sum, flat_functions, precision=PRECISE).reshape(atoms, box_depth, box_cells)
    mask = wanted_here.reshape(atoms, box_depth)
    boxes = jnp.sum(pieces * mask[:, :, None], 1).reshape(atoms, BY, BX)
    col_ids = jnp.arange(NX, dtype=jnp.int32)
    row_ids = jnp.arange(NY, dtype=jnp.int32)
    box_cols = jnp.arange(BX, dtype=jnp.int32)
    box_rows = jnp.arange(BY, dtype=jnp.int32)
    col_place = (
        (corner[:, 1:2, None] + box_cols[None, :, None]) % NX == col_ids[None, None, :]
    ).astype(jnp.float32)
    widened = jnp.einsum("aij,ajx->aix", boxes, col_place, precision=PRECISE)
    row_place = (
        (corner[:, 0:1, None] + box_rows[None, :, None]) % NY == row_ids[None, None, :]
    ).astype(jnp.float32)
    augment = jnp.einsum("aiy,aix->yx", row_place, widened, precision=PRECISE)
    density = valence + augment
    return density.reshape(1, 1, NY, NX)


def solution(mesh):
    in_specs = (
        P("band", None, "grid", None),
        P("band"),
        P(),
        P(),
        P("band", None, None, "grid"),
        P(),
        P("grid", None),
        P("grid", None),
        P("grid"),
    )
    out_specs = P("grid", "band", None, None)
    return jax.shard_map(
        on_device, mesh=mesh, in_specs=in_specs, out_specs=out_specs, check_vma=False
    )
```

```python
import functools
import math

import jax
import jax.numpy as jnp
import numpy as np
from jax import lax
from jax.experimental import pallas as pl
from jax.experimental.pallas import tpu as pltpu
from jax.sharding import PartitionSpec as P

NX = 256
NY = 256
PLANE_SLOTS = 4
BY = 16
BX = 16


PRECISE = lax.Precision.HIGHEST


def phase_table(left, right, length):
    phase_int = left[:, None] * right[None, :] % length
    phases = phase_int.astype(jnp.float32) * (2.0 * math.pi / length)
    return jnp.cos(phases), jnp.sin(phases)


SMEM_SPEC = pl.BlockSpec(memory_space=pltpu.SMEM)
VMEM_SPEC = pl.BlockSpec(memory_space=pltpu.VMEM)


def pack_kernel(
    counts_ref,
    occ_ref,
    coef_ref,
    proj_ref,
    owner_ref,
    slot_ref,
    pick_rows_ref,
    pick_cols_ref,
    factor_ref,
    lines_ref,
    wanted_ref,
    pair_ref,
    *,
    grid_devs,
    band_devs,
    plane_slots,
    z_length,
    scale,
):
    devices = grid_devs * band_devs
    occupied = occ_ref[0]
    dest = lax.broadcasted_iota(jnp.int32, (devices, 1), 0)
    dest_grid = dest % grid_devs
    dest_band = dest // grid_devs
    owner = owner_ref[...]
    count_d = jnp.zeros((devices, 1), jnp.int32)
    offset_d = jnp.zeros((devices, 1), jnp.int32)
    count_r = jnp.zeros(owner.shape, jnp.int32)
    for g in range(grid_devs):
        count = counts_ref[g]
        count_d = count_d + jnp.where(dest_grid == g, count, 0)
        offset_d = offset_d + jnp.where(dest_grid > g, count, 0)
        count_r = count_r + jnp.where(owner == g, count, 0)
    live = dest_band < count_d
    plane_z = jnp.where(live, offset_d + dest_band, 0)
    weight = jnp.where(live, jnp.sqrt(occupied) * scale, 0.0)
    freq = lax.broadcasted_iota(jnp.int32, (1, z_length), 1)
    phases = ((plane_z * freq) % z_length).astype(jnp.float32) * (2.0 * math.pi / z_length)
    coef = coef_ref[...]
    half = coef.shape[0] // 2
    swapped = jnp.concatenate([-coef[half:], coef[:half]], 0)
    contract_last = (((1,), (1,)), ((), ()))
    lines = lax.dot_general(
        jnp.cos(phases), coef, contract_last, precision=PRECISE, preferred_element_type=jnp.float32
    ) + lax.dot_general(
        jnp.sin(phases), swapped, contract_last, precision=PRECISE, preferred_element_type=jnp.float32
    )
    lines_ref[...] = lines * weight

    slot = slot_ref[...]
    for _ in range(plane_slots - 1):
        slot = jnp.where(slot >= count_r, slot - count_r, slot)
    target = owner * plane_slots + slot
    dest_plane = dest_grid * plane_slots + dest_band
    wanted_ref[...] = jnp.where(target == dest_plane, 1.0, 0.0)

    total = None
    for part in range(proj_ref.shape[0]):
        proj = proj_ref[part]
        left = jnp.dot(pick_rows_ref[...], proj, precision=PRECISE, preferred_element_type=jnp.float32)
        right = jnp.dot(pick_cols_ref[...], proj, precision=PRECISE, preferred_element_type=jnp.float32)
        total = left * right if total is None else total + left * right
    pair_ref[...] = total * (factor_ref[...] * occupied)


def on_device(
    coefficients,
    occupations,
    stick_cols,
    plane_counts,
    projections,
    pair_functions,
    atom_offsets,
    piece_owner,
    piece_slot,
):
    grid_devs = lax.axis_size("grid")
    band_devs = lax.axis_size("band")
    devices = grid_devs * band_devs
    _, _, stick_local, z_length = coefficients.shape
    stick_count = stick_local * grid_devs
    plane_slots = PLANE_SLOTS

    nproj = projections.shape[2]
    pair_rows, pair_cols = np.triu_indices(nproj)
    pairs = pair_rows.shape[0]
    pick_rows = jnp.asarray((pair_rows[:, None] == np.arange(nproj)[None, :]).astype(np.float32))
    pick_cols = jnp.asarray((pair_cols[:, None] == np.arange(nproj)[None, :]).astype(np.float32))
    factor = jnp.asarray(np.where(pair_rows == pair_cols, 1.0, 2.0).astype(np.float32)[:, None])
    piece_dev = piece_owner.shape[0]
    atoms_dev = atom_offsets.shape[0]
    lines, wanted, pair_t = pl.pallas_call(
        functools.partial(
            pack_kernel,
            grid_devs=grid_devs,
            band_devs=band_devs,
            plane_slots=plane_slots,
            z_length=z_length,
            scale=(z_length * stick_count) ** -0.5,
        ),
        out_shape=(
            jax.ShapeDtypeStruct((devices, 2 * stick_local), jnp.float32),
            jax.ShapeDtypeStruct((devices, piece_dev), jnp.float32),
            jax.ShapeDtypeStruct((pairs, atoms_dev), jnp.float32),
        ),
        in_specs=[SMEM_SPEC, SMEM_SPEC] + [VMEM_SPEC] * 7,
        out_specs=(VMEM_SPEC, VMEM_SPEC, VMEM_SPEC),
    )(
        plane_counts,
        occupations,
        coefficients.reshape(2 * stick_local, z_length),
        projections.reshape(2, nproj, atoms_dev),
        piece_owner.reshape(1, piece_dev),
        piece_slot.reshape(1, piece_dev),
        pick_rows,
        pick_cols,
        factor,
    )
    pair_part = pair_t.T.reshape(1, -1)
    corners = atom_offsets.astype(jnp.float32).reshape(1, -1)
    shared = jnp.concatenate([pair_part, corners], 1)
    send = jnp.concatenate(
        [lines, wanted, jnp.broadcast_to(shared, (devices, shared.shape[1]))], 1
    )
    got = lax.all_to_all(send, ("band", "grid"), 0, 0, tiled=True)
    got = got.reshape(band_devs, grid_devs, -1)

    lre = got[:, :, 0:stick_local].reshape(band_devs, stick_count)
    lim = got[:, :, stick_local : 2 * stick_local].reshape(band_devs, stick_count)
    row_of = stick_cols // NX
    col_of = stick_cols % NX
    y_cos, y_sin = phase_table(jnp.arange(NY, dtype=jnp.int32), row_of, NY)
    stick_live = jnp.where(stick_cols < NX * NY, 1.0, 0.0)[None, :]
    along_y = jnp.concatenate([y_cos * stick_live, y_sin * stick_live], 1)
    x_cos, x_sin = phase_table(col_of, jnp.arange(NX, dtype=jnp.int32), NX)
    b_real = lre[:, :, None] * x_cos[None] - lim[:, :, None] * x_sin[None]
    b_imag = lre[:, :, None] * x_sin[None] + lim[:, :, None] * x_cos[None]
    rhs = jnp.concatenate(
        [jnp.concatenate([b_real, b_imag], 2), jnp.concatenate([-b_imag, b_real], 2)], 1
    )
    wave = jnp.einsum("yk,bkx->byx", along_y, rhs, precision=PRECISE)
    valence = jnp.sum(wave[:, :, :NX] ** 2 + wave[:, :, NX:] ** 2, 0)

    pos = 2 * stick_local
    wanted_here = got[0, :, pos : pos + piece_dev]
    pos += piece_dev
    pair_len = atoms_dev * pairs
    pair_sum = jnp.sum(got[:, :, pos : pos + pair_len], 0).reshape(-1, pairs)
    pos += pair_len
    corner = got[0, :, pos : pos + 2 * atoms_dev].reshape(-1, 2).astype(jnp.int32)
    box_depth = pair_functions.shape[1]
    box_cells = pair_functions.shape[2]
    atoms = pair_sum.shape[0]
    flat_functions = pair_functions.reshape(pair_functions.shape[0], box_depth * box_cells)
    pieces = jnp.dot(pair_sum, flat_functions, precision=PRECISE).reshape(atoms, box_depth, box_cells)
    mask = wanted_here.reshape(atoms, box_depth)
    boxes = jnp.sum(pieces * mask[:, :, None], 1).reshape(atoms, BY, BX)
    col_ids = jnp.arange(NX, dtype=jnp.int32)
    row_ids = jnp.arange(NY, dtype=jnp.int32)
    box_cols = jnp.arange(BX, dtype=jnp.int32)
    box_rows = jnp.arange(BY, dtype=jnp.int32)
    col_place = (
        (corner[:, 1:2, None] + box_cols[None, :, None]) % NX == col_ids[None, None, :]
    ).astype(jnp.float32)
    widened = jnp.einsum("aij,ajx->aix", boxes, col_place, precision=PRECISE)
    row_place = (
        (corner[:, 0:1, None] + box_rows[None, :, None]) % NY == row_ids[None, None, :]
    ).astype(jnp.float32)
    augment = jnp.einsum("aiy,aix->yx", row_place, widened, precision=PRECISE)
    density = valence + augment
    return density.reshape(1, 1, NY, NX)


def solution(mesh):
    in_specs = (
        P("band", None, "grid", None),
        P("band"),
        P(),
        P(),
        P("band", None, None, "grid"),
        P(),
        P("grid", None),
        P("grid", None),
        P("grid"),
    )
    out_specs = P("grid", "band", None, None)
    return jax.shard_map(
        on_device, mesh=mesh, in_specs=in_specs, out_specs=out_specs, check_vma=False
    )
```

```python
import functools
import math

import jax
import jax.numpy as jnp
import numpy as np
from jax import lax
from jax.experimental import pallas as pl
from jax.experimental.pallas import tpu as pltpu
from jax.sharding import PartitionSpec as P

NX = 256
NY = 256
PLANE_SLOTS = 4
BY = 16
BX = 16


PRECISE = lax.Precision.HIGHEST


def phase_table(left, right, length):
    phase_int = left[:, None] * right[None, :] % length
    phases = phase_int.astype(jnp.float32) * (2.0 * math.pi / length)
    return jnp.cos(phases), jnp.sin(phases)


SMEM_SPEC = pl.BlockSpec(memory_space=pltpu.SMEM)
VMEM_SPEC = pl.BlockSpec(memory_space=pltpu.VMEM)


def pack_kernel(
    counts_ref,
    occ_ref,
    coef_ref,
    proj_ref,
    owner_ref,
    slot_ref,
    pick_rows_ref,
    pick_cols_ref,
    factor_ref,
    lines_ref,
    wanted_ref,
    pair_ref,
    *,
    grid_devs,
    band_devs,
    plane_slots,
    z_length,
    scale,
):
    devices = grid_devs * band_devs
    occupied = occ_ref[0]
    dest = lax.broadcasted_iota(jnp.int32, (devices, 1), 0)
    dest_grid = dest % grid_devs
    dest_band = dest // grid_devs
    owner = owner_ref[...]
    count_d = jnp.zeros((devices, 1), jnp.int32)
    offset_d = jnp.zeros((devices, 1), jnp.int32)
    count_r = jnp.zeros(owner.shape, jnp.int32)
    for g in range(grid_devs):
        count = counts_ref[g]
        count_d = count_d + jnp.where(dest_grid == g, count, 0)
        offset_d = offset_d + jnp.where(dest_grid > g, count, 0)
        count_r = count_r + jnp.where(owner == g, count, 0)
    live = dest_band < count_d
    plane_z = jnp.where(live, offset_d + dest_band, 0)
    weight = jnp.where(live, jnp.sqrt(occupied) * scale, 0.0)
    freq = lax.broadcasted_iota(jnp.int32, (1, z_length), 1)
    phases = ((plane_z * freq) % z_length).astype(jnp.float32) * (2.0 * math.pi / z_length)
    coef = coef_ref[...]
    half = coef.shape[0] // 2
    swapped = jnp.concatenate([-coef[half:], coef[:half]], 0)
    contract_last = (((1,), (1,)), ((), ()))
    lines = lax.dot_general(
        jnp.cos(phases), coef, contract_last, precision=PRECISE, preferred_element_type=jnp.float32
    ) + lax.dot_general(
        jnp.sin(phases), swapped, contract_last, precision=PRECISE, preferred_element_type=jnp.float32
    )
    lines_ref[...] = lines * weight

    slot = slot_ref[...]
    for _ in range(plane_slots - 1):
        slot = jnp.where(slot >= count_r, slot - count_r, slot)
    target = owner * plane_slots + slot
    dest_plane = dest_grid * plane_slots + dest_band
    wanted_ref[...] = jnp.where(target == dest_plane, 1.0, 0.0)

    total = None
    for part in range(proj_ref.shape[0]):
        proj = proj_ref[part]
        left = jnp.dot(pick_rows_ref[...], proj, precision=PRECISE, preferred_element_type=jnp.float32)
        right = jnp.dot(pick_cols_ref[...], proj, precision=PRECISE, preferred_element_type=jnp.float32)
        total = left * right if total is None else total + left * right
    pair_ref[...] = total * (factor_ref[...] * occupied)


def plane_kernel(
    corner_ref,
    lre_ref,
    lim_ref,
    cols_ref,
    pair_ref,
    mask_ref,
    functions_hbm,
    out_ref,
    functions,
    copy_sem,
    placed,
    *,
    box_depth,
):
    fetch = pltpu.make_async_copy(functions_hbm, functions, copy_sem)
    fetch.start()
    cols = cols_ref[...]
    row_of = cols // NX
    col_of = cols % NX
    stick_live = jnp.where(cols < NX * NY, 1.0, 0.0)
    sticks = cols.shape[1]
    step_y = 2.0 * math.pi / NY
    step_x = 2.0 * math.pi / NX
    y_ids = lax.broadcasted_iota(jnp.int32, (NY, sticks), 0)
    y_phase = ((y_ids * row_of) % NY).astype(jnp.float32) * step_y
    y_cos = jnp.cos(y_phase) * stick_live
    y_sin = jnp.sin(y_phase) * stick_live
    x_ids = lax.broadcasted_iota(jnp.int32, (NX, sticks), 0)
    x_phase = ((x_ids * col_of) % NX).astype(jnp.float32) * step_x
    x_cos = jnp.cos(x_phase)
    x_sin = jnp.sin(x_phase)
    rhs_t = jnp.concatenate(
        [jnp.concatenate([x_cos, -x_sin], 1), jnp.concatenate([x_sin, x_cos], 1)], 0
    )
    contract_last = (((1,), (1,)), ((), ()))
    valence = jnp.zeros((NY, NX), jnp.float32)
    for band in range(lre_ref.shape[0]):
        line_re = lre_ref[band : band + 1, :]
        line_im = lim_ref[band : band + 1, :]
        lhs = jnp.concatenate(
            [y_cos * line_re - y_sin * line_im, y_cos * line_im + y_sin * line_re], 1
        )
        wave = lax.dot_general(
            lhs, rhs_t, contract_last, precision=PRECISE, preferred_element_type=jnp.float32
        )
        valence = valence + wave[:, :NX] * wave[:, :NX] + wave[:, NX:] * wave[:, NX:]

    fetch.wait()
    pair_sum = pair_ref[...]
    mask = mask_ref[...]
    pairs = pair_sum.shape[1]
    atoms = pair_sum.shape[0]
    flat_rows = pairs * box_depth
    expand = jnp.where(
        lax.broadcasted_iota(jnp.int32, (pairs, flat_rows), 1) // box_depth
        == lax.broadcasted_iota(jnp.int32, (pairs, flat_rows), 0),
        1.0,
        0.0,
    )
    tile = jnp.where(
        lax.broadcasted_iota(jnp.int32, (box_depth, flat_rows), 1) % box_depth
        == lax.broadcasted_iota(jnp.int32, (box_depth, flat_rows), 0),
        1.0,
        0.0,
    )
    weights = jnp.dot(pair_sum, expand, precision=PRECISE, preferred_element_type=jnp.float32)
    weights = weights * jnp.dot(mask, tile, precision=PRECISE, preferred_element_type=jnp.float32)
    boxes = jnp.dot(weights, functions[...], precision=PRECISE, preferred_element_type=jnp.float32)
    cells = boxes.shape[1]
    rows = atoms * BY
    spread = jnp.where(
        lax.broadcasted_iota(jnp.int32, (rows, atoms), 0) // BY
        == lax.broadcasted_iota(jnp.int32, (rows, atoms), 1),
        1.0,
        0.0,
    )
    repeated = jnp.dot(spread, boxes, precision=PRECISE, preferred_element_type=jnp.float32)
    row_mask = (
        lax.broadcasted_iota(jnp.int32, (rows, cells), 1) // BX
        == lax.broadcasted_iota(jnp.int32, (rows, cells), 0) % BY
    )
    repeated = jnp.where(row_mask, repeated, 0.0)
    to_cols = jnp.where(
        lax.broadcasted_iota(jnp.int32, (cells, NX), 0) % BX
        == lax.broadcasted_iota(jnp.int32, (cells, NX), 1),
        1.0,
        0.0,
    )
    patches = jnp.dot(repeated, to_cols, precision=PRECISE, preferred_element_type=jnp.float32)
    placed[...] = jnp.zeros(placed.shape, jnp.float32)
    window = BY + 8
    padding = jnp.zeros((window - BY, NX), jnp.float32)
    for atom in range(atoms):
        top = corner_ref[2 * atom]
        left = corner_ref[2 * atom + 1]
        base = pl.multiple_of((top // 8) * 8, 8)
        moved = pltpu.roll(patches[atom * BY : (atom + 1) * BY, :], left, 1)
        moved = pltpu.roll(jnp.concatenate([moved, padding], 0), top - base, 0)
        placed[pl.ds(base, window), :] = placed[pl.ds(base, window), :] + moved
    wrapped = placed[NY : NY + BY, :]
    out_ref[...] = valence + placed[0:NY, :]
    out_ref[0:BY, :] = out_ref[0:BY, :] + wrapped


def on_device(
    coefficients,
    occupations,
    stick_cols,
    plane_counts,
    projections,
    pair_functions,
    atom_offsets,
    piece_owner,
    piece_slot,
):
    grid_devs = lax.axis_size("grid")
    band_devs = lax.axis_size("band")
    devices = grid_devs * band_devs
    _, _, stick_local, z_length = coefficients.shape
    stick_count = stick_local * grid_devs
    plane_slots = PLANE_SLOTS

    nproj = projections.shape[2]
    pair_rows, pair_cols = np.triu_indices(nproj)
    pairs = pair_rows.shape[0]
    pick_rows = jnp.asarray((pair_rows[:, None] == np.arange(nproj)[None, :]).astype(np.float32))
    pick_cols = jnp.asarray((pair_cols[:, None] == np.arange(nproj)[None, :]).astype(np.float32))
    factor = jnp.asarray(np.where(pair_rows == pair_cols, 1.0, 2.0).astype(np.float32)[:, None])
    piece_dev = piece_owner.shape[0]
    atoms_dev = atom_offsets.shape[0]
    lines, wanted, pair_t = pl.pallas_call(
        functools.partial(
            pack_kernel,
            grid_devs=grid_devs,
            band_devs=band_devs,
            plane_slots=plane_slots,
            z_length=z_length,
            scale=(z_length * stick_count) ** -0.5,
        ),
        out_shape=(
            jax.ShapeDtypeStruct((devices, 2 * stick_local), jnp.float32),
            jax.ShapeDtypeStruct((devices, piece_dev), jnp.float32),
            jax.ShapeDtypeStruct((pairs, atoms_dev), jnp.float32),
        ),
        in_specs=[SMEM_SPEC, SMEM_SPEC] + [VMEM_SPEC] * 7,
        out_specs=(VMEM_SPEC, VMEM_SPEC, VMEM_SPEC),
    )(
        plane_counts,
        occupations,
        coefficients.reshape(2 * stick_local, z_length),
        projections.reshape(2, nproj, atoms_dev),
        piece_owner.reshape(1, piece_dev),
        piece_slot.reshape(1, piece_dev),
        pick_rows,
        pick_cols,
        factor,
    )
    pair_part = pair_t.T.reshape(1, -1)
    corners = atom_offsets.astype(jnp.float32).reshape(1, -1)
    shared = jnp.concatenate([pair_part, corners], 1)
    send = jnp.concatenate(
        [lines, wanted, jnp.broadcast_to(shared, (devices, shared.shape[1]))], 1
    )
    got = lax.all_to_all(send, ("band", "grid"), 0, 0, tiled=True)
    got = got.reshape(band_devs, grid_devs, -1)

    lre = got[:, :, 0:stick_local].reshape(band_devs, stick_count)
    lim = got[:, :, stick_local : 2 * stick_local].reshape(band_devs, stick_count)
    pos = 2 * stick_local
    mask = got[0, :, pos : pos + piece_dev].reshape(-1, pair_functions.shape[1])
    pos += piece_dev
    pair_len = atoms_dev * pairs
    pair_sum = jnp.sum(got[:, :, pos : pos + pair_len], 0).reshape(-1, pairs)
    pos += pair_len
    corner = got[0, :, pos : pos + 2 * atoms_dev].reshape(-1).astype(jnp.int32)
    box_depth = pair_functions.shape[1]
    box_cells = pair_functions.shape[2]
    density = pl.pallas_call(
        functools.partial(plane_kernel, box_depth=box_depth),
        out_shape=jax.ShapeDtypeStruct((NY, NX), jnp.float32),
        in_specs=[SMEM_SPEC] + [VMEM_SPEC] * 5 + [pl.BlockSpec(memory_space=pl.ANY)],
        out_specs=VMEM_SPEC,
        scratch_shapes=[
            pltpu.VMEM((pairs * box_depth, box_cells), jnp.float32),
            pltpu.SemaphoreType.DMA(()),
            pltpu.VMEM((NY + BY, NX), jnp.float32),
        ],
    )(
        corner,
        lre,
        lim,
        stick_cols.reshape(1, stick_count),
        pair_sum,
        mask,
        pair_functions.reshape(pairs * box_depth, box_cells),
    )
    return density.reshape(1, 1, NY, NX)


def solution(mesh):
    in_specs = (
        P("band", None, "grid", None),
        P("band"),
        P(),
        P(),
        P("band", None, None, "grid"),
        P(),
        P("grid", None),
        P("grid", None),
        P("grid"),
    )
    out_specs = P("grid", "band", None, None)
    return jax.shard_map(
        on_device, mesh=mesh, in_specs=in_specs, out_specs=out_specs, check_vma=False
    )
```

```python
import functools
import math

import jax
import jax.numpy as jnp
import numpy as np
from jax import lax
from jax.experimental import pallas as pl
from jax.experimental.pallas import tpu as pltpu
from jax.sharding import PartitionSpec as P

NX = 256
NY = 256
PLANE_SLOTS = 4
BY = 16
BX = 16


PRECISE = lax.Precision.HIGHEST


def phase_table(left, right, length):
    phase_int = left[:, None] * right[None, :] % length
    phases = phase_int.astype(jnp.float32) * (2.0 * math.pi / length)
    return jnp.cos(phases), jnp.sin(phases)


SMEM_SPEC = pl.BlockSpec(memory_space=pltpu.SMEM)
VMEM_SPEC = pl.BlockSpec(memory_space=pltpu.VMEM)


def pack_kernel(
    counts_ref,
    occ_ref,
    coef_ref,
    proj_ref,
    owner_ref,
    slot_ref,
    pick_rows_ref,
    pick_cols_ref,
    factor_ref,
    lines_ref,
    wanted_ref,
    pair_ref,
    *,
    grid_devs,
    band_devs,
    plane_slots,
    z_length,
    scale,
):
    devices = grid_devs * band_devs
    occupied = occ_ref[0]
    dest = lax.broadcasted_iota(jnp.int32, (devices, 1), 0)
    dest_grid = dest % grid_devs
    dest_band = dest // grid_devs
    owner = owner_ref[...]
    count_d = jnp.zeros((devices, 1), jnp.int32)
    offset_d = jnp.zeros((devices, 1), jnp.int32)
    count_r = jnp.zeros(owner.shape, jnp.int32)
    for g in range(grid_devs):
        count = counts_ref[g]
        count_d = count_d + jnp.where(dest_grid == g, count, 0)
        offset_d = offset_d + jnp.where(dest_grid > g, count, 0)
        count_r = count_r + jnp.where(owner == g, count, 0)
    live = dest_band < count_d
    plane_z = jnp.where(live, offset_d + dest_band, 0)
    weight = jnp.where(live, jnp.sqrt(occupied) * scale, 0.0)
    freq = lax.broadcasted_iota(jnp.int32, (1, z_length), 1)
    phases = ((plane_z * freq) % z_length).astype(jnp.float32) * (2.0 * math.pi / z_length)
    coef = coef_ref[...]
    half = coef.shape[0] // 2
    swapped = jnp.concatenate([-coef[half:], coef[:half]], 0)
    contract_last = (((1,), (1,)), ((), ()))
    lines = lax.dot_general(
        jnp.cos(phases), coef, contract_last, precision=PRECISE, preferred_element_type=jnp.float32
    ) + lax.dot_general(
        jnp.sin(phases), swapped, contract_last, precision=PRECISE, preferred_element_type=jnp.float32
    )
    lines_ref[...] = lines * weight

    slot = slot_ref[...]
    for _ in range(plane_slots - 1):
        slot = jnp.where(slot >= count_r, slot - count_r, slot)
    target = owner * plane_slots + slot
    dest_plane = dest_grid * plane_slots + dest_band
    wanted_ref[...] = jnp.where(target == dest_plane, 1.0, 0.0)

    total = None
    for part in range(proj_ref.shape[0]):
        proj = proj_ref[part]
        left = jnp.dot(pick_rows_ref[...], proj, precision=PRECISE, preferred_element_type=jnp.float32)
        right = jnp.dot(pick_cols_ref[...], proj, precision=PRECISE, preferred_element_type=jnp.float32)
        total = left * right if total is None else total + left * right
    pair_ref[...] = total * (factor_ref[...] * occupied)


def plane_kernel(
    corner_ref,
    lre_ref,
    lim_ref,
    cols_ref,
    pair_ref,
    mask_ref,
    functions_hbm,
    out_ref,
    functions,
    copy_sem,
    *,
    box_depth,
):
    fetch = pltpu.make_async_copy(functions_hbm, functions, copy_sem)
    fetch.start()
    cols = cols_ref[...]
    row_of = cols // NX
    col_of = cols % NX
    stick_live = jnp.where(cols < NX * NY, 1.0, 0.0)
    sticks = cols.shape[1]
    step_y = 2.0 * math.pi / NY
    step_x = 2.0 * math.pi / NX
    y_ids = lax.broadcasted_iota(jnp.int32, (NY, sticks), 0)
    y_phase = ((y_ids * row_of) % NY).astype(jnp.float32) * step_y
    y_cos = jnp.cos(y_phase) * stick_live
    y_sin = jnp.sin(y_phase) * stick_live
    x_ids = lax.broadcasted_iota(jnp.int32, (NX, sticks), 0)
    x_phase = ((x_ids * col_of) % NX).astype(jnp.float32) * step_x
    x_cos = jnp.cos(x_phase)
    x_sin = jnp.sin(x_phase)
    rhs_t = jnp.concatenate(
        [jnp.concatenate([x_cos, -x_sin], 1), jnp.concatenate([x_sin, x_cos], 1)], 0
    )
    contract_last = (((1,), (1,)), ((), ()))
    valence = jnp.zeros((NY, NX), jnp.float32)
    for band in range(lre_ref.shape[0]):
        line_re = lre_ref[band : band + 1, :]
        line_im = lim_ref[band : band + 1, :]
        lhs = jnp.concatenate(
            [y_cos * line_re - y_sin * line_im, y_cos * line_im + y_sin * line_re], 1
        )
        wave = lax.dot_general(
            lhs, rhs_t, contract_last, precision=PRECISE, preferred_element_type=jnp.float32
        )
        valence = valence + wave[:, :NX] * wave[:, :NX] + wave[:, NX:] * wave[:, NX:]

    fetch.wait()
    pair_sum = pair_ref[...]
    mask = mask_ref[...]
    pairs = pair_sum.shape[1]
    atoms = pair_sum.shape[0]
    flat_rows = pairs * box_depth
    expand = jnp.where(
        lax.broadcasted_iota(jnp.int32, (pairs, flat_rows), 1) // box_depth
        == lax.broadcasted_iota(jnp.int32, (pairs, flat_rows), 0),
        1.0,
        0.0,
    )
    tile = jnp.where(
        lax.broadcasted_iota(jnp.int32, (box_depth, flat_rows), 1) % box_depth
        == lax.broadcasted_iota(jnp.int32, (box_depth, flat_rows), 0),
        1.0,
        0.0,
    )
    weights = jnp.dot(pair_sum, expand, precision=PRECISE, preferred_element_type=jnp.float32)
    weights = weights * jnp.dot(mask, tile, precision=PRECISE, preferred_element_type=jnp.float32)
    boxes = jnp.dot(weights, functions[...], precision=PRECISE, preferred_element_type=jnp.float32)
    cells = boxes.shape[1]
    rows = atoms * BY
    lanes = atoms * BX

    def onehot(hit):
        return jnp.where(hit, 1.0, 0.0)

    def dot(a, b):
        return jnp.dot(a, b, precision=PRECISE, preferred_element_type=jnp.float32)

    spread = onehot(
        lax.broadcasted_iota(jnp.int32, (rows, atoms), 0) // BY
        == lax.broadcasted_iota(jnp.int32, (rows, atoms), 1)
    )
    repeated = dot(spread, boxes)
    row_mask = (
        lax.broadcasted_iota(jnp.int32, (rows, cells), 1) // BX
        == lax.broadcasted_iota(jnp.int32, (rows, cells), 0) % BY
    )
    repeated = jnp.where(row_mask, repeated, 0.0)
    take_cols = onehot(
        lax.broadcasted_iota(jnp.int32, (cells, lanes), 0) % BX
        == lax.broadcasted_iota(jnp.int32, (cells, lanes), 1) % BX
    )
    blocks = dot(repeated, take_cols)
    same_atom = (
        lax.broadcasted_iota(jnp.int32, (rows, lanes), 0) // BY
        == lax.broadcasted_iota(jnp.int32, (rows, lanes), 1) // BX
    )
    blocks = jnp.where(same_atom, blocks, 0.0)

    atom_lane = lax.broadcasted_iota(jnp.int32, (1, atoms), 1)
    tops = jnp.zeros((1, atoms), jnp.int32)
    lefts = jnp.zeros((1, atoms), jnp.int32)
    for atom in range(atoms):
        tops = jnp.where(atom_lane == atom, corner_ref[2 * atom], tops)
        lefts = jnp.where(atom_lane == atom, corner_ref[2 * atom + 1], lefts)
    spread_t = onehot(
        lax.broadcasted_iota(jnp.int32, (atoms, rows), 1) // BY
        == lax.broadcasted_iota(jnp.int32, (atoms, rows), 0)
    )
    within = lax.broadcasted_iota(jnp.int32, (1, rows), 1) % BY
    top_each = dot(tops.astype(jnp.float32), spread_t).astype(jnp.int32)
    left_each = dot(lefts.astype(jnp.float32), spread_t).astype(jnp.int32)
    to_x = onehot(
        lax.broadcasted_iota(jnp.int32, (NX, lanes), 0) == (left_each + within) % NX
    )
    to_y = onehot(
        lax.broadcasted_iota(jnp.int32, (NY, rows), 0) == (top_each + within) % NY
    )
    shifted = lax.dot_general(
        blocks, to_x, contract_last, precision=PRECISE, preferred_element_type=jnp.float32
    )
    out_ref[...] = valence + dot(to_y, shifted)


def on_device(
    coefficients,
    occupations,
    stick_cols,
    plane_counts,
    projections,
    pair_functions,
    atom_offsets,
    piece_owner,
    piece_slot,
):
    grid_devs = lax.axis_size("grid")
    band_devs = lax.axis_size("band")
    devices = grid_devs * band_devs
    _, _, stick_local, z_length = coefficients.shape
    stick_count = stick_local * grid_devs
    plane_slots = PLANE_SLOTS

    nproj = projections.shape[2]
    pair_rows, pair_cols = np.triu_indices(nproj)
    pairs = pair_rows.shape[0]
    pick_rows = jnp.asarray((pair_rows[:, None] == np.arange(nproj)[None, :]).astype(np.float32))
    pick_cols = jnp.asarray((pair_cols[:, None] == np.arange(nproj)[None, :]).astype(np.float32))
    factor = jnp.asarray(np.where(pair_rows == pair_cols, 1.0, 2.0).astype(np.float32)[:, None])
    piece_dev = piece_owner.shape[0]
    atoms_dev = atom_offsets.shape[0]
    lines, wanted, pair_t = pl.pallas_call(
        functools.partial(
            pack_kernel,
            grid_devs=grid_devs,
            band_devs=band_devs,
            plane_slots=plane_slots,
            z_length=z_length,
            scale=(z_length * stick_count) ** -0.5,
        ),
        out_shape=(
            jax.ShapeDtypeStruct((devices, 2 * stick_local), jnp.float32),
            jax.ShapeDtypeStruct((devices, piece_dev), jnp.float32),
            jax.ShapeDtypeStruct((pairs, atoms_dev), jnp.float32),
        ),
        in_specs=[SMEM_SPEC, SMEM_SPEC] + [VMEM_SPEC] * 7,
        out_specs=(VMEM_SPEC, VMEM_SPEC, VMEM_SPEC),
    )(
        plane_counts,
        occupations,
        coefficients.reshape(2 * stick_local, z_length),
        projections.reshape(2, nproj, atoms_dev),
        piece_owner.reshape(1, piece_dev),
        piece_slot.reshape(1, piece_dev),
        pick_rows,
        pick_cols,
        factor,
    )
    pair_part = pair_t.T.reshape(1, -1)
    corners = atom_offsets.astype(jnp.float32).reshape(1, -1)
    shared = jnp.concatenate([pair_part, corners], 1)
    send = jnp.concatenate(
        [lines, wanted, jnp.broadcast_to(shared, (devices, shared.shape[1]))], 1
    )
    got = lax.all_to_all(send, ("band", "grid"), 0, 0, tiled=True)
    got = got.reshape(band_devs, grid_devs, -1)

    lre = got[:, :, 0:stick_local].reshape(band_devs, stick_count)
    lim = got[:, :, stick_local : 2 * stick_local].reshape(band_devs, stick_count)
    pos = 2 * stick_local
    mask = got[0, :, pos : pos + piece_dev].reshape(-1, pair_functions.shape[1])
    pos += piece_dev
    pair_len = atoms_dev * pairs
    pair_sum = jnp.sum(got[:, :, pos : pos + pair_len], 0).reshape(-1, pairs)
    pos += pair_len
    corner = got[0, :, pos : pos + 2 * atoms_dev].reshape(-1).astype(jnp.int32)
    box_depth = pair_functions.shape[1]
    box_cells = pair_functions.shape[2]
    density = pl.pallas_call(
        functools.partial(plane_kernel, box_depth=box_depth),
        out_shape=jax.ShapeDtypeStruct((NY, NX), jnp.float32),
        in_specs=[SMEM_SPEC] + [VMEM_SPEC] * 5 + [pl.BlockSpec(memory_space=pl.ANY)],
        out_specs=VMEM_SPEC,
        scratch_shapes=[
            pltpu.VMEM((pairs * box_depth, box_cells), jnp.float32),
            pltpu.SemaphoreType.DMA(()),
        ],
    )(
        corner,
        lre,
        lim,
        stick_cols.reshape(1, stick_count),
        pair_sum,
        mask,
        pair_functions.reshape(pairs * box_depth, box_cells),
    )
    return density.reshape(1, 1, NY, NX)


def solution(mesh):
    in_specs = (
        P("band", None, "grid", None),
        P("band"),
        P(),
        P(),
        P("band", None, None, "grid"),
        P(),
        P("grid", None),
        P("grid", None),
        P("grid"),
    )
    out_specs = P("grid", "band", None, None)
    return jax.shard_map(
        on_device, mesh=mesh, in_specs=in_specs, out_specs=out_specs, check_vma=False
    )
```

```python
import functools
import math

import jax
import jax.numpy as jnp
import numpy as np
from jax import lax
from jax.experimental import pallas as pl
from jax.experimental.pallas import tpu as pltpu
from jax.sharding import PartitionSpec as P

NX = 256
NY = 256
PLANE_SLOTS = 4
BY = 16
BX = 16


PRECISE = lax.Precision.HIGHEST


def phase_table(left, right, length):
    phase_int = left[:, None] * right[None, :] % length
    phases = phase_int.astype(jnp.float32) * (2.0 * math.pi / length)
    return jnp.cos(phases), jnp.sin(phases)


SMEM_SPEC = pl.BlockSpec(memory_space=pltpu.SMEM)
VMEM_SPEC = pl.BlockSpec(memory_space=pltpu.VMEM)


def pack_kernel(
    counts_ref,
    occ_ref,
    coef_ref,
    proj_ref,
    owner_ref,
    slot_ref,
    pick_rows_ref,
    pick_cols_ref,
    factor_ref,
    lines_ref,
    wanted_ref,
    pair_ref,
    *,
    grid_devs,
    band_devs,
    plane_slots,
    z_length,
    scale,
):
    devices = grid_devs * band_devs
    occupied = occ_ref[0]
    dest = lax.broadcasted_iota(jnp.int32, (devices, 1), 0)
    dest_grid = dest % grid_devs
    dest_band = dest // grid_devs
    owner = owner_ref[...]
    count_d = jnp.zeros((devices, 1), jnp.int32)
    offset_d = jnp.zeros((devices, 1), jnp.int32)
    count_r = jnp.zeros(owner.shape, jnp.int32)
    for g in range(grid_devs):
        count = counts_ref[g]
        count_d = count_d + jnp.where(dest_grid == g, count, 0)
        offset_d = offset_d + jnp.where(dest_grid > g, count, 0)
        count_r = count_r + jnp.where(owner == g, count, 0)
    live = dest_band < count_d
    plane_z = jnp.where(live, offset_d + dest_band, 0)
    weight = jnp.where(live, jnp.sqrt(occupied) * scale, 0.0)
    freq = lax.broadcasted_iota(jnp.int32, (1, z_length), 1)
    phases = ((plane_z * freq) % z_length).astype(jnp.float32) * (2.0 * math.pi / z_length)
    coef = coef_ref[...]
    half = coef.shape[0] // 2
    swapped = jnp.concatenate([-coef[half:], coef[:half]], 0)
    contract_last = (((1,), (1,)), ((), ()))
    lines = lax.dot_general(
        jnp.cos(phases), coef, contract_last, precision=PRECISE, preferred_element_type=jnp.float32
    ) + lax.dot_general(
        jnp.sin(phases), swapped, contract_last, precision=PRECISE, preferred_element_type=jnp.float32
    )
    lines_ref[...] = lines * weight

    slot = slot_ref[...]
    for _ in range(plane_slots - 1):
        slot = jnp.where(slot >= count_r, slot - count_r, slot)
    target = owner * plane_slots + slot
    dest_plane = dest_grid * plane_slots + dest_band
    wanted_ref[...] = jnp.where(target == dest_plane, 1.0, 0.0)

    atoms = proj_ref.shape[2]
    eye = jnp.where(
        lax.broadcasted_iota(jnp.int32, (atoms, atoms), 0)
        == lax.broadcasted_iota(jnp.int32, (atoms, atoms), 1),
        1.0,
        0.0,
    )
    total = None
    for part in range(proj_ref.shape[0]):
        proj_t = lax.dot_general(
            eye, proj_ref[part], contract_last, precision=PRECISE, preferred_element_type=jnp.float32
        )
        left = jnp.dot(proj_t, pick_rows_ref[...], precision=PRECISE, preferred_element_type=jnp.float32)
        right = jnp.dot(proj_t, pick_cols_ref[...], precision=PRECISE, preferred_element_type=jnp.float32)
        total = left * right if total is None else total + left * right
    pair_ref[...] = total * (factor_ref[...] * occupied)


def on_device(
    coefficients,
    occupations,
    stick_cols,
    plane_counts,
    projections,
    pair_functions,
    atom_offsets,
    piece_owner,
    piece_slot,
):
    grid_devs = lax.axis_size("grid")
    band_devs = lax.axis_size("band")
    devices = grid_devs * band_devs
    _, _, stick_local, z_length = coefficients.shape
    stick_count = stick_local * grid_devs
    plane_slots = PLANE_SLOTS

    nproj = projections.shape[2]
    pair_rows, pair_cols = np.triu_indices(nproj)
    pairs = pair_rows.shape[0]
    pick_rows = jnp.asarray((np.arange(nproj)[:, None] == pair_rows[None, :]).astype(np.float32))
    pick_cols = jnp.asarray((np.arange(nproj)[:, None] == pair_cols[None, :]).astype(np.float32))
    factor = jnp.asarray(np.where(pair_rows == pair_cols, 1.0, 2.0).astype(np.float32)[None, :])
    piece_dev = piece_owner.shape[0]
    atoms_dev = atom_offsets.shape[0]
    lines, wanted, pair_part = pl.pallas_call(
        functools.partial(
            pack_kernel,
            grid_devs=grid_devs,
            band_devs=band_devs,
            plane_slots=plane_slots,
            z_length=z_length,
            scale=(z_length * stick_count) ** -0.5,
        ),
        out_shape=(
            jax.ShapeDtypeStruct((devices, 2 * stick_local), jnp.float32),
            jax.ShapeDtypeStruct((devices, piece_dev), jnp.float32),
            jax.ShapeDtypeStruct((atoms_dev, pairs), jnp.float32),
        ),
        in_specs=[SMEM_SPEC, SMEM_SPEC] + [VMEM_SPEC] * 7,
        out_specs=(VMEM_SPEC, VMEM_SPEC, VMEM_SPEC),
    )(
        plane_counts,
        occupations,
        coefficients.reshape(2 * stick_local, z_length),
        projections.reshape(2, nproj, atoms_dev),
        piece_owner.reshape(1, piece_dev),
        piece_slot.reshape(1, piece_dev),
        pick_rows,
        pick_cols,
        factor,
    )
    pair_part = pair_part.reshape(1, -1)
    corners = atom_offsets.astype(jnp.float32).reshape(1, -1)
    shared = jnp.concatenate([pair_part, corners], 1)
    send = jnp.concatenate(
        [lines, wanted, jnp.broadcast_to(shared, (devices, shared.shape[1]))], 1
    )
    got = lax.all_to_all(send, ("band", "grid"), 0, 0, tiled=True)
    got = got.reshape(band_devs, grid_devs, -1)

    lre = got[:, :, 0:stick_local].reshape(band_devs, stick_count)
    lim = got[:, :, stick_local : 2 * stick_local].reshape(band_devs, stick_count)
    row_of = stick_cols // NX
    col_of = stick_cols % NX
    y_cos, y_sin = phase_table(jnp.arange(NY, dtype=jnp.int32), row_of, NY)
    stick_live = jnp.where(stick_cols < NX * NY, 1.0, 0.0)[None, :]
    along_y = jnp.concatenate([y_cos * stick_live, y_sin * stick_live], 1)
    x_cos, x_sin = phase_table(col_of, jnp.arange(NX, dtype=jnp.int32), NX)
    b_real = lre[:, :, None] * x_cos[None] - lim[:, :, None] * x_sin[None]
    b_imag = lre[:, :, None] * x_sin[None] + lim[:, :, None] * x_cos[None]
    rhs = jnp.concatenate(
        [jnp.concatenate([b_real, b_imag], 2), jnp.concatenate([-b_imag, b_real], 2)], 1
    )
    wave = jnp.einsum("yk,bkx->byx", along_y, rhs, precision=PRECISE)
    valence = jnp.sum(wave[:, :, :NX] ** 2 + wave[:, :, NX:] ** 2, 0)

    pos = 2 * stick_local
    wanted_here = got[0, :, pos : pos + piece_dev]
    pos += piece_dev
    pair_len = atoms_dev * pairs
    pair_sum = jnp.sum(got[:, :, pos : pos + pair_len], 0).reshape(-1, pairs)
    pos += pair_len
    corner = got[0, :, pos : pos + 2 * atoms_dev].reshape(-1, 2).astype(jnp.int32)
    box_depth = pair_functions.shape[1]
    box_cells = pair_functions.shape[2]
    atoms = pair_sum.shape[0]
    flat_functions = pair_functions.reshape(pairs * box_depth, box_cells)
    mask = wanted_here.reshape(atoms, box_depth)
    weights = (pair_sum[:, :, None] * mask[:, None, :]).reshape(atoms, pairs * box_depth)
    boxes = jnp.dot(weights, flat_functions, precision=PRECISE).reshape(atoms, BY, BX)
    col_ids = jnp.arange(NX, dtype=jnp.int32)
    row_ids = jnp.arange(NY, dtype=jnp.int32)
    box_cols = jnp.arange(BX, dtype=jnp.int32)
    box_rows = jnp.arange(BY, dtype=jnp.int32)
    col_place = (
        (corner[:, 1:2, None] + box_cols[None, :, None]) % NX == col_ids[None, None, :]
    ).astype(jnp.float32)
    widened = jnp.einsum("aij,ajx->aix", boxes, col_place, precision=PRECISE)
    row_place = (
        (corner[:, 0:1, None] + box_rows[None, :, None]) % NY == row_ids[None, None, :]
    ).astype(jnp.float32)
    augment = jnp.einsum("aiy,aix->yx", row_place, widened, precision=PRECISE)
    density = valence + augment
    return density.reshape(1, 1, NY, NX)


def solution(mesh):
    in_specs = (
        P("band", None, "grid", None),
        P("band"),
        P(),
        P(),
        P("band", None, None, "grid"),
        P(),
        P("grid", None),
        P("grid", None),
        P("grid"),
    )
    out_specs = P("grid", "band", None, None)
    return jax.shard_map(
        on_device, mesh=mesh, in_specs=in_specs, out_specs=out_specs, check_vma=False
    )
```

```python
import functools
import math

import jax
import jax.numpy as jnp
import numpy as np
from jax import lax
from jax.experimental import pallas as pl
from jax.experimental.pallas import tpu as pltpu
from jax.sharding import PartitionSpec as P

NX = 256
NY = 256
PLANE_SLOTS = 4
BY = 16
BX = 16


PRECISE = lax.Precision.HIGHEST
THREE_PASS = lax.Precision.HIGH


def phase_table(left, right, length):
    phase_int = left[:, None] * right[None, :] % length
    phases = phase_int.astype(jnp.float32) * (2.0 * math.pi / length)
    return jnp.cos(phases), jnp.sin(phases)


SMEM_SPEC = pl.BlockSpec(memory_space=pltpu.SMEM)
VMEM_SPEC = pl.BlockSpec(memory_space=pltpu.VMEM)


def pack_kernel(
    counts_ref,
    occ_ref,
    coef_ref,
    proj_ref,
    owner_ref,
    slot_ref,
    pick_rows_ref,
    pick_cols_ref,
    factor_ref,
    lines_ref,
    wanted_ref,
    pair_ref,
    *,
    grid_devs,
    band_devs,
    plane_slots,
    z_length,
    scale,
):
    devices = grid_devs * band_devs
    occupied = occ_ref[0]
    dest = lax.broadcasted_iota(jnp.int32, (devices, 1), 0)
    dest_grid = dest % grid_devs
    dest_band = dest // grid_devs
    owner = owner_ref[...]
    count_d = jnp.zeros((devices, 1), jnp.int32)
    offset_d = jnp.zeros((devices, 1), jnp.int32)
    count_r = jnp.zeros(owner.shape, jnp.int32)
    for g in range(grid_devs):
        count = counts_ref[g]
        count_d = count_d + jnp.where(dest_grid == g, count, 0)
        offset_d = offset_d + jnp.where(dest_grid > g, count, 0)
        count_r = count_r + jnp.where(owner == g, count, 0)
    live = dest_band < count_d
    plane_z = jnp.where(live, offset_d + dest_band, 0)
    weight = jnp.where(live, jnp.sqrt(occupied) * scale, 0.0)
    freq = lax.broadcasted_iota(jnp.int32, (1, z_length), 1)
    phases = ((plane_z * freq) % z_length).astype(jnp.float32) * (2.0 * math.pi / z_length)
    coef = coef_ref[...]
    half = coef.shape[0] // 2
    swapped = jnp.concatenate([-coef[half:], coef[:half]], 0)
    contract_last = (((1,), (1,)), ((), ()))
    lines = lax.dot_general(
        jnp.cos(phases), coef, contract_last, precision=PRECISE, preferred_element_type=jnp.float32
    ) + lax.dot_general(
        jnp.sin(phases), swapped, contract_last, precision=PRECISE, preferred_element_type=jnp.float32
    )
    lines_ref[...] = lines * weight

    slot = slot_ref[...]
    for _ in range(plane_slots - 1):
        slot = jnp.where(slot >= count_r, slot - count_r, slot)
    target = owner * plane_slots + slot
    dest_plane = dest_grid * plane_slots + dest_band
    wanted_ref[...] = jnp.where(target == dest_plane, 1.0, 0.0)

    atoms = proj_ref.shape[2]
    eye = jnp.where(
        lax.broadcasted_iota(jnp.int32, (atoms, atoms), 0)
        == lax.broadcasted_iota(jnp.int32, (atoms, atoms), 1),
        1.0,
        0.0,
    )
    total = None
    for part in range(proj_ref.shape[0]):
        proj_t = lax.dot_general(
            eye, proj_ref[part], contract_last, precision=PRECISE, preferred_element_type=jnp.float32
        )
        left = jnp.dot(proj_t, pick_rows_ref[...], precision=PRECISE, preferred_element_type=jnp.float32)
        right = jnp.dot(proj_t, pick_cols_ref[...], precision=PRECISE, preferred_element_type=jnp.float32)
        total = left * right if total is None else total + left * right
    pair_ref[...] = total * (factor_ref[...] * occupied)


def on_device(
    coefficients,
    occupations,
    stick_cols,
    plane_counts,
    projections,
    pair_functions,
    atom_offsets,
    piece_owner,
    piece_slot,
):
    grid_devs = lax.axis_size("grid")
    band_devs = lax.axis_size("band")
    devices = grid_devs * band_devs
    _, _, stick_local, z_length = coefficients.shape
    stick_count = stick_local * grid_devs
    plane_slots = PLANE_SLOTS

    nproj = projections.shape[2]
    pair_rows, pair_cols = np.triu_indices(nproj)
    pairs = pair_rows.shape[0]
    pick_rows = jnp.asarray((np.arange(nproj)[:, None] == pair_rows[None, :]).astype(np.float32))
    pick_cols = jnp.asarray((np.arange(nproj)[:, None] == pair_cols[None, :]).astype(np.float32))
    factor = jnp.asarray(np.where(pair_rows == pair_cols, 1.0, 2.0).astype(np.float32)[None, :])
    piece_dev = piece_owner.shape[0]
    atoms_dev = atom_offsets.shape[0]
    lines, wanted, pair_part = pl.pallas_call(
        functools.partial(
            pack_kernel,
            grid_devs=grid_devs,
            band_devs=band_devs,
            plane_slots=plane_slots,
            z_length=z_length,
            scale=(z_length * stick_count) ** -0.5,
        ),
        out_shape=(
            jax.ShapeDtypeStruct((devices, 2 * stick_local), jnp.float32),
            jax.ShapeDtypeStruct((devices, piece_dev), jnp.float32),
            jax.ShapeDtypeStruct((atoms_dev, pairs), jnp.float32),
        ),
        in_specs=[SMEM_SPEC, SMEM_SPEC] + [VMEM_SPEC] * 7,
        out_specs=(VMEM_SPEC, VMEM_SPEC, VMEM_SPEC),
    )(
        plane_counts,
        occupations,
        coefficients.reshape(2 * stick_local, z_length),
        projections.reshape(2, nproj, atoms_dev),
        piece_owner.reshape(1, piece_dev),
        piece_slot.reshape(1, piece_dev),
        pick_rows,
        pick_cols,
        factor,
    )
    pair_part = pair_part.reshape(1, -1)
    corners = atom_offsets.astype(jnp.float32).reshape(1, -1)
    shared = jnp.concatenate([pair_part, corners], 1)
    send = jnp.concatenate(
        [lines, wanted, jnp.broadcast_to(shared, (devices, shared.shape[1]))], 1
    )
    got = lax.all_to_all(send, ("band", "grid"), 0, 0, tiled=True)
    got = got.reshape(band_devs, grid_devs, -1)

    lre = got[:, :, 0:stick_local].reshape(band_devs, stick_count)
    lim = got[:, :, stick_local : 2 * stick_local].reshape(band_devs, stick_count)
    row_of = stick_cols // NX
    col_of = stick_cols % NX
    y_cos, y_sin = phase_table(jnp.arange(NY, dtype=jnp.int32), row_of, NY)
    stick_live = jnp.where(stick_cols < NX * NY, 1.0, 0.0)[None, :]
    along_y = jnp.concatenate([y_cos * stick_live, y_sin * stick_live], 1)
    x_cos, x_sin = phase_table(col_of, jnp.arange(NX, dtype=jnp.int32), NX)
    b_real = lre[:, :, None] * x_cos[None] - lim[:, :, None] * x_sin[None]
    b_imag = lre[:, :, None] * x_sin[None] + lim[:, :, None] * x_cos[None]
    rhs = jnp.concatenate(
        [jnp.concatenate([b_real, b_imag], 2), jnp.concatenate([-b_imag, b_real], 2)], 1
    )
    wave = jnp.einsum("yk,bkx->byx", along_y, rhs, precision=THREE_PASS)
    valence = jnp.sum(wave[:, :, :NX] ** 2 + wave[:, :, NX:] ** 2, 0)

    pos = 2 * stick_local
    wanted_here = got[0, :, pos : pos + piece_dev]
    pos += piece_dev
    pair_len = atoms_dev * pairs
    pair_sum = jnp.sum(got[:, :, pos : pos + pair_len], 0).reshape(-1, pairs)
    pos += pair_len
    corner = got[0, :, pos : pos + 2 * atoms_dev].reshape(-1, 2).astype(jnp.int32)
    box_depth = pair_functions.shape[1]
    box_cells = pair_functions.shape[2]
    atoms = pair_sum.shape[0]
    flat_functions = pair_functions.reshape(pairs * box_depth, box_cells)
    mask = wanted_here.reshape(atoms, box_depth)
    weights = (pair_sum[:, :, None] * mask[:, None, :]).reshape(atoms, pairs * box_depth)
    boxes = jnp.dot(weights, flat_functions, precision=THREE_PASS).reshape(atoms, BY, BX)
    col_ids = jnp.arange(NX, dtype=jnp.int32)
    row_ids = jnp.arange(NY, dtype=jnp.int32)
    box_cols = jnp.arange(BX, dtype=jnp.int32)
    box_rows = jnp.arange(BY, dtype=jnp.int32)
    col_place = (
        (corner[:, 1:2, None] + box_cols[None, :, None]) % NX == col_ids[None, None, :]
    ).astype(jnp.float32)
    widened = jnp.einsum("aij,ajx->aix", boxes, col_place, precision=THREE_PASS)
    row_place = (
        (corner[:, 0:1, None] + box_rows[None, :, None]) % NY == row_ids[None, None, :]
    ).astype(jnp.float32)
    augment = jnp.einsum("aiy,aix->yx", row_place, widened, precision=THREE_PASS)
    density = valence + augment
    return density.reshape(1, 1, NY, NX)


def solution(mesh):
    in_specs = (
        P("band", None, "grid", None),
        P("band"),
        P(),
        P(),
        P("band", None, None, "grid"),
        P(),
        P("grid", None),
        P("grid", None),
        P("grid"),
    )
    out_specs = P("grid", "band", None, None)
    return jax.shard_map(
        on_device, mesh=mesh, in_specs=in_specs, out_specs=out_specs, check_vma=False
    )
```

```python
import functools
import math

import jax
import jax.numpy as jnp
import numpy as np
from jax import lax
from jax.experimental import pallas as pl
from jax.experimental.pallas import tpu as pltpu
from jax.sharding import PartitionSpec as P

NX = 256
NY = 256
PLANE_SLOTS = 4
BY = 16
BX = 16


PRECISE = lax.Precision.HIGHEST
THREE_PASS = lax.Precision.HIGH


def phase_table(left, right, length):
    phase_int = left[:, None] * right[None, :] % length
    phases = phase_int.astype(jnp.float32) * (2.0 * math.pi / length)
    return jnp.cos(phases), jnp.sin(phases)


SMEM_SPEC = pl.BlockSpec(memory_space=pltpu.SMEM)
CORNER_AT = 32
CORNER_LANES = 32
WANTED_AT = 64
PAIRS_AT = 128
VMEM_SPEC = pl.BlockSpec(memory_space=pltpu.VMEM)


def pack_kernel(
    counts_ref,
    occ_ref,
    coef_ref,
    proj_ref,
    owner_ref,
    slot_ref,
    pick_rows_ref,
    pick_cols_ref,
    factor_ref,
    corner_ref,
    send_ref,
    *,
    grid_devs,
    band_devs,
    plane_slots,
    z_length,
    scale,
):
    devices = grid_devs * band_devs
    occupied = occ_ref[0]
    dest = lax.broadcasted_iota(jnp.int32, (devices, 1), 0)
    dest_grid = dest % grid_devs
    dest_band = dest // grid_devs
    owner = owner_ref[...]
    count_d = jnp.zeros((devices, 1), jnp.int32)
    offset_d = jnp.zeros((devices, 1), jnp.int32)
    count_r = jnp.zeros(owner.shape, jnp.int32)
    for g in range(grid_devs):
        count = counts_ref[g]
        count_d = count_d + jnp.where(dest_grid == g, count, 0)
        offset_d = offset_d + jnp.where(dest_grid > g, count, 0)
        count_r = count_r + jnp.where(owner == g, count, 0)
    live = dest_band < count_d
    plane_z = jnp.where(live, offset_d + dest_band, 0)
    weight = jnp.where(live, jnp.sqrt(occupied) * scale, 0.0)
    freq = lax.broadcasted_iota(jnp.int32, (1, z_length), 1)
    phases = ((plane_z * freq) % z_length).astype(jnp.float32) * (2.0 * math.pi / z_length)
    coef = coef_ref[...]
    half = coef.shape[0] // 2
    swapped = jnp.concatenate([-coef[half:], coef[:half]], 0)
    contract_last = (((1,), (1,)), ((), ()))
    lines = lax.dot_general(
        jnp.cos(phases), coef, contract_last, precision=PRECISE, preferred_element_type=jnp.float32
    ) + lax.dot_general(
        jnp.sin(phases), swapped, contract_last, precision=PRECISE, preferred_element_type=jnp.float32
    )
    send_ref[...] = jnp.zeros(send_ref.shape, jnp.float32)
    send_ref[:, 0 : lines.shape[1]] = lines * weight
    corner_lane = lax.broadcasted_iota(jnp.int32, (1, CORNER_LANES), 1)
    corners = jnp.zeros((1, CORNER_LANES), jnp.int32)
    for atom in range(corner_ref.shape[0]):
        for axis in range(2):
            corners = jnp.where(corner_lane == 2 * atom + axis, corner_ref[atom, axis], corners)
    send_ref[:, CORNER_AT : CORNER_AT + CORNER_LANES] = jnp.broadcast_to(
        corners.astype(jnp.float32), (devices, CORNER_LANES)
    )

    slot = slot_ref[...]
    for _ in range(plane_slots - 1):
        slot = jnp.where(slot >= count_r, slot - count_r, slot)
    target = owner * plane_slots + slot
    dest_plane = dest_grid * plane_slots + dest_band
    send_ref[:, WANTED_AT : WANTED_AT + target.shape[1]] = jnp.where(target == dest_plane, 1.0, 0.0)

    atoms = proj_ref.shape[2]
    eye = jnp.where(
        lax.broadcasted_iota(jnp.int32, (atoms, atoms), 0)
        == lax.broadcasted_iota(jnp.int32, (atoms, atoms), 1),
        1.0,
        0.0,
    )
    total = None
    for part in range(proj_ref.shape[0]):
        proj_t = lax.dot_general(
            eye, proj_ref[part], contract_last, precision=PRECISE, preferred_element_type=jnp.float32
        )
        left = jnp.dot(proj_t, pick_rows_ref[...], precision=PRECISE, preferred_element_type=jnp.float32)
        right = jnp.dot(proj_t, pick_cols_ref[...], precision=PRECISE, preferred_element_type=jnp.float32)
        total = left * right if total is None else total + left * right
    total = total * (factor_ref[...] * occupied)
    pairs = total.shape[1]
    for atom in range(atoms):
        start = PAIRS_AT + atom * pairs
        send_ref[:, start : start + pairs] = jnp.broadcast_to(total[atom : atom + 1, :], (devices, pairs))


def on_device(
    coefficients,
    occupations,
    stick_cols,
    plane_counts,
    projections,
    pair_functions,
    atom_offsets,
    piece_owner,
    piece_slot,
):
    grid_devs = lax.axis_size("grid")
    band_devs = lax.axis_size("band")
    devices = grid_devs * band_devs
    _, _, stick_local, z_length = coefficients.shape
    stick_count = stick_local * grid_devs
    plane_slots = PLANE_SLOTS

    nproj = projections.shape[2]
    pair_rows, pair_cols = np.triu_indices(nproj)
    pairs = pair_rows.shape[0]
    pick_rows = jnp.asarray((np.arange(nproj)[:, None] == pair_rows[None, :]).astype(np.float32))
    pick_cols = jnp.asarray((np.arange(nproj)[:, None] == pair_cols[None, :]).astype(np.float32))
    factor = jnp.asarray(np.where(pair_rows == pair_cols, 1.0, 2.0).astype(np.float32)[None, :])
    piece_dev = piece_owner.shape[0]
    atoms_dev = atom_offsets.shape[0]
    assert 2 * stick_local <= CORNER_AT and 2 * atoms_dev <= CORNER_LANES
    assert WANTED_AT + piece_dev <= PAIRS_AT
    row_len = PAIRS_AT + atoms_dev * pairs
    send = pl.pallas_call(
        functools.partial(
            pack_kernel,
            grid_devs=grid_devs,
            band_devs=band_devs,
            plane_slots=plane_slots,
            z_length=z_length,
            scale=(z_length * stick_count) ** -0.5,
        ),
        out_shape=jax.ShapeDtypeStruct((devices, row_len), jnp.float32),
        in_specs=[SMEM_SPEC, SMEM_SPEC] + [VMEM_SPEC] * 7 + [SMEM_SPEC],
        out_specs=VMEM_SPEC,
    )(
        plane_counts,
        occupations,
        coefficients.reshape(2 * stick_local, z_length),
        projections.reshape(2, nproj, atoms_dev),
        piece_owner.reshape(1, piece_dev),
        piece_slot.reshape(1, piece_dev),
        pick_rows,
        pick_cols,
        factor,
        atom_offsets,
    )
    got = lax.all_to_all(send, ("band", "grid"), 0, 0, tiled=True)
    got = got.reshape(band_devs, grid_devs, -1)

    lre = got[:, :, 0:stick_local].reshape(band_devs, stick_count)
    lim = got[:, :, stick_local : 2 * stick_local].reshape(band_devs, stick_count)
    row_of = stick_cols // NX
    col_of = stick_cols % NX
    y_cos, y_sin = phase_table(jnp.arange(NY, dtype=jnp.int32), row_of, NY)
    stick_live = jnp.where(stick_cols < NX * NY, 1.0, 0.0)[None, :]
    along_y = jnp.concatenate([y_cos * stick_live, y_sin * stick_live], 1)
    x_cos, x_sin = phase_table(col_of, jnp.arange(NX, dtype=jnp.int32), NX)
    b_real = lre[:, :, None] * x_cos[None] - lim[:, :, None] * x_sin[None]
    b_imag = lre[:, :, None] * x_sin[None] + lim[:, :, None] * x_cos[None]
    rhs = jnp.concatenate(
        [jnp.concatenate([b_real, b_imag], 2), jnp.concatenate([-b_imag, b_real], 2)], 1
    )
    wave = jnp.einsum("yk,bkx->byx", along_y, rhs, precision=THREE_PASS)
    valence = jnp.sum(wave[:, :, :NX] ** 2 + wave[:, :, NX:] ** 2, 0)

    wanted_here = got[0, :, WANTED_AT : WANTED_AT + piece_dev]
    pair_len = atoms_dev * pairs
    pair_sum = jnp.sum(got[:, :, PAIRS_AT : PAIRS_AT + pair_len], 0).reshape(-1, pairs)
    corner = got[0, :, CORNER_AT : CORNER_AT + 2 * atoms_dev].reshape(-1, 2).astype(jnp.int32)
    box_depth = pair_functions.shape[1]
    box_cells = pair_functions.shape[2]
    atoms = pair_sum.shape[0]
    flat_functions = pair_functions.reshape(pairs * box_depth, box_cells)
    mask = wanted_here.reshape(atoms, box_depth)
    weights = (pair_sum[:, :, None] * mask[:, None, :]).reshape(atoms, pairs * box_depth)
    boxes = jnp.dot(weights, flat_functions, precision=THREE_PASS).reshape(atoms, BY, BX)
    col_ids = jnp.arange(NX, dtype=jnp.int32)
    row_ids = jnp.arange(NY, dtype=jnp.int32)
    box_cols = jnp.arange(BX, dtype=jnp.int32)
    box_rows = jnp.arange(BY, dtype=jnp.int32)
    col_place = (
        (corner[:, 1:2, None] + box_cols[None, :, None]) % NX == col_ids[None, None, :]
    ).astype(jnp.float32)
    widened = jnp.einsum("aij,ajx->aix", boxes, col_place, precision=THREE_PASS)
    row_place = (
        (corner[:, 0:1, None] + box_rows[None, :, None]) % NY == row_ids[None, None, :]
    ).astype(jnp.float32)
    augment = jnp.einsum("aiy,aix->yx", row_place, widened, precision=THREE_PASS)
    density = valence + augment
    return density.reshape(1, 1, NY, NX)


def solution(mesh):
    in_specs = (
        P("band", None, "grid", None),
        P("band"),
        P(),
        P(),
        P("band", None, None, "grid"),
        P(),
        P("grid", None),
        P("grid", None),
        P("grid"),
    )
    out_specs = P("grid", "band", None, None)
    return jax.shard_map(
        on_device, mesh=mesh, in_specs=in_specs, out_specs=out_specs, check_vma=False
    )
```

```python
import functools
import math

import jax
import jax.numpy as jnp
import numpy as np
from jax import lax
from jax.experimental import pallas as pl
from jax.experimental.pallas import tpu as pltpu
from jax.sharding import PartitionSpec as P

NX = 256
NY = 256
PLANE_SLOTS = 4
BY = 16
BX = 16


PRECISE = lax.Precision.HIGHEST
THREE_PASS = lax.Precision.HIGH


def phase_table(left, right, length):
    phase_int = left[:, None] * right[None, :] % length
    phases = phase_int.astype(jnp.float32) * (2.0 * math.pi / length)
    return jnp.cos(phases), jnp.sin(phases)


SMEM_SPEC = pl.BlockSpec(memory_space=pltpu.SMEM)
CORNER_AT = 32
CORNER_LANES = 32
WANTED_AT = 64
PAIRS_AT = 128
VMEM_SPEC = pl.BlockSpec(memory_space=pltpu.VMEM)


def pack_kernel(
    counts_ref,
    occ_ref,
    coef_ref,
    proj_ref,
    owner_ref,
    slot_ref,
    pick_rows_ref,
    pick_cols_ref,
    factor_ref,
    corner_ref,
    send_ref,
    *,
    grid_devs,
    band_devs,
    plane_slots,
    z_length,
    scale,
):
    devices = grid_devs * band_devs
    occupied = occ_ref[0]
    dest = lax.broadcasted_iota(jnp.int32, (devices, 1), 0)
    dest_grid = dest % grid_devs
    dest_band = dest // grid_devs
    owner = owner_ref[...]
    count_d = jnp.zeros((devices, 1), jnp.int32)
    offset_d = jnp.zeros((devices, 1), jnp.int32)
    count_r = jnp.zeros(owner.shape, jnp.int32)
    for g in range(grid_devs):
        count = counts_ref[g]
        count_d = count_d + jnp.where(dest_grid == g, count, 0)
        offset_d = offset_d + jnp.where(dest_grid > g, count, 0)
        count_r = count_r + jnp.where(owner == g, count, 0)
    live = dest_band < count_d
    plane_z = jnp.where(live, offset_d + dest_band, 0)
    weight = jnp.where(live, jnp.sqrt(occupied) * scale, 0.0)
    freq = lax.broadcasted_iota(jnp.int32, (1, z_length), 1)
    phases = ((plane_z * freq) % z_length).astype(jnp.float32) * (2.0 * math.pi / z_length)
    coef = coef_ref[...]
    half = coef.shape[0] // 2
    swapped = jnp.concatenate([-coef[half:], coef[:half]], 0)
    contract_last = (((1,), (1,)), ((), ()))
    lines = lax.dot_general(
        jnp.cos(phases), coef, contract_last, precision=PRECISE, preferred_element_type=jnp.float32
    ) + lax.dot_general(
        jnp.sin(phases), swapped, contract_last, precision=PRECISE, preferred_element_type=jnp.float32
    )
    send_ref[...] = jnp.zeros(send_ref.shape, jnp.float32)
    send_ref[:, 0 : lines.shape[1]] = lines * weight
    corners = corner_ref[...].astype(jnp.float32)
    atoms_here = corners.shape[1]
    for axis in range(2):
        start = CORNER_AT + axis * atoms_here
        send_ref[:, start : start + atoms_here] = jnp.broadcast_to(
            corners[axis : axis + 1, :], (devices, atoms_here)
        )

    slot = slot_ref[...]
    for _ in range(plane_slots - 1):
        slot = jnp.where(slot >= count_r, slot - count_r, slot)
    target = owner * plane_slots + slot
    dest_plane = dest_grid * plane_slots + dest_band
    send_ref[:, WANTED_AT : WANTED_AT + target.shape[1]] = jnp.where(target == dest_plane, 1.0, 0.0)

    atoms = proj_ref.shape[1]
    total = None
    for part in range(proj_ref.shape[0]):
        proj_t = proj_ref[part]
        left = jnp.dot(proj_t, pick_rows_ref[...], precision=PRECISE, preferred_element_type=jnp.float32)
        right = jnp.dot(proj_t, pick_cols_ref[...], precision=PRECISE, preferred_element_type=jnp.float32)
        total = left * right if total is None else total + left * right
    total = total * (factor_ref[...] * occupied)
    pairs = total.shape[1]
    for atom in range(atoms):
        start = PAIRS_AT + atom * pairs
        send_ref[:, start : start + pairs] = jnp.broadcast_to(total[atom : atom + 1, :], (devices, pairs))


def on_device(
    coefficients,
    occupations,
    stick_cols,
    plane_counts,
    projections,
    pair_functions,
    atom_offsets,
    piece_owner,
    piece_slot,
):
    grid_devs = lax.axis_size("grid")
    band_devs = lax.axis_size("band")
    devices = grid_devs * band_devs
    _, _, stick_local, z_length = coefficients.shape
    stick_count = stick_local * grid_devs
    plane_slots = PLANE_SLOTS

    nproj = projections.shape[2]
    pair_rows, pair_cols = np.triu_indices(nproj)
    pairs = pair_rows.shape[0]
    pick_rows = jnp.asarray((np.arange(nproj)[:, None] == pair_rows[None, :]).astype(np.float32))
    pick_cols = jnp.asarray((np.arange(nproj)[:, None] == pair_cols[None, :]).astype(np.float32))
    factor = jnp.asarray(np.where(pair_rows == pair_cols, 1.0, 2.0).astype(np.float32)[None, :])
    piece_dev = piece_owner.shape[0]
    atoms_dev = atom_offsets.shape[0]
    assert 2 * stick_local <= CORNER_AT and 2 * atoms_dev <= CORNER_LANES
    assert WANTED_AT + piece_dev <= PAIRS_AT
    row_len = PAIRS_AT + atoms_dev * pairs
    send = pl.pallas_call(
        functools.partial(
            pack_kernel,
            grid_devs=grid_devs,
            band_devs=band_devs,
            plane_slots=plane_slots,
            z_length=z_length,
            scale=(z_length * stick_count) ** -0.5,
        ),
        out_shape=jax.ShapeDtypeStruct((devices, row_len), jnp.float32),
        in_specs=[SMEM_SPEC, SMEM_SPEC] + [VMEM_SPEC] * 8,
        out_specs=VMEM_SPEC,
    )(
        plane_counts,
        occupations,
        coefficients.reshape(2 * stick_local, z_length),
        jnp.transpose(projections, (0, 1, 3, 2)).reshape(2, atoms_dev, nproj),
        piece_owner.reshape(1, piece_dev),
        piece_slot.reshape(1, piece_dev),
        pick_rows,
        pick_cols,
        factor,
        atom_offsets.T,
    )
    got = lax.all_to_all(send, ("band", "grid"), 0, 0, tiled=True)
    got = got.reshape(band_devs, grid_devs, -1)

    lre = got[:, :, 0:stick_local].reshape(band_devs, stick_count)
    lim = got[:, :, stick_local : 2 * stick_local].reshape(band_devs, stick_count)
    row_of = stick_cols // NX
    col_of = stick_cols % NX
    y_cos, y_sin = phase_table(jnp.arange(NY, dtype=jnp.int32), row_of, NY)
    stick_live = jnp.where(stick_cols < NX * NY, 1.0, 0.0)[None, :]
    along_y = jnp.concatenate([y_cos * stick_live, y_sin * stick_live], 1)
    x_cos, x_sin = phase_table(col_of, jnp.arange(NX, dtype=jnp.int32), NX)
    b_real = lre[:, :, None] * x_cos[None] - lim[:, :, None] * x_sin[None]
    b_imag = lre[:, :, None] * x_sin[None] + lim[:, :, None] * x_cos[None]
    rhs = jnp.concatenate(
        [jnp.concatenate([b_real, b_imag], 2), jnp.concatenate([-b_imag, b_real], 2)], 1
    )
    wave = jnp.einsum("yk,bkx->byx", along_y, rhs, precision=THREE_PASS)
    valence = jnp.sum(wave[:, :, :NX] ** 2 + wave[:, :, NX:] ** 2, 0)

    wanted_here = got[0, :, WANTED_AT : WANTED_AT + piece_dev]
    pair_len = atoms_dev * pairs
    pair_sum = jnp.sum(got[:, :, PAIRS_AT : PAIRS_AT + pair_len], 0).reshape(-1, pairs)
    corner = got[0, :, CORNER_AT : CORNER_AT + 2 * atoms_dev].reshape(grid_devs, 2, atoms_dev)
    corner = jnp.transpose(corner, (0, 2, 1)).reshape(-1, 2).astype(jnp.int32)
    box_depth = pair_functions.shape[1]
    box_cells = pair_functions.shape[2]
    atoms = pair_sum.shape[0]
    flat_functions = pair_functions.reshape(pairs * box_depth, box_cells)
    mask = wanted_here.reshape(atoms, box_depth)
    weights = (pair_sum[:, :, None] * mask[:, None, :]).reshape(atoms, pairs * box_depth)
    boxes = jnp.dot(weights, flat_functions, precision=THREE_PASS).reshape(atoms, BY, BX)
    col_ids = jnp.arange(NX, dtype=jnp.int32)
    row_ids = jnp.arange(NY, dtype=jnp.int32)
    box_cols = jnp.arange(BX, dtype=jnp.int32)
    box_rows = jnp.arange(BY, dtype=jnp.int32)
    col_place = (
        (corner[:, 1:2, None] + box_cols[None, :, None]) % NX == col_ids[None, None, :]
    ).astype(jnp.float32)
    widened = jnp.einsum("aij,ajx->aix", boxes, col_place, precision=THREE_PASS)
    row_place = (
        (corner[:, 0:1, None] + box_rows[None, :, None]) % NY == row_ids[None, None, :]
    ).astype(jnp.float32)
    augment = jnp.einsum("aiy,aix->yx", row_place, widened, precision=THREE_PASS)
    density = valence + augment
    return density.reshape(1, 1, NY, NX)


def solution(mesh):
    in_specs = (
        P("band", None, "grid", None),
        P("band"),
        P(),
        P(),
        P("band", None, None, "grid"),
        P(),
        P("grid", None),
        P("grid", None),
        P("grid"),
    )
    out_specs = P("grid", "band", None, None)
    return jax.shard_map(
        on_device, mesh=mesh, in_specs=in_specs, out_specs=out_specs, check_vma=False
    )
```

```python
import functools
import math

import jax
import jax.numpy as jnp
import numpy as np
from jax import lax
from jax.experimental import pallas as pl
from jax.experimental.pallas import tpu as pltpu
from jax.sharding import PartitionSpec as P

NX = 256
NY = 256
PLANE_SLOTS = 4
BY = 16
BX = 16


PRECISE = lax.Precision.HIGHEST
THREE_PASS = lax.Precision.HIGH


def phase_table(left, right, length):
    phase_int = left[:, None] * right[None, :] % length
    phases = phase_int.astype(jnp.float32) * (2.0 * math.pi / length)
    return jnp.cos(phases), jnp.sin(phases)


SMEM_SPEC = pl.BlockSpec(memory_space=pltpu.SMEM)
CORNER_AT = 32
CORNER_LANES = 32
WANTED_AT = 64
LANES = 128
VMEM_SPEC = pl.BlockSpec(memory_space=pltpu.VMEM)


def pack_kernel(
    counts_ref,
    occ_ref,
    coef_ref,
    proj_ref,
    owner_ref,
    slot_ref,
    pick_rows_ref,
    pick_cols_ref,
    factor_ref,
    corner_ref,
    send_ref,
    *,
    grid_devs,
    band_devs,
    plane_slots,
    z_length,
    scale,
):
    devices = grid_devs * band_devs
    occupied = occ_ref[0]
    dest = lax.broadcasted_iota(jnp.int32, (devices, 1), 0)
    dest_grid = dest % grid_devs
    dest_band = dest // grid_devs
    owner = owner_ref[...]
    count_d = jnp.zeros((devices, 1), jnp.int32)
    offset_d = jnp.zeros((devices, 1), jnp.int32)
    count_r = jnp.zeros(owner.shape, jnp.int32)
    for g in range(grid_devs):
        count = counts_ref[g]
        count_d = count_d + jnp.where(dest_grid == g, count, 0)
        offset_d = offset_d + jnp.where(dest_grid > g, count, 0)
        count_r = count_r + jnp.where(owner == g, count, 0)
    live = dest_band < count_d
    plane_z = jnp.where(live, offset_d + dest_band, 0)
    weight = jnp.where(live, jnp.sqrt(occupied) * scale, 0.0)
    freq = lax.broadcasted_iota(jnp.int32, (1, z_length), 1)
    phases = ((plane_z * freq) % z_length).astype(jnp.float32) * (2.0 * math.pi / z_length)
    coef = coef_ref[...]
    half = coef.shape[0] // 2
    swapped = jnp.concatenate([-coef[half:], coef[:half]], 0)
    contract_last = (((1,), (1,)), ((), ()))
    lines = lax.dot_general(
        jnp.cos(phases), coef, contract_last, precision=PRECISE, preferred_element_type=jnp.float32
    ) + lax.dot_general(
        jnp.sin(phases), swapped, contract_last, precision=PRECISE, preferred_element_type=jnp.float32
    )
    send_ref[...] = jnp.zeros(send_ref.shape, jnp.float32)
    lines = lines * weight
    corners = corner_ref[...].astype(jnp.float32)
    atoms_here = corners.shape[1]
    head = jnp.zeros((devices, LANES), jnp.float32)
    head = jnp.concatenate([lines, head[:, lines.shape[1] :]], 1)

    slot = slot_ref[...]
    for _ in range(plane_slots - 1):
        slot = jnp.where(slot >= count_r, slot - count_r, slot)
    target = owner * plane_slots + slot
    dest_plane = dest_grid * plane_slots + dest_band
    wanted = jnp.where(target == dest_plane, 1.0, 0.0)
    head = jnp.concatenate(
        [head[:, :CORNER_AT], jnp.broadcast_to(corners[0:1, :], (devices, atoms_here)),
         jnp.broadcast_to(corners[1:2, :], (devices, atoms_here)),
         head[:, CORNER_AT + 2 * atoms_here : WANTED_AT], wanted], 1)
    for dest_id in range(devices):
        send_ref[dest_id, 0:1, :] = head[dest_id : dest_id + 1, :]

    atoms = proj_ref.shape[1]
    total = None
    for part in range(proj_ref.shape[0]):
        proj_t = proj_ref[part]
        left = jnp.dot(proj_t, pick_rows_ref[...], precision=PRECISE, preferred_element_type=jnp.float32)
        right = jnp.dot(proj_t, pick_cols_ref[...], precision=PRECISE, preferred_element_type=jnp.float32)
        total = left * right if total is None else total + left * right
    total = total * (factor_ref[...] * occupied)
    pairs = total.shape[1]
    send_ref[:, 1 : 1 + atoms, :] = jnp.broadcast_to(total[None, :, :LANES], (devices, atoms, LANES))
    tail = pairs - LANES
    per_row = LANES // tail
    for atom in range(atoms):
        row = 1 + atoms + atom // per_row
        start = (atom % per_row) * tail
        send_ref[:, row : row + 1, start : start + tail] = jnp.broadcast_to(
            total[None, atom : atom + 1, LANES:], (devices, 1, tail)
        )


def on_device(
    coefficients,
    occupations,
    stick_cols,
    plane_counts,
    projections,
    pair_functions,
    atom_offsets,
    piece_owner,
    piece_slot,
):
    grid_devs = lax.axis_size("grid")
    band_devs = lax.axis_size("band")
    devices = grid_devs * band_devs
    _, _, stick_local, z_length = coefficients.shape
    stick_count = stick_local * grid_devs
    plane_slots = PLANE_SLOTS

    nproj = projections.shape[2]
    pair_rows, pair_cols = np.triu_indices(nproj)
    pairs = pair_rows.shape[0]
    pick_rows = jnp.asarray((np.arange(nproj)[:, None] == pair_rows[None, :]).astype(np.float32))
    pick_cols = jnp.asarray((np.arange(nproj)[:, None] == pair_cols[None, :]).astype(np.float32))
    factor = jnp.asarray(np.where(pair_rows == pair_cols, 1.0, 2.0).astype(np.float32)[None, :])
    piece_dev = piece_owner.shape[0]
    atoms_dev = atom_offsets.shape[0]
    assert 2 * stick_local <= CORNER_AT and 2 * atoms_dev <= CORNER_LANES
    assert WANTED_AT + piece_dev == LANES and LANES < pairs < 2 * LANES
    tail = pairs - LANES
    per_row = LANES // tail
    slab_rows = 1 + atoms_dev + -(-atoms_dev // per_row)
    send = pl.pallas_call(
        functools.partial(
            pack_kernel,
            grid_devs=grid_devs,
            band_devs=band_devs,
            plane_slots=plane_slots,
            z_length=z_length,
            scale=(z_length * stick_count) ** -0.5,
        ),
        out_shape=jax.ShapeDtypeStruct((devices, slab_rows, LANES), jnp.float32),
        in_specs=[SMEM_SPEC, SMEM_SPEC] + [VMEM_SPEC] * 8,
        out_specs=VMEM_SPEC,
    )(
        plane_counts,
        occupations,
        coefficients.reshape(2 * stick_local, z_length),
        jnp.transpose(projections, (0, 1, 3, 2)).reshape(2, atoms_dev, nproj),
        piece_owner.reshape(1, piece_dev),
        piece_slot.reshape(1, piece_dev),
        pick_rows,
        pick_cols,
        factor,
        atom_offsets.T,
    )
    got = lax.all_to_all(send, ("band", "grid"), 0, 0, tiled=True)
    got = got.reshape(band_devs, grid_devs, slab_rows, LANES)
    tails = got[:, :, 1 + atoms_dev :, : per_row * tail].reshape(band_devs, grid_devs, -1)
    tails = tails[:, :, : atoms_dev * tail]
    pair_rows_got = jnp.concatenate(
        [got[:, :, 1 : 1 + atoms_dev, :], tails.reshape(band_devs, grid_devs, atoms_dev, tail)], 3
    )
    got = got[:, :, 0, :]

    lre = got[:, :, 0:stick_local].reshape(band_devs, stick_count)
    lim = got[:, :, stick_local : 2 * stick_local].reshape(band_devs, stick_count)
    row_of = stick_cols // NX
    col_of = stick_cols % NX
    y_cos, y_sin = phase_table(jnp.arange(NY, dtype=jnp.int32), row_of, NY)
    stick_live = jnp.where(stick_cols < NX * NY, 1.0, 0.0)[None, :]
    along_y = jnp.concatenate([y_cos * stick_live, y_sin * stick_live], 1)
    x_cos, x_sin = phase_table(col_of, jnp.arange(NX, dtype=jnp.int32), NX)
    b_real = lre[:, :, None] * x_cos[None] - lim[:, :, None] * x_sin[None]
    b_imag = lre[:, :, None] * x_sin[None] + lim[:, :, None] * x_cos[None]
    rhs = jnp.concatenate(
        [jnp.concatenate([b_real, b_imag], 2), jnp.concatenate([-b_imag, b_real], 2)], 1
    )
    wave = jnp.einsum("yk,bkx->byx", along_y, rhs, precision=THREE_PASS)
    valence = jnp.sum(wave[:, :, :NX] ** 2 + wave[:, :, NX:] ** 2, 0)

    wanted_here = got[0, :, WANTED_AT : WANTED_AT + piece_dev]
    pair_len = atoms_dev * pairs
    pair_sum = jnp.sum(pair_rows_got, 0).reshape(-1, pairs)
    corner = got[0, :, CORNER_AT : CORNER_AT + 2 * atoms_dev].reshape(grid_devs, 2, atoms_dev)
    corner = jnp.transpose(corner, (0, 2, 1)).reshape(-1, 2).astype(jnp.int32)
    box_depth = pair_functions.shape[1]
    box_cells = pair_functions.shape[2]
    atoms = pair_sum.shape[0]
    flat_functions = pair_functions.reshape(pairs * box_depth, box_cells)
    mask = wanted_here.reshape(atoms, box_depth)
    weights = (pair_sum[:, :, None] * mask[:, None, :]).reshape(atoms, pairs * box_depth)
    boxes = jnp.dot(weights, flat_functions, precision=THREE_PASS).reshape(atoms, BY, BX)
    col_ids = jnp.arange(NX, dtype=jnp.int32)
    row_ids = jnp.arange(NY, dtype=jnp.int32)
    box_cols = jnp.arange(BX, dtype=jnp.int32)
    box_rows = jnp.arange(BY, dtype=jnp.int32)
    col_place = (
        (corner[:, 1:2, None] + box_cols[None, :, None]) % NX == col_ids[None, None, :]
    ).astype(jnp.float32)
    widened = jnp.einsum("aij,ajx->aix", boxes, col_place, precision=THREE_PASS)
    row_place = (
        (corner[:, 0:1, None] + box_rows[None, :, None]) % NY == row_ids[None, None, :]
    ).astype(jnp.float32)
    augment = jnp.einsum("aiy,aix->yx", row_place, widened, precision=THREE_PASS)
    density = valence + augment
    return density.reshape(1, 1, NY, NX)


def solution(mesh):
    in_specs = (
        P("band", None, "grid", None),
        P("band"),
        P(),
        P(),
        P("band", None, None, "grid"),
        P(),
        P("grid", None),
        P("grid", None),
        P("grid"),
    )
    out_specs = P("grid", "band", None, None)
    return jax.shard_map(
        on_device, mesh=mesh, in_specs=in_specs, out_specs=out_specs, check_vma=False
    )
```

```python
import functools
import math

import jax
import jax.numpy as jnp
import numpy as np
from jax import lax
from jax.experimental import pallas as pl
from jax.experimental.pallas import tpu as pltpu
from jax.sharding import PartitionSpec as P

NX = 256
NY = 256
PLANE_SLOTS = 4
BY = 16
BX = 16


PRECISE = lax.Precision.HIGHEST
THREE_PASS = lax.Precision.HIGH


def phase_table(left, right, length):
    phase_int = left[:, None] * right[None, :] % length
    phases = phase_int.astype(jnp.float32) * (2.0 * math.pi / length)
    return jnp.cos(phases), jnp.sin(phases)


SMEM_SPEC = pl.BlockSpec(memory_space=pltpu.SMEM)
CORNER_AT = 32
CORNER_LANES = 32
WANTED_AT = 64
LANES = 128
VMEM_SPEC = pl.BlockSpec(memory_space=pltpu.VMEM)


def pack_kernel(
    counts_ref,
    occ_ref,
    coef_ref,
    proj_ref,
    owner_ref,
    slot_ref,
    pick_rows_ref,
    pick_cols_ref,
    factor_ref,
    corner_ref,
    send_ref,
    *,
    grid_devs,
    band_devs,
    plane_slots,
    z_length,
    scale,
):
    devices = grid_devs * band_devs
    occupied = occ_ref[0]
    dest = lax.broadcasted_iota(jnp.int32, (devices, 1), 0)
    dest_grid = dest % grid_devs
    dest_band = dest // grid_devs
    owner = owner_ref[...]
    count_d = jnp.zeros((devices, 1), jnp.int32)
    offset_d = jnp.zeros((devices, 1), jnp.int32)
    count_r = jnp.zeros(owner.shape, jnp.int32)
    for g in range(grid_devs):
        count = counts_ref[g]
        count_d = count_d + jnp.where(dest_grid == g, count, 0)
        offset_d = offset_d + jnp.where(dest_grid > g, count, 0)
        count_r = count_r + jnp.where(owner == g, count, 0)
    live = dest_band < count_d
    plane_z = jnp.where(live, offset_d + dest_band, 0)
    weight = jnp.where(live, jnp.sqrt(occupied) * scale, 0.0)
    freq = lax.broadcasted_iota(jnp.int32, (1, z_length), 1)
    phases = ((plane_z * freq) % z_length).astype(jnp.float32) * (2.0 * math.pi / z_length)
    coef = coef_ref[...]
    half = coef.shape[0] // 2
    swapped = jnp.concatenate([-coef[half:], coef[:half]], 0)
    contract_last = (((1,), (1,)), ((), ()))
    lines = lax.dot_general(
        jnp.cos(phases), coef, contract_last, precision=PRECISE, preferred_element_type=jnp.float32
    ) + lax.dot_general(
        jnp.sin(phases), swapped, contract_last, precision=PRECISE, preferred_element_type=jnp.float32
    )
    send_ref[...] = jnp.zeros(send_ref.shape, jnp.float32)
    lines = lines * weight
    corners = corner_ref[...].astype(jnp.float32)
    atoms_here = corners.shape[1]
    head = jnp.zeros((devices, LANES), jnp.float32)
    head = jnp.concatenate([lines, head[:, lines.shape[1] :]], 1)

    slot = slot_ref[...]
    for _ in range(plane_slots - 1):
        slot = jnp.where(slot >= count_r, slot - count_r, slot)
    target = owner * plane_slots + slot
    dest_plane = dest_grid * plane_slots + dest_band
    wanted = jnp.where(target == dest_plane, 1.0, 0.0)
    head = jnp.concatenate(
        [head[:, :CORNER_AT], jnp.broadcast_to(corners[0:1, :], (devices, atoms_here)),
         jnp.broadcast_to(corners[1:2, :], (devices, atoms_here)),
         head[:, CORNER_AT + 2 * atoms_here : WANTED_AT], wanted], 1)
    for dest_id in range(devices):
        send_ref[dest_id, 0:1, :] = head[dest_id : dest_id + 1, :]

    atoms = proj_ref.shape[1]
    total = None
    for part in range(proj_ref.shape[0]):
        proj_t = proj_ref[part]
        left = jnp.dot(proj_t, pick_rows_ref[...], precision=PRECISE, preferred_element_type=jnp.float32)
        right = jnp.dot(proj_t, pick_cols_ref[...], precision=PRECISE, preferred_element_type=jnp.float32)
        total = left * right if total is None else total + left * right
    total = total * (factor_ref[...] * occupied)
    pairs = total.shape[1]
    send_ref[:, 1 : 1 + atoms, :] = jnp.broadcast_to(total[None, :, :LANES], (devices, atoms, LANES))
    tail = pairs - LANES
    per_row = LANES // tail
    for atom in range(atoms):
        row = 1 + atoms + atom // per_row
        start = (atom % per_row) * tail
        send_ref[:, row : row + 1, start : start + tail] = jnp.broadcast_to(
            total[None, atom : atom + 1, LANES:], (devices, 1, tail)
        )


def on_device(
    coefficients,
    occupations,
    stick_cols,
    plane_counts,
    projections,
    pair_functions,
    atom_offsets,
    piece_owner,
    piece_slot,
):
    grid_devs = lax.axis_size("grid")
    band_devs = lax.axis_size("band")
    devices = grid_devs * band_devs
    _, _, stick_local, z_length = coefficients.shape
    stick_count = stick_local * grid_devs
    plane_slots = PLANE_SLOTS

    nproj = projections.shape[2]
    pair_rows, pair_cols = np.triu_indices(nproj)
    pairs = pair_rows.shape[0]
    pick_rows = jnp.asarray((np.arange(nproj)[:, None] == pair_rows[None, :]).astype(np.float32))
    pick_cols = jnp.asarray((np.arange(nproj)[:, None] == pair_cols[None, :]).astype(np.float32))
    factor = jnp.asarray(np.where(pair_rows == pair_cols, 1.0, 2.0).astype(np.float32)[None, :])
    piece_dev = piece_owner.shape[0]
    atoms_dev = atom_offsets.shape[0]
    assert 2 * stick_local <= CORNER_AT and 2 * atoms_dev <= CORNER_LANES
    assert WANTED_AT + piece_dev == LANES and LANES < pairs < 2 * LANES
    tail = pairs - LANES
    per_row = LANES // tail
    slab_rows = 1 + atoms_dev + -(-atoms_dev // per_row)
    send = pl.pallas_call(
        functools.partial(
            pack_kernel,
            grid_devs=grid_devs,
            band_devs=band_devs,
            plane_slots=plane_slots,
            z_length=z_length,
            scale=(z_length * stick_count) ** -0.5,
        ),
        out_shape=jax.ShapeDtypeStruct((devices, slab_rows, LANES), jnp.float32),
        in_specs=[SMEM_SPEC, SMEM_SPEC] + [VMEM_SPEC] * 8,
        out_specs=VMEM_SPEC,
    )(
        plane_counts,
        occupations,
        coefficients.reshape(2 * stick_local, z_length),
        jnp.transpose(projections, (0, 1, 3, 2)).reshape(2, atoms_dev, nproj),
        piece_owner.reshape(1, piece_dev),
        piece_slot.reshape(1, piece_dev),
        pick_rows,
        pick_cols,
        factor,
        atom_offsets.T,
    )
    got = lax.all_to_all(send, ("band", "grid"), 0, 0, tiled=True)
    got = got.reshape(band_devs, grid_devs, slab_rows * LANES)
    pair_parts = []
    for atom in range(atoms_dev):
        head_at = (1 + atom) * LANES
        tail_at = (1 + atoms_dev + atom // per_row) * LANES + (atom % per_row) * tail
        pair_parts.append(
            jnp.concatenate(
                [got[:, :, head_at : head_at + LANES], got[:, :, tail_at : tail_at + tail]], 2
            )
        )
    pair_rows_got = jnp.stack(pair_parts, 2)

    lre = got[:, :, 0:stick_local].reshape(band_devs, stick_count)
    lim = got[:, :, stick_local : 2 * stick_local].reshape(band_devs, stick_count)
    row_of = stick_cols // NX
    col_of = stick_cols % NX
    y_cos, y_sin = phase_table(jnp.arange(NY, dtype=jnp.int32), row_of, NY)
    stick_live = jnp.where(stick_cols < NX * NY, 1.0, 0.0)[None, :]
    along_y = jnp.concatenate([y_cos * stick_live, y_sin * stick_live], 1)
    x_cos, x_sin = phase_table(col_of, jnp.arange(NX, dtype=jnp.int32), NX)
    b_real = lre[:, :, None] * x_cos[None] - lim[:, :, None] * x_sin[None]
    b_imag = lre[:, :, None] * x_sin[None] + lim[:, :, None] * x_cos[None]
    rhs = jnp.concatenate(
        [jnp.concatenate([b_real, b_imag], 2), jnp.concatenate([-b_imag, b_real], 2)], 1
    )
    wave = jnp.einsum("yk,bkx->byx", along_y, rhs, precision=THREE_PASS)
    valence = jnp.sum(wave[:, :, :NX] ** 2 + wave[:, :, NX:] ** 2, 0)

    wanted_here = got[0, :, WANTED_AT : WANTED_AT + piece_dev]
    pair_len = atoms_dev * pairs
    pair_sum = jnp.sum(pair_rows_got, 0).reshape(-1, pairs)
    corner = got[0, :, CORNER_AT : CORNER_AT + 2 * atoms_dev].reshape(grid_devs, 2, atoms_dev)
    corner = jnp.transpose(corner, (0, 2, 1)).reshape(-1, 2).astype(jnp.int32)
    box_depth = pair_functions.shape[1]
    box_cells = pair_functions.shape[2]
    atoms = pair_sum.shape[0]
    flat_functions = pair_functions.reshape(pairs * box_depth, box_cells)
    mask = wanted_here.reshape(atoms, box_depth)
    weights = (pair_sum[:, :, None] * mask[:, None, :]).reshape(atoms, pairs * box_depth)
    boxes = jnp.dot(weights, flat_functions, precision=THREE_PASS).reshape(atoms, BY, BX)
    col_ids = jnp.arange(NX, dtype=jnp.int32)
    row_ids = jnp.arange(NY, dtype=jnp.int32)
    box_cols = jnp.arange(BX, dtype=jnp.int32)
    box_rows = jnp.arange(BY, dtype=jnp.int32)
    col_place = (
        (corner[:, 1:2, None] + box_cols[None, :, None]) % NX == col_ids[None, None, :]
    ).astype(jnp.float32)
    widened = jnp.einsum("aij,ajx->aix", boxes, col_place, precision=THREE_PASS)
    row_place = (
        (corner[:, 0:1, None] + box_rows[None, :, None]) % NY == row_ids[None, None, :]
    ).astype(jnp.float32)
    augment = jnp.einsum("aiy,aix->yx", row_place, widened, precision=THREE_PASS)
    density = valence + augment
    return density.reshape(1, 1, NY, NX)


def solution(mesh):
    in_specs = (
        P("band", None, "grid", None),
        P("band"),
        P(),
        P(),
        P("band", None, None, "grid"),
        P(),
        P("grid", None),
        P("grid", None),
        P("grid"),
    )
    out_specs = P("grid", "band", None, None)
    return jax.shard_map(
        on_device, mesh=mesh, in_specs=in_specs, out_specs=out_specs, check_vma=False
    )
```

```python
import functools
import math

import jax
import jax.numpy as jnp
import numpy as np
from jax import lax
from jax.experimental import pallas as pl
from jax.experimental.pallas import tpu as pltpu
from jax.sharding import PartitionSpec as P

NX = 256
NY = 256
PLANE_SLOTS = 4
BY = 16
BX = 16


PRECISE = lax.Precision.HIGHEST
THREE_PASS = lax.Precision.HIGH


def phase_table(left, right, length):
    phase_int = left[:, None] * right[None, :] % length
    phases = phase_int.astype(jnp.float32) * (2.0 * math.pi / length)
    return jnp.cos(phases), jnp.sin(phases)


SMEM_SPEC = pl.BlockSpec(memory_space=pltpu.SMEM)
CORNER_AT = 32
CORNER_LANES = 32
WANTED_AT = 64
LANES = 128
VMEM_SPEC = pl.BlockSpec(memory_space=pltpu.VMEM)


def pack_kernel(
    counts_ref,
    occ_ref,
    coef_ref,
    proj_ref,
    owner_ref,
    slot_ref,
    pick_rows_ref,
    pick_cols_ref,
    factor_ref,
    corner_ref,
    send_ref,
    *,
    grid_devs,
    band_devs,
    plane_slots,
    z_length,
    scale,
):
    devices = grid_devs * band_devs
    occupied = occ_ref[0]
    dest = lax.broadcasted_iota(jnp.int32, (devices, 1), 0)
    dest_grid = dest % grid_devs
    dest_band = dest // grid_devs
    owner = owner_ref[...]
    count_d = jnp.zeros((devices, 1), jnp.int32)
    offset_d = jnp.zeros((devices, 1), jnp.int32)
    count_r = jnp.zeros(owner.shape, jnp.int32)
    for g in range(grid_devs):
        count = counts_ref[g]
        count_d = count_d + jnp.where(dest_grid == g, count, 0)
        offset_d = offset_d + jnp.where(dest_grid > g, count, 0)
        count_r = count_r + jnp.where(owner == g, count, 0)
    live = dest_band < count_d
    plane_z = jnp.where(live, offset_d + dest_band, 0)
    weight = jnp.where(live, jnp.sqrt(occupied) * scale, 0.0)
    freq = lax.broadcasted_iota(jnp.int32, (1, z_length), 1)
    phases = ((plane_z * freq) % z_length).astype(jnp.float32) * (2.0 * math.pi / z_length)
    coef = coef_ref[...]
    half = coef.shape[0] // 2
    swapped = jnp.concatenate([-coef[half:], coef[:half]], 0)
    contract_last = (((1,), (1,)), ((), ()))
    lines = lax.dot_general(
        jnp.cos(phases), coef, contract_last, precision=PRECISE, preferred_element_type=jnp.float32
    ) + lax.dot_general(
        jnp.sin(phases), swapped, contract_last, precision=PRECISE, preferred_element_type=jnp.float32
    )
    send_ref[...] = jnp.zeros(send_ref.shape, jnp.float32)
    lines = lines * weight
    corners = corner_ref[...].astype(jnp.float32)
    atoms_here = corners.shape[1]
    head = jnp.zeros((devices, LANES), jnp.float32)
    head = jnp.concatenate([lines, head[:, lines.shape[1] :]], 1)

    slot = slot_ref[...]
    for _ in range(plane_slots - 1):
        slot = jnp.where(slot >= count_r, slot - count_r, slot)
    target = owner * plane_slots + slot
    dest_plane = dest_grid * plane_slots + dest_band
    wanted = jnp.where(target == dest_plane, 1.0, 0.0)
    head = jnp.concatenate(
        [head[:, :CORNER_AT], jnp.broadcast_to(corners[0:1, :], (devices, atoms_here)),
         jnp.broadcast_to(corners[1:2, :], (devices, atoms_here)),
         head[:, CORNER_AT + 2 * atoms_here : WANTED_AT], wanted], 1)
    for dest_id in range(devices):
        send_ref[dest_id, 0:1, :] = head[dest_id : dest_id + 1, :]

    atoms = proj_ref.shape[1]
    total = None
    for part in range(proj_ref.shape[0]):
        proj_t = proj_ref[part]
        left = jnp.dot(proj_t, pick_rows_ref[...], precision=PRECISE, preferred_element_type=jnp.float32)
        right = jnp.dot(proj_t, pick_cols_ref[...], precision=PRECISE, preferred_element_type=jnp.float32)
        total = left * right if total is None else total + left * right
    total = total * (factor_ref[...] * occupied)
    pairs = total.shape[1]
    send_ref[:, 1 : 1 + atoms, :] = jnp.broadcast_to(total[None, :, :LANES], (devices, atoms, LANES))
    tail = pairs - LANES
    per_row = LANES // tail
    for atom in range(atoms):
        row = 1 + atoms + atom // per_row
        start = (atom % per_row) * tail
        send_ref[:, row : row + 1, start : start + tail] = jnp.broadcast_to(
            total[None, atom : atom + 1, LANES:], (devices, 1, tail)
        )


def on_device(
    coefficients,
    occupations,
    stick_cols,
    plane_counts,
    projections,
    pair_functions,
    atom_offsets,
    piece_owner,
    piece_slot,
):
    grid_devs = lax.axis_size("grid")
    band_devs = lax.axis_size("band")
    devices = grid_devs * band_devs
    _, _, stick_local, z_length = coefficients.shape
    stick_count = stick_local * grid_devs
    plane_slots = PLANE_SLOTS

    nproj = projections.shape[2]
    pair_rows, pair_cols = np.triu_indices(nproj)
    pairs = pair_rows.shape[0]
    pick_rows = jnp.asarray((np.arange(nproj)[:, None] == pair_rows[None, :]).astype(np.float32))
    pick_cols = jnp.asarray((np.arange(nproj)[:, None] == pair_cols[None, :]).astype(np.float32))
    factor = jnp.asarray(np.where(pair_rows == pair_cols, 1.0, 2.0).astype(np.float32)[None, :])
    piece_dev = piece_owner.shape[0]
    atoms_dev = atom_offsets.shape[0]
    assert 2 * stick_local <= CORNER_AT and 2 * atoms_dev <= CORNER_LANES
    assert WANTED_AT + piece_dev == LANES and LANES < pairs < 2 * LANES
    tail = pairs - LANES
    per_row = LANES // tail
    slab_rows = 1 + atoms_dev + -(-atoms_dev // per_row)
    send = pl.pallas_call(
        functools.partial(
            pack_kernel,
            grid_devs=grid_devs,
            band_devs=band_devs,
            plane_slots=plane_slots,
            z_length=z_length,
            scale=(z_length * stick_count) ** -0.5,
        ),
        out_shape=jax.ShapeDtypeStruct((devices, slab_rows, LANES), jnp.float32),
        in_specs=[SMEM_SPEC, SMEM_SPEC] + [VMEM_SPEC] * 8,
        out_specs=VMEM_SPEC,
    )(
        plane_counts,
        occupations,
        coefficients.reshape(2 * stick_local, z_length),
        jnp.transpose(projections, (0, 1, 3, 2)).reshape(2, atoms_dev, nproj),
        piece_owner.reshape(1, piece_dev),
        piece_slot.reshape(1, piece_dev),
        pick_rows,
        pick_cols,
        factor,
        atom_offsets.T,
    )
    got = lax.all_to_all(send, ("band", "grid"), 0, 0, tiled=True)
    got = got.reshape(band_devs, grid_devs, slab_rows * LANES)
    pair_parts = []
    for atom in range(atoms_dev):
        head_at = (1 + atom) * LANES
        tail_at = (1 + atoms_dev + atom // per_row) * LANES + (atom % per_row) * tail
        pair_parts.append(
            jnp.concatenate(
                [got[:, :, head_at : head_at + LANES], got[:, :, tail_at : tail_at + tail]], 2
            )
        )
    pair_rows_got = jnp.stack(pair_parts, 2)

    lre = got[:, :, 0:stick_local].reshape(band_devs, stick_count)
    lim = got[:, :, stick_local : 2 * stick_local].reshape(band_devs, stick_count)
    row_of = stick_cols // NX
    col_of = stick_cols % NX
    y_cos, y_sin = phase_table(jnp.arange(NY, dtype=jnp.int32), row_of, NY)
    stick_live = jnp.where(stick_cols < NX * NY, 1.0, 0.0)[None, :]
    along_y = jnp.concatenate([y_cos * stick_live, y_sin * stick_live], 1)
    x_cos, x_sin = phase_table(col_of, jnp.arange(NX, dtype=jnp.int32), NX)
    b_real = lre[:, :, None] * x_cos[None] - lim[:, :, None] * x_sin[None]
    b_imag = lre[:, :, None] * x_sin[None] + lim[:, :, None] * x_cos[None]
    rhs = jnp.concatenate(
        [jnp.concatenate([b_real, b_imag], 2), jnp.concatenate([-b_imag, b_real], 2)], 1
    )
    wave = jnp.einsum("yk,bkx->byx", along_y, rhs, precision=THREE_PASS)
    valence = jnp.sum(wave[:, :, :NX] ** 2 + wave[:, :, NX:] ** 2, 0)

    wanted_here = got[0, :, WANTED_AT : WANTED_AT + piece_dev]
    pair_len = atoms_dev * pairs
    pair_sum = jnp.sum(pair_rows_got, 0).reshape(-1, pairs)
    corner = got[0, :, CORNER_AT : CORNER_AT + 2 * atoms_dev].reshape(grid_devs, 2, atoms_dev)
    corner = jnp.transpose(corner, (0, 2, 1)).reshape(-1, 2)
    box_depth = pair_functions.shape[1]
    box_cells = pair_functions.shape[2]
    atoms = pair_sum.shape[0]
    flat_functions = pair_functions.reshape(pairs * box_depth, box_cells)
    mask = wanted_here.reshape(atoms, box_depth)
    weights = (pair_sum[:, :, None] * mask[:, None, :]).reshape(atoms, pairs * box_depth)
    boxes = jnp.dot(weights, flat_functions, precision=THREE_PASS).reshape(atoms, BY, BX)
    col_ids = jnp.arange(NX, dtype=jnp.float32)
    row_ids = jnp.arange(NY, dtype=jnp.float32)
    box_cols = jnp.arange(BX, dtype=jnp.float32)
    box_rows = jnp.arange(BY, dtype=jnp.float32)
    col_place = (
        jnp.mod(corner[:, 1:2, None] + box_cols[None, :, None], NX) == col_ids[None, None, :]
    ).astype(jnp.float32)
    widened = jnp.einsum("aij,ajx->aix", boxes, col_place, precision=THREE_PASS)
    row_place = (
        jnp.mod(corner[:, 0:1, None] + box_rows[None, :, None], NY) == row_ids[None, None, :]
    ).astype(jnp.float32)
    augment = jnp.einsum("aiy,aix->yx", row_place, widened, precision=THREE_PASS)
    density = valence + augment
    return density.reshape(1, 1, NY, NX)


def solution(mesh):
    in_specs = (
        P("band", None, "grid", None),
        P("band"),
        P(),
        P(),
        P("band", None, None, "grid"),
        P(),
        P("grid", None),
        P("grid", None),
        P("grid"),
    )
    out_specs = P("grid", "band", None, None)
    return jax.shard_map(
        on_device, mesh=mesh, in_specs=in_specs, out_specs=out_specs, check_vma=False
    )
```

```python
import functools
import math

import jax
import jax.numpy as jnp
import numpy as np
from jax import lax
from jax.experimental import pallas as pl
from jax.experimental.pallas import tpu as pltpu
from jax.sharding import PartitionSpec as P

NX = 256
NY = 256
PLANE_SLOTS = 4
BY = 16
BX = 16


PRECISE = lax.Precision.HIGHEST
THREE_PASS = lax.Precision.HIGH


def phase_table(left, right, length):
    phase_int = left[:, None] * right[None, :] % length
    phases = phase_int.astype(jnp.float32) * (2.0 * math.pi / length)
    return jnp.cos(phases), jnp.sin(phases)


SMEM_SPEC = pl.BlockSpec(memory_space=pltpu.SMEM)
CORNER_AT = 32
CORNER_LANES = 32
WANTED_AT = 64
LANES = 128
VMEM_SPEC = pl.BlockSpec(memory_space=pltpu.VMEM)


def pack_kernel(
    counts_ref,
    occ_ref,
    coef_ref,
    proj_ref,
    owner_ref,
    slot_ref,
    pick_rows_ref,
    pick_cols_ref,
    factor_ref,
    corner_ref,
    send_ref,
    *,
    grid_devs,
    band_devs,
    plane_slots,
    z_length,
    scale,
):
    devices = grid_devs * band_devs
    occupied = occ_ref[0]
    dest = lax.broadcasted_iota(jnp.int32, (devices, 1), 0)
    dest_grid = dest % grid_devs
    dest_band = dest // grid_devs
    owner = owner_ref[...]
    count_d = jnp.zeros((devices, 1), jnp.int32)
    offset_d = jnp.zeros((devices, 1), jnp.int32)
    count_r = jnp.zeros(owner.shape, jnp.int32)
    for g in range(grid_devs):
        count = counts_ref[g]
        count_d = count_d + jnp.where(dest_grid == g, count, 0)
        offset_d = offset_d + jnp.where(dest_grid > g, count, 0)
        count_r = count_r + jnp.where(owner == g, count, 0)
    live = dest_band < count_d
    plane_z = jnp.where(live, offset_d + dest_band, 0)
    weight = jnp.where(live, jnp.sqrt(occupied) * scale, 0.0)
    freq = lax.broadcasted_iota(jnp.int32, (1, z_length), 1)
    phases = ((plane_z * freq) % z_length).astype(jnp.float32) * (2.0 * math.pi / z_length)
    coef = coef_ref[...]
    half = coef.shape[0] // 2
    swapped = jnp.concatenate([-coef[half:], coef[:half]], 0)
    contract_last = (((1,), (1,)), ((), ()))
    lines = lax.dot_general(
        jnp.cos(phases), coef, contract_last, precision=PRECISE, preferred_element_type=jnp.float32
    ) + lax.dot_general(
        jnp.sin(phases), swapped, contract_last, precision=PRECISE, preferred_element_type=jnp.float32
    )
    send_ref[...] = jnp.zeros(send_ref.shape, jnp.float32)
    lines = lines * weight
    corners = corner_ref[...].astype(jnp.float32)
    atoms_here = corners.shape[1]
    head = jnp.zeros((devices, LANES), jnp.float32)
    head = jnp.concatenate([lines, head[:, lines.shape[1] :]], 1)

    slot = slot_ref[...]
    for _ in range(plane_slots - 1):
        slot = jnp.where(slot >= count_r, slot - count_r, slot)
    target = owner * plane_slots + slot
    dest_plane = dest_grid * plane_slots + dest_band
    wanted = jnp.where(target == dest_plane, 1.0, 0.0)
    head = jnp.concatenate(
        [head[:, :CORNER_AT], jnp.broadcast_to(corners[0:1, :], (devices, atoms_here)),
         jnp.broadcast_to(corners[1:2, :], (devices, atoms_here)),
         head[:, CORNER_AT + 2 * atoms_here : WANTED_AT], wanted], 1)
    for dest_id in range(devices):
        send_ref[dest_id, 0:1, :] = head[dest_id : dest_id + 1, :]

    atoms = proj_ref.shape[1]
    total = None
    for part in range(proj_ref.shape[0]):
        proj_t = proj_ref[part]
        left = jnp.dot(proj_t, pick_rows_ref[...], precision=PRECISE, preferred_element_type=jnp.float32)
        right = jnp.dot(proj_t, pick_cols_ref[...], precision=PRECISE, preferred_element_type=jnp.float32)
        total = left * right if total is None else total + left * right
    total = total * (factor_ref[...] * occupied)
    pairs = total.shape[1]
    send_ref[:, 1 : 1 + atoms, :] = jnp.broadcast_to(total[None, :, :LANES], (devices, atoms, LANES))
    tail = pairs - LANES
    per_row = LANES // tail
    for atom in range(atoms):
        row = 1 + atoms + atom // per_row
        start = (atom % per_row) * tail
        send_ref[:, row : row + 1, start : start + tail] = jnp.broadcast_to(
            total[None, atom : atom + 1, LANES:], (devices, 1, tail)
        )


def on_device(
    coefficients,
    occupations,
    stick_cols,
    plane_counts,
    projections,
    pair_functions,
    atom_offsets,
    piece_owner,
    piece_slot,
):
    grid_devs = lax.axis_size("grid")
    band_devs = lax.axis_size("band")
    devices = grid_devs * band_devs
    _, _, stick_local, z_length = coefficients.shape
    stick_count = stick_local * grid_devs
    plane_slots = PLANE_SLOTS

    nproj = projections.shape[2]
    pair_rows, pair_cols = np.triu_indices(nproj)
    pairs = pair_rows.shape[0]
    pick_rows = jnp.asarray((np.arange(nproj)[:, None] == pair_rows[None, :]).astype(np.float32))
    pick_cols = jnp.asarray((np.arange(nproj)[:, None] == pair_cols[None, :]).astype(np.float32))
    factor = jnp.asarray(np.where(pair_rows == pair_cols, 1.0, 2.0).astype(np.float32)[None, :])
    piece_dev = piece_owner.shape[0]
    atoms_dev = atom_offsets.shape[0]
    assert 2 * stick_local <= CORNER_AT and 2 * atoms_dev <= CORNER_LANES
    assert WANTED_AT + piece_dev == LANES and LANES < pairs < 2 * LANES
    tail = pairs - LANES
    per_row = LANES // tail
    slab_rows = 1 + atoms_dev + -(-atoms_dev // per_row)
    send = pl.pallas_call(
        functools.partial(
            pack_kernel,
            grid_devs=grid_devs,
            band_devs=band_devs,
            plane_slots=plane_slots,
            z_length=z_length,
            scale=(z_length * stick_count) ** -0.5,
        ),
        out_shape=jax.ShapeDtypeStruct((devices, slab_rows, LANES), jnp.float32),
        in_specs=[SMEM_SPEC, SMEM_SPEC] + [VMEM_SPEC] * 8,
        out_specs=VMEM_SPEC,
    )(
        plane_counts,
        occupations,
        coefficients.reshape(2 * stick_local, z_length),
        jnp.transpose(projections, (0, 1, 3, 2)).reshape(2, atoms_dev, nproj),
        piece_owner.reshape(1, piece_dev),
        piece_slot.reshape(1, piece_dev),
        pick_rows,
        pick_cols,
        factor,
        atom_offsets.T,
    )
    got = lax.all_to_all(send, ("band", "grid"), 0, 0, tiled=True)
    got = got.reshape(band_devs, grid_devs, slab_rows * LANES)
    pair_parts = []
    for atom in range(atoms_dev):
        head_at = (1 + atom) * LANES
        tail_at = (1 + atoms_dev + atom // per_row) * LANES + (atom % per_row) * tail
        pair_parts.append(
            jnp.concatenate(
                [got[:, :, head_at : head_at + LANES], got[:, :, tail_at : tail_at + tail]], 2
            )
        )
    pair_rows_got = jnp.stack(pair_parts, 2)

    lre = got[:, :, 0:stick_local].reshape(band_devs, stick_count)
    lim = got[:, :, stick_local : 2 * stick_local].reshape(band_devs, stick_count)
    row_of = stick_cols // NX
    col_of = stick_cols % NX
    y_cos, y_sin = phase_table(jnp.arange(NY, dtype=jnp.int32), row_of, NY)
    stick_live = jnp.where(stick_cols < NX * NY, 1.0, 0.0)[None, :]
    along_y = jnp.concatenate([y_cos * stick_live, y_sin * stick_live], 1)
    x_cos, x_sin = phase_table(col_of, jnp.arange(NX, dtype=jnp.int32), NX)
    b_real = lre[:, :, None] * x_cos[None] - lim[:, :, None] * x_sin[None]
    b_imag = lre[:, :, None] * x_sin[None] + lim[:, :, None] * x_cos[None]
    rhs = jnp.concatenate(
        [jnp.concatenate([b_real, b_imag], 2), jnp.concatenate([-b_imag, b_real], 2)], 1
    )
    wave = jnp.einsum("yk,bkx->byx", along_y, rhs, precision=THREE_PASS)
    valence = jnp.sum(wave[:, :, :NX] ** 2 + wave[:, :, NX:] ** 2, 0)

    head_row = got[0, :, CORNER_AT : WANTED_AT + piece_dev]
    wanted_here = head_row[:, WANTED_AT - CORNER_AT :]
    pair_len = atoms_dev * pairs
    pair_sum = jnp.sum(pair_rows_got, 0).reshape(-1, pairs)
    corner = head_row[:, : 2 * atoms_dev].reshape(grid_devs, 2, atoms_dev)
    corner = jnp.transpose(corner, (0, 2, 1)).reshape(-1, 2)
    box_depth = pair_functions.shape[1]
    box_cells = pair_functions.shape[2]
    atoms = pair_sum.shape[0]
    flat_functions = pair_functions.reshape(pairs * box_depth, box_cells)
    mask = wanted_here.reshape(atoms, box_depth)
    weights = (pair_sum[:, :, None] * mask[:, None, :]).reshape(atoms, pairs * box_depth)
    boxes = jnp.dot(weights, flat_functions, precision=THREE_PASS).reshape(atoms, BY, BX)
    col_ids = jnp.arange(NX, dtype=jnp.float32)
    row_ids = jnp.arange(NY, dtype=jnp.float32)
    box_cols = jnp.arange(BX, dtype=jnp.float32)
    box_rows = jnp.arange(BY, dtype=jnp.float32)
    col_place = (
        jnp.mod(corner[:, 1:2, None] + box_cols[None, :, None], NX) == col_ids[None, None, :]
    ).astype(jnp.float32)
    widened = jnp.einsum("aij,ajx->aix", boxes, col_place, precision=THREE_PASS)
    row_place = (
        jnp.mod(corner[:, 0:1, None] + box_rows[None, :, None], NY) == row_ids[None, None, :]
    ).astype(jnp.float32)
    augment = jnp.einsum("aiy,aix->yx", row_place, widened, precision=THREE_PASS)
    density = valence + augment
    return density.reshape(1, 1, NY, NX)


def solution(mesh):
    in_specs = (
        P("band", None, "grid", None),
        P("band"),
        P(),
        P(),
        P("band", None, None, "grid"),
        P(),
        P("grid", None),
        P("grid", None),
        P("grid"),
    )
    out_specs = P("grid", "band", None, None)
    return jax.shard_map(
        on_device, mesh=mesh, in_specs=in_specs, out_specs=out_specs, check_vma=False
    )
```

```python
import functools
import math

import jax
import jax.numpy as jnp
import numpy as np
from jax import lax
from jax.experimental import pallas as pl
from jax.experimental.pallas import tpu as pltpu
from jax.sharding import PartitionSpec as P

NX = 256
NY = 256
PLANE_SLOTS = 4
BY = 16
BX = 16


PRECISE = lax.Precision.HIGHEST
THREE_PASS = lax.Precision.HIGH


def phase_table(left, right, length):
    phase_int = left[:, None] * right[None, :] % length
    phases = phase_int.astype(jnp.float32) * (2.0 * math.pi / length)
    return jnp.cos(phases), jnp.sin(phases)


SMEM_SPEC = pl.BlockSpec(memory_space=pltpu.SMEM)
CORNER_AT = 32
CORNER_LANES = 32
WANTED_AT = 64
LANES = 128
VMEM_SPEC = pl.BlockSpec(memory_space=pltpu.VMEM)


def pack_kernel(
    counts_ref,
    occ_ref,
    coef_ref,
    proj_ref,
    owner_ref,
    slot_ref,
    pick_rows_ref,
    pick_cols_ref,
    factor_ref,
    corner_ref,
    send_ref,
    *,
    grid_devs,
    band_devs,
    plane_slots,
    z_length,
    scale,
):
    devices = grid_devs * band_devs
    occupied = occ_ref[0]
    dest = lax.broadcasted_iota(jnp.int32, (devices, 1), 0)
    dest_grid = dest % grid_devs
    dest_band = dest // grid_devs
    owner = owner_ref[...]
    count_d = jnp.zeros((devices, 1), jnp.int32)
    offset_d = jnp.zeros((devices, 1), jnp.int32)
    count_r = jnp.zeros(owner.shape, jnp.int32)
    for g in range(grid_devs):
        count = counts_ref[g]
        count_d = count_d + jnp.where(dest_grid == g, count, 0)
        offset_d = offset_d + jnp.where(dest_grid > g, count, 0)
        count_r = count_r + jnp.where(owner == g, count, 0)
    live = dest_band < count_d
    plane_z = jnp.where(live, offset_d + dest_band, 0)
    weight = jnp.where(live, jnp.sqrt(occupied) * scale, 0.0)
    freq = lax.broadcasted_iota(jnp.int32, (1, z_length), 1)
    phases = ((plane_z * freq) % z_length).astype(jnp.float32) * (2.0 * math.pi / z_length)
    coef = coef_ref[...]
    half = coef.shape[0] // 2
    swapped = jnp.concatenate([-coef[half:], coef[:half]], 0)
    contract_last = (((1,), (1,)), ((), ()))
    lines = lax.dot_general(
        jnp.cos(phases), coef, contract_last, precision=PRECISE, preferred_element_type=jnp.float32
    ) + lax.dot_general(
        jnp.sin(phases), swapped, contract_last, precision=PRECISE, preferred_element_type=jnp.float32
    )
    send_ref[...] = jnp.zeros(send_ref.shape, jnp.float32)
    lines = lines * weight
    corners = corner_ref[...].astype(jnp.float32)
    atoms_here = corners.shape[1]
    head = jnp.zeros((devices, LANES), jnp.float32)
    head = jnp.concatenate([lines, head[:, lines.shape[1] :]], 1)

    slot = slot_ref[...]
    for _ in range(plane_slots - 1):
        slot = jnp.where(slot >= count_r, slot - count_r, slot)
    target = owner * plane_slots + slot
    dest_plane = dest_grid * plane_slots + dest_band
    wanted = jnp.where(target == dest_plane, 1.0, 0.0)
    head = jnp.concatenate(
        [head[:, :CORNER_AT], jnp.broadcast_to(corners[0:1, :], (devices, atoms_here)),
         jnp.broadcast_to(corners[1:2, :], (devices, atoms_here)),
         head[:, CORNER_AT + 2 * atoms_here : WANTED_AT], wanted], 1)
    for dest_id in range(devices):
        send_ref[dest_id, 0:1, :] = head[dest_id : dest_id + 1, :]

    atoms = proj_ref.shape[1]
    total = None
    for part in range(proj_ref.shape[0]):
        proj_t = proj_ref[part]
        left = jnp.dot(proj_t, pick_rows_ref[...], precision=PRECISE, preferred_element_type=jnp.float32)
        right = jnp.dot(proj_t, pick_cols_ref[...], precision=PRECISE, preferred_element_type=jnp.float32)
        total = left * right if total is None else total + left * right
    total = total * (factor_ref[...] * occupied)
    pairs = total.shape[1]
    send_ref[:, 1 : 1 + atoms, :] = jnp.broadcast_to(total[None, :, :LANES], (devices, atoms, LANES))
    tail = pairs - LANES
    per_row = LANES // tail
    for atom in range(atoms):
        row = 1 + atoms + atom // per_row
        start = (atom % per_row) * tail
        send_ref[:, row : row + 1, start : start + tail] = jnp.broadcast_to(
            total[None, atom : atom + 1, LANES:], (devices, 1, tail)
        )


def on_device(
    coefficients,
    occupations,
    stick_cols,
    plane_counts,
    projections,
    pair_functions,
    atom_offsets,
    piece_owner,
    piece_slot,
):
    grid_devs = lax.axis_size("grid")
    band_devs = lax.axis_size("band")
    devices = grid_devs * band_devs
    _, _, stick_local, z_length = coefficients.shape
    stick_count = stick_local * grid_devs
    plane_slots = PLANE_SLOTS

    nproj = projections.shape[2]
    pair_rows, pair_cols = np.triu_indices(nproj)
    pairs = pair_rows.shape[0]
    pick_rows = jnp.asarray((np.arange(nproj)[:, None] == pair_rows[None, :]).astype(np.float32))
    pick_cols = jnp.asarray((np.arange(nproj)[:, None] == pair_cols[None, :]).astype(np.float32))
    factor = jnp.asarray(np.where(pair_rows == pair_cols, 1.0, 2.0).astype(np.float32)[None, :])
    piece_dev = piece_owner.shape[0]
    atoms_dev = atom_offsets.shape[0]
    assert 2 * stick_local <= CORNER_AT and 2 * atoms_dev <= CORNER_LANES
    assert WANTED_AT + piece_dev == LANES and LANES < pairs < 2 * LANES
    tail = pairs - LANES
    per_row = LANES // tail
    slab_rows = 1 + atoms_dev + -(-atoms_dev // per_row)
    send = pl.pallas_call(
        functools.partial(
            pack_kernel,
            grid_devs=grid_devs,
            band_devs=band_devs,
            plane_slots=plane_slots,
            z_length=z_length,
            scale=(z_length * stick_count) ** -0.5,
        ),
        out_shape=jax.ShapeDtypeStruct((devices, slab_rows, LANES), jnp.float32),
        in_specs=[SMEM_SPEC, SMEM_SPEC] + [VMEM_SPEC] * 8,
        out_specs=VMEM_SPEC,
    )(
        plane_counts,
        occupations,
        coefficients.reshape(2 * stick_local, z_length),
        jnp.transpose(projections, (0, 1, 3, 2)).reshape(2, atoms_dev, nproj),
        piece_owner.reshape(1, piece_dev),
        piece_slot.reshape(1, piece_dev),
        pick_rows,
        pick_cols,
        factor,
        atom_offsets.T,
    )
    got = lax.all_to_all(send, ("band", "grid"), 0, 0, tiled=True)
    got = got.reshape(band_devs, grid_devs, slab_rows * LANES)
    pair_parts = []
    for atom in range(atoms_dev):
        head_at = (1 + atom) * LANES
        tail_at = (1 + atoms_dev + atom // per_row) * LANES + (atom % per_row) * tail
        pair_parts.append(
            jnp.concatenate(
                [got[:, :, head_at : head_at + LANES], got[:, :, tail_at : tail_at + tail]], 2
            )
        )
    pair_rows_got = jnp.stack(pair_parts, 2)

    lre = got[:, :, 0:stick_local].reshape(band_devs, stick_count)
    lim = got[:, :, stick_local : 2 * stick_local].reshape(band_devs, stick_count)
    row_of = stick_cols // NX
    col_of = stick_cols % NX
    y_cos, y_sin = phase_table(jnp.arange(NY, dtype=jnp.int32), row_of, NY)
    stick_live = jnp.where(stick_cols < NX * NY, 1.0, 0.0)[None, :]
    along_y = jnp.concatenate([y_cos * stick_live, y_sin * stick_live], 1)
    x_cos, x_sin = phase_table(col_of, jnp.arange(NX, dtype=jnp.int32), NX)
    b_real = lre[:, :, None] * x_cos[None] - lim[:, :, None] * x_sin[None]
    b_imag = lre[:, :, None] * x_sin[None] + lim[:, :, None] * x_cos[None]
    rhs = jnp.concatenate(
        [jnp.concatenate([b_real, b_imag], 2), jnp.concatenate([-b_imag, b_real], 2)], 1
    )
    wave = jnp.einsum("yk,bkx->byx", along_y, rhs, precision=THREE_PASS)
    valence = jnp.sum(wave[:, :, :NX] ** 2 + wave[:, :, NX:] ** 2, 0)

    head_row = got[0, :, CORNER_AT : WANTED_AT + piece_dev]
    wanted_here = head_row[:, WANTED_AT - CORNER_AT :]
    pair_len = atoms_dev * pairs
    pair_sum = jnp.sum(pair_rows_got, 0).reshape(-1, pairs)
    corner = head_row[:, : 2 * atoms_dev].reshape(grid_devs, 2, atoms_dev)
    corner = jnp.transpose(corner, (0, 2, 1)).reshape(-1, 2)
    box_depth = pair_functions.shape[1]
    box_cells = pair_functions.shape[2]
    atoms = pair_sum.shape[0]
    flat_functions = pair_functions.reshape(pairs * box_depth, box_cells)
    mask = wanted_here.reshape(atoms, box_depth)
    weights = (pair_sum[:, :, None] * mask[:, None, :]).reshape(atoms, pairs * box_depth)
    boxes = jnp.dot(weights, flat_functions, precision=THREE_PASS).reshape(atoms, BY, BX)
    col_ids = jnp.arange(NX, dtype=jnp.float32)
    row_ids = jnp.arange(NY, dtype=jnp.float32)
    box_cols = jnp.arange(BX, dtype=jnp.float32)
    box_rows = jnp.arange(BY, dtype=jnp.float32)
    col_place = (
        jnp.mod(corner[:, 1:2, None] + box_cols[None, :, None], NX) == col_ids[None, None, :]
    ).astype(jnp.float32)
    widened = jnp.einsum("aij,ajx->aix", boxes, col_place, precision=THREE_PASS)
    row_place = (
        jnp.mod(corner[:, 0:1, None] + box_rows[None, :, None], NY) == row_ids[None, None, :]
    ).astype(jnp.float32)
    widened_hi = lax.reduce_precision(widened, exponent_bits=8, mantissa_bits=7)
    augment = jnp.einsum(
        "aiy,aix->yx",
        jnp.concatenate([row_place, row_place], 0),
        jnp.concatenate([widened_hi, widened - widened_hi], 0),
        precision=lax.Precision.DEFAULT,
        preferred_element_type=jnp.float32,
    )
    density = valence + augment
    return density.reshape(1, 1, NY, NX)


def solution(mesh):
    in_specs = (
        P("band", None, "grid", None),
        P("band"),
        P(),
        P(),
        P("band", None, None, "grid"),
        P(),
        P("grid", None),
        P("grid", None),
        P("grid"),
    )
    out_specs = P("grid", "band", None, None)
    return jax.shard_map(
        on_device, mesh=mesh, in_specs=in_specs, out_specs=out_specs, check_vma=False
    )
```

```python
import functools
import math

import jax
import jax.numpy as jnp
import numpy as np
from jax import lax
from jax.experimental import pallas as pl
from jax.experimental.pallas import tpu as pltpu
from jax.sharding import PartitionSpec as P

NX = 256
NY = 256
PLANE_SLOTS = 4
BY = 16
BX = 16


PRECISE = lax.Precision.HIGHEST
THREE_PASS = lax.Precision.HIGH


def phase_table(left, right, length):
    phase_int = left[:, None] * right[None, :] % length
    phases = phase_int.astype(jnp.float32) * (2.0 * math.pi / length)
    return jnp.cos(phases), jnp.sin(phases)


SMEM_SPEC = pl.BlockSpec(memory_space=pltpu.SMEM)
CORNER_AT = 32
CORNER_LANES = 32
WANTED_AT = 64
LANES = 128
VMEM_SPEC = pl.BlockSpec(memory_space=pltpu.VMEM)


def pack_kernel(
    counts_ref,
    occ_ref,
    coef_ref,
    proj_ref,
    owner_ref,
    slot_ref,
    pick_rows_ref,
    pick_cols_ref,
    factor_ref,
    corner_ref,
    send_ref,
    *,
    grid_devs,
    band_devs,
    plane_slots,
    z_length,
    scale,
):
    devices = grid_devs * band_devs
    occupied = occ_ref[0]
    dest = lax.broadcasted_iota(jnp.int32, (devices, 1), 0)
    dest_grid = dest % grid_devs
    dest_band = dest // grid_devs
    owner = owner_ref[...]
    count_d = jnp.zeros((devices, 1), jnp.int32)
    offset_d = jnp.zeros((devices, 1), jnp.int32)
    count_r = jnp.zeros(owner.shape, jnp.int32)
    for g in range(grid_devs):
        count = counts_ref[g]
        count_d = count_d + jnp.where(dest_grid == g, count, 0)
        offset_d = offset_d + jnp.where(dest_grid > g, count, 0)
        count_r = count_r + jnp.where(owner == g, count, 0)
    live = dest_band < count_d
    plane_z = jnp.where(live, offset_d + dest_band, 0)
    weight = jnp.where(live, jnp.sqrt(occupied) * scale, 0.0)
    freq = lax.broadcasted_iota(jnp.int32, (1, z_length), 1)
    phases = ((plane_z * freq) % z_length).astype(jnp.float32) * (2.0 * math.pi / z_length)
    coef = coef_ref[...]
    half = coef.shape[0] // 2
    swapped = jnp.concatenate([-coef[half:], coef[:half]], 0)
    contract_last = (((1,), (1,)), ((), ()))
    lines = lax.dot_general(
        jnp.cos(phases), coef, contract_last, precision=PRECISE, preferred_element_type=jnp.float32
    ) + lax.dot_general(
        jnp.sin(phases), swapped, contract_last, precision=PRECISE, preferred_element_type=jnp.float32
    )
    send_ref[...] = jnp.zeros(send_ref.shape, jnp.float32)
    lines = lines * weight
    corners = corner_ref[...].astype(jnp.float32)
    atoms_here = corners.shape[1]
    head = jnp.zeros((devices, LANES), jnp.float32)
    head = jnp.concatenate([lines, head[:, lines.shape[1] :]], 1)

    slot = slot_ref[...]
    for _ in range(plane_slots - 1):
        slot = jnp.where(slot >= count_r, slot - count_r, slot)
    target = owner * plane_slots + slot
    dest_plane = dest_grid * plane_slots + dest_band
    wanted = jnp.where(target == dest_plane, 1.0, 0.0)
    head = jnp.concatenate(
        [head[:, :CORNER_AT], jnp.broadcast_to(corners[0:1, :], (devices, atoms_here)),
         jnp.broadcast_to(corners[1:2, :], (devices, atoms_here)),
         head[:, CORNER_AT + 2 * atoms_here : WANTED_AT], wanted], 1)
    send_ref[:, 0:1, :] = head.reshape(devices, 1, LANES)

    atoms = proj_ref.shape[1]
    total = None
    for part in range(proj_ref.shape[0]):
        proj_t = proj_ref[part]
        left = jnp.dot(proj_t, pick_rows_ref[...], precision=PRECISE, preferred_element_type=jnp.float32)
        right = jnp.dot(proj_t, pick_cols_ref[...], precision=PRECISE, preferred_element_type=jnp.float32)
        total = left * right if total is None else total + left * right
    total = total * (factor_ref[...] * occupied)
    pairs = total.shape[1]
    send_ref[:, 1 : 1 + atoms, :] = jnp.broadcast_to(total[None, :, :LANES], (devices, atoms, LANES))
    tail = pairs - LANES
    per_row = LANES // tail
    for atom in range(atoms):
        row = 1 + atoms + atom // per_row
        start = (atom % per_row) * tail
        send_ref[:, row : row + 1, start : start + tail] = jnp.broadcast_to(
            total[None, atom : atom + 1, LANES:], (devices, 1, tail)
        )


def on_device(
    coefficients,
    occupations,
    stick_cols,
    plane_counts,
    projections,
    pair_functions,
    atom_offsets,
    piece_owner,
    piece_slot,
):
    grid_devs = lax.axis_size("grid")
    band_devs = lax.axis_size("band")
    devices = grid_devs * band_devs
    _, _, stick_local, z_length = coefficients.shape
    stick_count = stick_local * grid_devs
    plane_slots = PLANE_SLOTS

    nproj = projections.shape[2]
    pair_rows, pair_cols = np.triu_indices(nproj)
    pairs = pair_rows.shape[0]
    pick_rows = jnp.asarray((np.arange(nproj)[:, None] == pair_rows[None, :]).astype(np.float32))
    pick_cols = jnp.asarray((np.arange(nproj)[:, None] == pair_cols[None, :]).astype(np.float32))
    factor = jnp.asarray(np.where(pair_rows == pair_cols, 1.0, 2.0).astype(np.float32)[None, :])
    piece_dev = piece_owner.shape[0]
    atoms_dev = atom_offsets.shape[0]
    assert 2 * stick_local <= CORNER_AT and 2 * atoms_dev <= CORNER_LANES
    assert WANTED_AT + piece_dev == LANES and LANES < pairs < 2 * LANES
    tail = pairs - LANES
    per_row = LANES // tail
    slab_rows = 1 + atoms_dev + -(-atoms_dev // per_row)
    send = pl.pallas_call(
        functools.partial(
            pack_kernel,
            grid_devs=grid_devs,
            band_devs=band_devs,
            plane_slots=plane_slots,
            z_length=z_length,
            scale=(z_length * stick_count) ** -0.5,
        ),
        out_shape=jax.ShapeDtypeStruct((devices, slab_rows, LANES), jnp.float32),
        in_specs=[SMEM_SPEC, SMEM_SPEC] + [VMEM_SPEC] * 8,
        out_specs=VMEM_SPEC,
    )(
        plane_counts,
        occupations,
        coefficients.reshape(2 * stick_local, z_length),
        jnp.transpose(projections, (0, 1, 3, 2)).reshape(2, atoms_dev, nproj),
        piece_owner.reshape(1, piece_dev),
        piece_slot.reshape(1, piece_dev),
        pick_rows,
        pick_cols,
        factor,
        atom_offsets.T,
    )
    got = lax.all_to_all(send, ("band", "grid"), 0, 0, tiled=True)
    got = got.reshape(band_devs, grid_devs, slab_rows * LANES)
    pair_parts = []
    for atom in range(atoms_dev):
        head_at = (1 + atom) * LANES
        tail_at = (1 + atoms_dev + atom // per_row) * LANES + (atom % per_row) * tail
        pair_parts.append(
            jnp.concatenate(
                [got[:, :, head_at : head_at + LANES], got[:, :, tail_at : tail_at + tail]], 2
            )
        )
    pair_rows_got = jnp.stack(pair_parts, 2)

    lre = got[:, :, 0:stick_local].reshape(band_devs, stick_count)
    lim = got[:, :, stick_local : 2 * stick_local].reshape(band_devs, stick_count)
    row_of = stick_cols // NX
    col_of = stick_cols % NX
    y_cos, y_sin = phase_table(jnp.arange(NY, dtype=jnp.int32), row_of, NY)
    stick_live = jnp.where(stick_cols < NX * NY, 1.0, 0.0)[None, :]
    along_y = jnp.concatenate([y_cos * stick_live, y_sin * stick_live], 1)
    x_cos, x_sin = phase_table(col_of, jnp.arange(NX, dtype=jnp.int32), NX)
    b_real = lre[:, :, None] * x_cos[None] - lim[:, :, None] * x_sin[None]
    b_imag = lre[:, :, None] * x_sin[None] + lim[:, :, None] * x_cos[None]
    rhs = jnp.concatenate(
        [jnp.concatenate([b_real, b_imag], 2), jnp.concatenate([-b_imag, b_real], 2)], 1
    )
    wave = jnp.einsum("yk,bkx->byx", along_y, rhs, precision=THREE_PASS)
    valence = jnp.sum(wave[:, :, :NX] ** 2 + wave[:, :, NX:] ** 2, 0)

    head_row = got[0, :, CORNER_AT : WANTED_AT + piece_dev]
    wanted_here = head_row[:, WANTED_AT - CORNER_AT :]
    pair_len = atoms_dev * pairs
    pair_sum = jnp.sum(pair_rows_got, 0).reshape(-1, pairs)
    corner = head_row[:, : 2 * atoms_dev].reshape(grid_devs, 2, atoms_dev)
    corner = jnp.transpose(corner, (0, 2, 1)).reshape(-1, 2)
    box_depth = pair_functions.shape[1]
    box_cells = pair_functions.shape[2]
    atoms = pair_sum.shape[0]
    flat_functions = pair_functions.reshape(pairs * box_depth, box_cells)
    mask = wanted_here.reshape(atoms, box_depth)
    weights = (pair_sum[:, :, None] * mask[:, None, :]).reshape(atoms, pairs * box_depth)
    boxes = jnp.dot(weights, flat_functions, precision=THREE_PASS).reshape(atoms, BY, BX)
    col_ids = jnp.arange(NX, dtype=jnp.float32)
    row_ids = jnp.arange(NY, dtype=jnp.float32)
    box_cols = jnp.arange(BX, dtype=jnp.float32)
    box_rows = jnp.arange(BY, dtype=jnp.float32)
    col_place = (
        jnp.mod(corner[:, 1:2, None] + box_cols[None, :, None], NX) == col_ids[None, None, :]
    ).astype(jnp.float32)
    widened = jnp.einsum("aij,ajx->aix", boxes, col_place, precision=THREE_PASS)
    row_place = (
        jnp.mod(corner[:, 0:1, None] + box_rows[None, :, None], NY) == row_ids[None, None, :]
    ).astype(jnp.float32)
    augment = jnp.einsum("aiy,aix->yx", row_place, widened, precision=THREE_PASS)
    density = valence + augment
    return density.reshape(1, 1, NY, NX)


def solution(mesh):
    in_specs = (
        P("band", None, "grid", None),
        P("band"),
        P(),
        P(),
        P("band", None, None, "grid"),
        P(),
        P("grid", None),
        P("grid", None),
        P("grid"),
    )
    out_specs = P("grid", "band", None, None)
    return jax.shard_map(
        on_device, mesh=mesh, in_specs=in_specs, out_specs=out_specs, check_vma=False
    )
```

```python
import functools
import math

import jax
import jax.numpy as jnp
import numpy as np
from jax import lax
from jax.experimental import pallas as pl
from jax.experimental.pallas import tpu as pltpu
from jax.sharding import PartitionSpec as P

NX = 256
NY = 256
PLANE_SLOTS = 4
BY = 16
BX = 16


PRECISE = lax.Precision.HIGHEST
THREE_PASS = lax.Precision.HIGH


def phase_table(left, right, length):
    phase_int = left[:, None] * right[None, :] % length
    phases = phase_int.astype(jnp.float32) * (2.0 * math.pi / length)
    return jnp.cos(phases), jnp.sin(phases)


SMEM_SPEC = pl.BlockSpec(memory_space=pltpu.SMEM)
CORNER_AT = 32
CORNER_LANES = 32
WANTED_AT = 64
LANES = 128
VMEM_SPEC = pl.BlockSpec(memory_space=pltpu.VMEM)


def pack_kernel(
    counts_ref,
    occ_ref,
    coef_ref,
    proj_ref,
    owner_ref,
    slot_ref,
    pick_rows_ref,
    pick_cols_ref,
    factor_ref,
    corner_ref,
    send_ref,
    *,
    grid_devs,
    band_devs,
    plane_slots,
    z_length,
    scale,
):
    devices = grid_devs * band_devs
    occupied = occ_ref[0]
    dest = lax.broadcasted_iota(jnp.int32, (devices, 1), 0)
    dest_grid = dest % grid_devs
    dest_band = dest // grid_devs
    owner = owner_ref[...]
    count_d = jnp.zeros((devices, 1), jnp.int32)
    offset_d = jnp.zeros((devices, 1), jnp.int32)
    count_r = jnp.zeros(owner.shape, jnp.int32)
    for g in range(grid_devs):
        count = counts_ref[g]
        count_d = count_d + jnp.where(dest_grid == g, count, 0)
        offset_d = offset_d + jnp.where(dest_grid > g, count, 0)
        count_r = count_r + jnp.where(owner == g, count, 0)
    live = dest_band < count_d
    plane_z = jnp.where(live, offset_d + dest_band, 0)
    weight = jnp.where(live, jnp.sqrt(occupied) * scale, 0.0)
    freq = lax.broadcasted_iota(jnp.int32, (1, z_length), 1)
    phases = ((plane_z * freq) % z_length).astype(jnp.float32) * (2.0 * math.pi / z_length)
    coef = coef_ref[...]
    half = coef.shape[0] // 2
    swapped = jnp.concatenate([-coef[half:], coef[:half]], 0)
    contract_last = (((1,), (1,)), ((), ()))
    lines = lax.dot_general(
        jnp.cos(phases), coef, contract_last, precision=PRECISE, preferred_element_type=jnp.float32
    ) + lax.dot_general(
        jnp.sin(phases), swapped, contract_last, precision=PRECISE, preferred_element_type=jnp.float32
    )
    send_ref[...] = jnp.zeros(send_ref.shape, jnp.float32)
    lines = lines * weight
    corners = corner_ref[...].astype(jnp.float32)
    atoms_here = corners.shape[1]
    head = jnp.zeros((devices, LANES), jnp.float32)
    head = jnp.concatenate([lines, head[:, lines.shape[1] :]], 1)

    slot = slot_ref[...]
    for _ in range(plane_slots - 1):
        slot = jnp.where(slot >= count_r, slot - count_r, slot)
    target = owner * plane_slots + slot
    dest_plane = dest_grid * plane_slots + dest_band
    wanted = jnp.where(target == dest_plane, 1.0, 0.0)
    head = jnp.concatenate(
        [head[:, :CORNER_AT], jnp.broadcast_to(corners[0:1, :], (devices, atoms_here)),
         jnp.broadcast_to(corners[1:2, :], (devices, atoms_here)),
         head[:, CORNER_AT + 2 * atoms_here : WANTED_AT], wanted], 1)
    send_ref[:, 0:1, :] = head.reshape(devices, 1, LANES)

    atoms = proj_ref.shape[1]
    total = None
    for part in range(proj_ref.shape[0]):
        proj_t = proj_ref[part]
        left = jnp.dot(proj_t, pick_rows_ref[...], precision=PRECISE, preferred_element_type=jnp.float32)
        right = jnp.dot(proj_t, pick_cols_ref[...], precision=PRECISE, preferred_element_type=jnp.float32)
        total = left * right if total is None else total + left * right
    total = total * (factor_ref[...] * occupied)
    pairs = total.shape[1]
    send_ref[:, 1 : 1 + atoms, :] = jnp.broadcast_to(total[None, :, :LANES], (devices, atoms, LANES))
    tail = pairs - LANES
    per_row = LANES // tail
    for atom in range(atoms):
        row = 1 + atoms + atom // per_row
        start = (atom % per_row) * tail
        send_ref[:, row : row + 1, start : start + tail] = jnp.broadcast_to(
            total[None, atom : atom + 1, LANES:], (devices, 1, tail)
        )


def on_device(
    coefficients,
    occupations,
    stick_cols,
    plane_counts,
    projections,
    pair_functions,
    atom_offsets,
    piece_owner,
    piece_slot,
):
    grid_devs = lax.axis_size("grid")
    band_devs = lax.axis_size("band")
    devices = grid_devs * band_devs
    _, _, stick_local, z_length = coefficients.shape
    stick_count = stick_local * grid_devs
    plane_slots = PLANE_SLOTS

    nproj = projections.shape[2]
    pair_rows, pair_cols = np.triu_indices(nproj)
    pairs = pair_rows.shape[0]
    pick_rows = jnp.asarray((np.arange(nproj)[:, None] == pair_rows[None, :]).astype(np.float32))
    pick_cols = jnp.asarray((np.arange(nproj)[:, None] == pair_cols[None, :]).astype(np.float32))
    factor = jnp.asarray(np.where(pair_rows == pair_cols, 1.0, 2.0).astype(np.float32)[None, :])
    piece_dev = piece_owner.shape[0]
    atoms_dev = atom_offsets.shape[0]
    assert 2 * stick_local <= CORNER_AT and 2 * atoms_dev <= CORNER_LANES
    assert WANTED_AT + piece_dev == LANES and LANES < pairs < 2 * LANES
    tail = pairs - LANES
    per_row = LANES // tail
    slab_rows = 1 + atoms_dev + -(-atoms_dev // per_row)
    send = pl.pallas_call(
        functools.partial(
            pack_kernel,
            grid_devs=grid_devs,
            band_devs=band_devs,
            plane_slots=plane_slots,
            z_length=z_length,
            scale=(z_length * stick_count) ** -0.5,
        ),
        out_shape=jax.ShapeDtypeStruct((devices, slab_rows, LANES), jnp.float32),
        in_specs=[SMEM_SPEC, SMEM_SPEC] + [VMEM_SPEC] * 8,
        out_specs=VMEM_SPEC,
    )(
        plane_counts,
        occupations,
        coefficients.reshape(2 * stick_local, z_length),
        jnp.transpose(projections, (0, 1, 3, 2)).reshape(2, atoms_dev, nproj),
        piece_owner.reshape(1, piece_dev),
        piece_slot.reshape(1, piece_dev),
        pick_rows,
        pick_cols,
        factor,
        atom_offsets.T,
    )
    got = lax.all_to_all(send, ("band", "grid"), 0, 0, tiled=True)
    got = got.reshape(band_devs, grid_devs, slab_rows * LANES)
    pair_parts = []
    for atom in range(atoms_dev):
        head_at = (1 + atom) * LANES
        tail_at = (1 + atoms_dev + atom // per_row) * LANES + (atom % per_row) * tail
        pair_parts.append(
            jnp.concatenate(
                [got[:, :, head_at : head_at + LANES], got[:, :, tail_at : tail_at + tail]], 2
            )
        )
    pair_rows_got = jnp.stack(pair_parts, 2)

    lre = got[:, :, 0:stick_local].reshape(band_devs, stick_count)
    lim = got[:, :, stick_local : 2 * stick_local].reshape(band_devs, stick_count)
    row_of = stick_cols // NX
    col_of = stick_cols % NX
    y_cos, y_sin = phase_table(jnp.arange(NY, dtype=jnp.int32), row_of, NY)
    stick_live = jnp.where(stick_cols < NX * NY, 1.0, 0.0)[None, :]
    along_y = jnp.concatenate([y_cos * stick_live, y_sin * stick_live], 1)
    x_cos, x_sin = phase_table(col_of, jnp.arange(NX, dtype=jnp.int32), NX)
    b_real = lre[:, :, None] * x_cos[None] - lim[:, :, None] * x_sin[None]
    b_imag = lre[:, :, None] * x_sin[None] + lim[:, :, None] * x_cos[None]
    rhs = jnp.concatenate(
        [jnp.concatenate([b_real, b_imag], 2), jnp.concatenate([-b_imag, b_real], 2)], 1
    )
    wave = jnp.einsum("yk,bkx->byx", along_y, rhs, precision=THREE_PASS)
    valence = jnp.sum(wave[:, :, :NX] ** 2 + wave[:, :, NX:] ** 2, 0)

    head_row = got[0, :, CORNER_AT : WANTED_AT + piece_dev]
    wanted_here = head_row[:, WANTED_AT - CORNER_AT :]
    pair_len = atoms_dev * pairs
    pair_sum = jnp.sum(pair_rows_got, 0).reshape(-1, pairs)
    corner = head_row[:, : 2 * atoms_dev].reshape(grid_devs, 2, atoms_dev)
    corner = jnp.transpose(corner, (0, 2, 1)).reshape(-1, 2)
    box_depth = pair_functions.shape[1]
    box_cells = pair_functions.shape[2]
    atoms = pair_sum.shape[0]
    flat_functions = pair_functions.reshape(pairs * box_depth, box_cells)
    mask = wanted_here.reshape(atoms, box_depth)
    weights = (pair_sum[:, :, None] * mask[:, None, :]).reshape(atoms, pairs * box_depth)
    boxes_t = lax.dot_general(
        flat_functions, weights, (((0,), (1,)), ((), ())), precision=THREE_PASS
    )
    boxes = boxes_t.T.reshape(atoms, BY, BX)
    col_ids = jnp.arange(NX, dtype=jnp.float32)
    row_ids = jnp.arange(NY, dtype=jnp.float32)
    box_cols = jnp.arange(BX, dtype=jnp.float32)
    box_rows = jnp.arange(BY, dtype=jnp.float32)
    col_place = (
        jnp.mod(corner[:, 1:2, None] + box_cols[None, :, None], NX) == col_ids[None, None, :]
    ).astype(jnp.float32)
    widened = jnp.einsum("aij,ajx->aix", boxes, col_place, precision=THREE_PASS)
    row_place = (
        jnp.mod(corner[:, 0:1, None] + box_rows[None, :, None], NY) == row_ids[None, None, :]
    ).astype(jnp.float32)
    augment = jnp.einsum("aiy,aix->yx", row_place, widened, precision=THREE_PASS)
    density = valence + augment
    return density.reshape(1, 1, NY, NX)


def solution(mesh):
    in_specs = (
        P("band", None, "grid", None),
        P("band"),
        P(),
        P(),
        P("band", None, None, "grid"),
        P(),
        P("grid", None),
        P("grid", None),
        P("grid"),
    )
    out_specs = P("grid", "band", None, None)
    return jax.shard_map(
        on_device, mesh=mesh, in_specs=in_specs, out_specs=out_specs, check_vma=False
    )
```

```python
import functools
import math

import jax
import jax.numpy as jnp
import numpy as np
from jax import lax
from jax.experimental import pallas as pl
from jax.experimental.pallas import tpu as pltpu
from jax.sharding import PartitionSpec as P

NX = 256
NY = 256
PLANE_SLOTS = 4
BY = 16
BX = 16


PRECISE = lax.Precision.HIGHEST
THREE_PASS = lax.Precision.HIGH


def phase_table(left, right, length):
    phase_int = left[:, None] * right[None, :] % length
    phases = phase_int.astype(jnp.float32) * (2.0 * math.pi / length)
    return jnp.cos(phases), jnp.sin(phases)


SMEM_SPEC = pl.BlockSpec(memory_space=pltpu.SMEM)
CORNER_AT = 32
CORNER_LANES = 32
WANTED_AT = 64
LANES = 128
VMEM_SPEC = pl.BlockSpec(memory_space=pltpu.VMEM)


def pack_kernel(
    counts_ref,
    occ_ref,
    coef_ref,
    proj_ref,
    owner_ref,
    slot_ref,
    pick_rows_ref,
    pick_cols_ref,
    factor_ref,
    corner_ref,
    send_ref,
    *,
    grid_devs,
    band_devs,
    plane_slots,
    z_length,
    scale,
):
    devices = grid_devs * band_devs
    occupied = occ_ref[0]
    dest = lax.broadcasted_iota(jnp.int32, (devices, 1), 0)
    dest_grid = dest % grid_devs
    dest_band = dest // grid_devs
    owner = owner_ref[...]
    count_d = jnp.zeros((devices, 1), jnp.int32)
    offset_d = jnp.zeros((devices, 1), jnp.int32)
    count_r = jnp.zeros(owner.shape, jnp.int32)
    for g in range(grid_devs):
        count = counts_ref[g]
        count_d = count_d + jnp.where(dest_grid == g, count, 0)
        offset_d = offset_d + jnp.where(dest_grid > g, count, 0)
        count_r = count_r + jnp.where(owner == g, count, 0)
    live = dest_band < count_d
    plane_z = jnp.where(live, offset_d + dest_band, 0)
    weight = jnp.where(live, jnp.sqrt(occupied) * scale, 0.0)
    freq = lax.broadcasted_iota(jnp.int32, (1, z_length), 1)
    phases = ((plane_z * freq) % z_length).astype(jnp.float32) * (2.0 * math.pi / z_length)
    coef = coef_ref[...]
    half = coef.shape[0] // 2
    swapped = jnp.concatenate([-coef[half:], coef[:half]], 0)
    contract_last = (((1,), (1,)), ((), ()))
    lines = lax.dot_general(
        jnp.cos(phases), coef, contract_last, precision=PRECISE, preferred_element_type=jnp.float32
    ) + lax.dot_general(
        jnp.sin(phases), swapped, contract_last, precision=PRECISE, preferred_element_type=jnp.float32
    )
    lines = lines * weight
    corners = corner_ref[...].astype(jnp.float32)
    atoms_here = corners.shape[1]
    head = jnp.zeros((devices, LANES), jnp.float32)
    head = jnp.concatenate([lines, head[:, lines.shape[1] :]], 1)

    slot = slot_ref[...]
    for _ in range(plane_slots - 1):
        slot = jnp.where(slot >= count_r, slot - count_r, slot)
    target = owner * plane_slots + slot
    dest_plane = dest_grid * plane_slots + dest_band
    wanted = jnp.where(target == dest_plane, 1.0, 0.0)
    head = jnp.concatenate(
        [head[:, :CORNER_AT], jnp.broadcast_to(corners[0:1, :], (devices, atoms_here)),
         jnp.broadcast_to(corners[1:2, :], (devices, atoms_here)),
         head[:, CORNER_AT + 2 * atoms_here : WANTED_AT], wanted], 1)
    send_ref[:, 0:1, :] = head.reshape(devices, 1, LANES)

    atoms = proj_ref.shape[1]
    tail_rows = send_ref.shape[1] - 1 - atoms
    send_ref[:, 1 + atoms :, :] = jnp.zeros((devices, tail_rows, LANES), jnp.float32)
    total = None
    for part in range(proj_ref.shape[0]):
        proj_t = proj_ref[part]
        left = jnp.dot(proj_t, pick_rows_ref[...], precision=PRECISE, preferred_element_type=jnp.float32)
        right = jnp.dot(proj_t, pick_cols_ref[...], precision=PRECISE, preferred_element_type=jnp.float32)
        total = left * right if total is None else total + left * right
    total = total * (factor_ref[...] * occupied)
    pairs = total.shape[1]
    send_ref[:, 1 : 1 + atoms, :] = jnp.broadcast_to(total[None, :, :LANES], (devices, atoms, LANES))
    tail = pairs - LANES
    per_row = LANES // tail
    for atom in range(atoms):
        row = 1 + atoms + atom // per_row
        start = (atom % per_row) * tail
        send_ref[:, row : row + 1, start : start + tail] = jnp.broadcast_to(
            total[None, atom : atom + 1, LANES:], (devices, 1, tail)
        )


def on_device(
    coefficients,
    occupations,
    stick_cols,
    plane_counts,
    projections,
    pair_functions,
    atom_offsets,
    piece_owner,
    piece_slot,
):
    grid_devs = lax.axis_size("grid")
    band_devs = lax.axis_size("band")
    devices = grid_devs * band_devs
    _, _, stick_local, z_length = coefficients.shape
    stick_count = stick_local * grid_devs
    plane_slots = PLANE_SLOTS

    nproj = projections.shape[2]
    pair_rows, pair_cols = np.triu_indices(nproj)
    pairs = pair_rows.shape[0]
    pick_rows = jnp.asarray((np.arange(nproj)[:, None] == pair_rows[None, :]).astype(np.float32))
    pick_cols = jnp.asarray((np.arange(nproj)[:, None] == pair_cols[None, :]).astype(np.float32))
    factor = jnp.asarray(np.where(pair_rows == pair_cols, 1.0, 2.0).astype(np.float32)[None, :])
    piece_dev = piece_owner.shape[0]
    atoms_dev = atom_offsets.shape[0]
    assert 2 * stick_local <= CORNER_AT and 2 * atoms_dev <= CORNER_LANES
    assert WANTED_AT + piece_dev == LANES and LANES < pairs < 2 * LANES
    tail = pairs - LANES
    per_row = LANES // tail
    slab_rows = 1 + atoms_dev + -(-atoms_dev // per_row)
    send = pl.pallas_call(
        functools.partial(
            pack_kernel,
            grid_devs=grid_devs,
            band_devs=band_devs,
            plane_slots=plane_slots,
            z_length=z_length,
            scale=(z_length * stick_count) ** -0.5,
        ),
        out_shape=jax.ShapeDtypeStruct((devices, slab_rows, LANES), jnp.float32),
        in_specs=[SMEM_SPEC, SMEM_SPEC] + [VMEM_SPEC] * 8,
        out_specs=VMEM_SPEC,
    )(
        plane_counts,
        occupations,
        coefficients.reshape(2 * stick_local, z_length),
        jnp.transpose(projections, (0, 1, 3, 2)).reshape(2, atoms_dev, nproj),
        piece_owner.reshape(1, piece_dev),
        piece_slot.reshape(1, piece_dev),
        pick_rows,
        pick_cols,
        factor,
        atom_offsets.T,
    )
    got = lax.all_to_all(send, ("band", "grid"), 0, 0, tiled=True)
    got = got.reshape(band_devs, grid_devs, slab_rows * LANES)
    pair_parts = []
    for atom in range(atoms_dev):
        head_at = (1 + atom) * LANES
        tail_at = (1 + atoms_dev + atom // per_row) * LANES + (atom % per_row) * tail
        pair_parts.append(
            jnp.concatenate(
                [got[:, :, head_at : head_at + LANES], got[:, :, tail_at : tail_at + tail]], 2
            )
        )
    pair_rows_got = jnp.stack(pair_parts, 2)

    lre = got[:, :, 0:stick_local].reshape(band_devs, stick_count)
    lim = got[:, :, stick_local : 2 * stick_local].reshape(band_devs, stick_count)
    row_of = stick_cols // NX
    col_of = stick_cols % NX
    y_cos, y_sin = phase_table(jnp.arange(NY, dtype=jnp.int32), row_of, NY)
    stick_live = jnp.where(stick_cols < NX * NY, 1.0, 0.0)[None, :]
    along_y = jnp.concatenate([y_cos * stick_live, y_sin * stick_live], 1)
    x_cos, x_sin = phase_table(col_of, jnp.arange(NX, dtype=jnp.int32), NX)
    b_real = lre[:, :, None] * x_cos[None] - lim[:, :, None] * x_sin[None]
    b_imag = lre[:, :, None] * x_sin[None] + lim[:, :, None] * x_cos[None]
    rhs = jnp.concatenate(
        [jnp.concatenate([b_real, b_imag], 2), jnp.concatenate([-b_imag, b_real], 2)], 1
    )
    wave = jnp.einsum("yk,bkx->byx", along_y, rhs, precision=THREE_PASS)
    valence = jnp.sum(wave[:, :, :NX] ** 2 + wave[:, :, NX:] ** 2, 0)

    head_row = got[0, :, CORNER_AT : WANTED_AT + piece_dev]
    wanted_here = head_row[:, WANTED_AT - CORNER_AT :]
    pair_len = atoms_dev * pairs
    pair_sum = jnp.sum(pair_rows_got, 0).reshape(-1, pairs)
    corner = head_row[:, : 2 * atoms_dev].reshape(grid_devs, 2, atoms_dev)
    corner = jnp.transpose(corner, (0, 2, 1)).reshape(-1, 2)
    box_depth = pair_functions.shape[1]
    box_cells = pair_functions.shape[2]
    atoms = pair_sum.shape[0]
    flat_functions = pair_functions.reshape(pairs * box_depth, box_cells)
    mask = wanted_here.reshape(atoms, box_depth)
    weights = (pair_sum[:, :, None] * mask[:, None, :]).reshape(atoms, pairs * box_depth)
    boxes = jnp.dot(weights, flat_functions, precision=THREE_PASS).reshape(atoms, BY, BX)
    col_ids = jnp.arange(NX, dtype=jnp.float32)
    row_ids = jnp.arange(NY, dtype=jnp.float32)
    box_cols = jnp.arange(BX, dtype=jnp.float32)
    box_rows = jnp.arange(BY, dtype=jnp.float32)
    col_place = (
        jnp.mod(corner[:, 1:2, None] + box_cols[None, :, None], NX) == col_ids[None, None, :]
    ).astype(jnp.float32)
    widened = jnp.einsum("aij,ajx->aix", boxes, col_place, precision=THREE_PASS)
    row_place = (
        jnp.mod(corner[:, 0:1, None] + box_rows[None, :, None], NY) == row_ids[None, None, :]
    ).astype(jnp.float32)
    augment = jnp.einsum("aiy,aix->yx", row_place, widened, precision=THREE_PASS)
    density = valence + augment
    return density.reshape(1, 1, NY, NX)


def solution(mesh):
    in_specs = (
        P("band", None, "grid", None),
        P("band"),
        P(),
        P(),
        P("band", None, None, "grid"),
        P(),
        P("grid", None),
        P("grid", None),
        P("grid"),
    )
    out_specs = P("grid", "band", None, None)
    return jax.shard_map(
        on_device, mesh=mesh, in_specs=in_specs, out_specs=out_specs, check_vma=False
    )
```

```python
import functools
import math

import jax
import jax.numpy as jnp
import numpy as np
from jax import lax
from jax.experimental import pallas as pl
from jax.experimental.pallas import tpu as pltpu
from jax.sharding import PartitionSpec as P

NX = 256
NY = 256
PLANE_SLOTS = 4
BY = 16
BX = 16


PRECISE = lax.Precision.HIGHEST
THREE_PASS = lax.Precision.HIGH


def phase_table(left, right, length):
    phase_int = left[:, None] * right[None, :] % length
    phases = phase_int.astype(jnp.float32) * (2.0 * math.pi / length)
    return jnp.cos(phases), jnp.sin(phases)


SMEM_SPEC = pl.BlockSpec(memory_space=pltpu.SMEM)
CORNER_AT = 32
CORNER_LANES = 32
WANTED_AT = 64
LANES = 128
VMEM_SPEC = pl.BlockSpec(memory_space=pltpu.VMEM)


def pack_kernel(
    counts_ref,
    occ_ref,
    coef_ref,
    proj_ref,
    owner_ref,
    slot_ref,
    pick_rows_ref,
    pick_cols_ref,
    factor_ref,
    corner_ref,
    send_ref,
    *,
    grid_devs,
    band_devs,
    plane_slots,
    z_length,
    scale,
):
    devices = grid_devs * band_devs
    occupied = occ_ref[0]
    dest = lax.broadcasted_iota(jnp.int32, (devices, 1), 0)
    dest_grid = dest % grid_devs
    dest_band = dest // grid_devs
    owner = owner_ref[...]
    count_d = jnp.zeros((devices, 1), jnp.int32)
    offset_d = jnp.zeros((devices, 1), jnp.int32)
    count_r = jnp.zeros(owner.shape, jnp.int32)
    for g in range(grid_devs):
        count = counts_ref[g]
        count_d = count_d + jnp.where(dest_grid == g, count, 0)
        offset_d = offset_d + jnp.where(dest_grid > g, count, 0)
        count_r = count_r + jnp.where(owner == g, count, 0)
    live = dest_band < count_d
    plane_z = jnp.where(live, offset_d + dest_band, 0)
    weight = jnp.where(live, jnp.sqrt(occupied) * scale, 0.0)
    freq = lax.broadcasted_iota(jnp.int32, (1, z_length), 1)
    phases = ((plane_z * freq) % z_length).astype(jnp.float32) * (2.0 * math.pi / z_length)
    coef = coef_ref[...]
    half = coef.shape[0] // 2
    swapped = jnp.concatenate([-coef[half:], coef[:half]], 0)
    contract_last = (((1,), (1,)), ((), ()))
    lines = lax.dot_general(
        jnp.cos(phases), coef, contract_last, precision=THREE_PASS, preferred_element_type=jnp.float32
    ) + lax.dot_general(
        jnp.sin(phases), swapped, contract_last, precision=THREE_PASS, preferred_element_type=jnp.float32
    )
    send_ref[...] = jnp.zeros(send_ref.shape, jnp.float32)
    lines = lines * weight
    corners = corner_ref[...].astype(jnp.float32)
    atoms_here = corners.shape[1]
    head = jnp.zeros((devices, LANES), jnp.float32)
    head = jnp.concatenate([lines, head[:, lines.shape[1] :]], 1)

    slot = slot_ref[...]
    for _ in range(plane_slots - 1):
        slot = jnp.where(slot >= count_r, slot - count_r, slot)
    target = owner * plane_slots + slot
    dest_plane = dest_grid * plane_slots + dest_band
    wanted = jnp.where(target == dest_plane, 1.0, 0.0)
    head = jnp.concatenate(
        [head[:, :CORNER_AT], jnp.broadcast_to(corners[0:1, :], (devices, atoms_here)),
         jnp.broadcast_to(corners[1:2, :], (devices, atoms_here)),
         head[:, CORNER_AT + 2 * atoms_here : WANTED_AT], wanted], 1)
    send_ref[:, 0:1, :] = head.reshape(devices, 1, LANES)

    atoms = proj_ref.shape[1]
    total = None
    for part in range(proj_ref.shape[0]):
        proj_t = proj_ref[part]
        left = jnp.dot(proj_t, pick_rows_ref[...], precision=THREE_PASS, preferred_element_type=jnp.float32)
        right = jnp.dot(proj_t, pick_cols_ref[...], precision=THREE_PASS, preferred_element_type=jnp.float32)
        total = left * right if total is None else total + left * right
    total = total * (factor_ref[...] * occupied)
    pairs = total.shape[1]
    send_ref[:, 1 : 1 + atoms, :] = jnp.broadcast_to(total[None, :, :LANES], (devices, atoms, LANES))
    tail = pairs - LANES
    per_row = LANES // tail
    for atom in range(atoms):
        row = 1 + atoms + atom // per_row
        start = (atom % per_row) * tail
        send_ref[:, row : row + 1, start : start + tail] = jnp.broadcast_to(
            total[None, atom : atom + 1, LANES:], (devices, 1, tail)
        )


def on_device(
    coefficients,
    occupations,
    stick_cols,
    plane_counts,
    projections,
    pair_functions,
    atom_offsets,
    piece_owner,
    piece_slot,
):
    grid_devs = lax.axis_size("grid")
    band_devs = lax.axis_size("band")
    devices = grid_devs * band_devs
    _, _, stick_local, z_length = coefficients.shape
    stick_count = stick_local * grid_devs
    plane_slots = PLANE_SLOTS

    nproj = projections.shape[2]
    pair_rows, pair_cols = np.triu_indices(nproj)
    pairs = pair_rows.shape[0]
    pick_rows = jnp.asarray((np.arange(nproj)[:, None] == pair_rows[None, :]).astype(np.float32))
    pick_cols = jnp.asarray((np.arange(nproj)[:, None] == pair_cols[None, :]).astype(np.float32))
    factor = jnp.asarray(np.where(pair_rows == pair_cols, 1.0, 2.0).astype(np.float32)[None, :])
    piece_dev = piece_owner.shape[0]
    atoms_dev = atom_offsets.shape[0]
    assert 2 * stick_local <= CORNER_AT and 2 * atoms_dev <= CORNER_LANES
    assert WANTED_AT + piece_dev == LANES and LANES < pairs < 2 * LANES
    tail = pairs - LANES
    per_row = LANES // tail
    slab_rows = 1 + atoms_dev + -(-atoms_dev // per_row)
    send = pl.pallas_call(
        functools.partial(
            pack_kernel,
            grid_devs=grid_devs,
            band_devs=band_devs,
            plane_slots=plane_slots,
            z_length=z_length,
            scale=(z_length * stick_count) ** -0.5,
        ),
        out_shape=jax.ShapeDtypeStruct((devices, slab_rows, LANES), jnp.float32),
        in_specs=[SMEM_SPEC, SMEM_SPEC] + [VMEM_SPEC] * 8,
        out_specs=VMEM_SPEC,
    )(
        plane_counts,
        occupations,
        coefficients.reshape(2 * stick_local, z_length),
        jnp.transpose(projections, (0, 1, 3, 2)).reshape(2, atoms_dev, nproj),
        piece_owner.reshape(1, piece_dev),
        piece_slot.reshape(1, piece_dev),
        pick_rows,
        pick_cols,
        factor,
        atom_offsets.T,
    )
    got = lax.all_to_all(send, ("band", "grid"), 0, 0, tiled=True)
    got = got.reshape(band_devs, grid_devs, slab_rows * LANES)
    pair_parts = []
    for atom in range(atoms_dev):
        head_at = (1 + atom) * LANES
        tail_at = (1 + atoms_dev + atom // per_row) * LANES + (atom % per_row) * tail
        pair_parts.append(
            jnp.concatenate(
                [got[:, :, head_at : head_at + LANES], got[:, :, tail_at : tail_at + tail]], 2
            )
        )
    pair_rows_got = jnp.stack(pair_parts, 2)

    lre = got[:, :, 0:stick_local].reshape(band_devs, stick_count)
    lim = got[:, :, stick_local : 2 * stick_local].reshape(band_devs, stick_count)
    row_of = stick_cols // NX
    col_of = stick_cols % NX
    y_cos, y_sin = phase_table(jnp.arange(NY, dtype=jnp.int32), row_of, NY)
    stick_live = jnp.where(stick_cols < NX * NY, 1.0, 0.0)[None, :]
    along_y = jnp.concatenate([y_cos * stick_live, y_sin * stick_live], 1)
    x_cos, x_sin = phase_table(col_of, jnp.arange(NX, dtype=jnp.int32), NX)
    b_real = lre[:, :, None] * x_cos[None] - lim[:, :, None] * x_sin[None]
    b_imag = lre[:, :, None] * x_sin[None] + lim[:, :, None] * x_cos[None]
    rhs = jnp.concatenate(
        [jnp.concatenate([b_real, b_imag], 2), jnp.concatenate([-b_imag, b_real], 2)], 1
    )
    wave = jnp.einsum("yk,bkx->byx", along_y, rhs, precision=THREE_PASS)
    valence = jnp.sum(wave[:, :, :NX] ** 2 + wave[:, :, NX:] ** 2, 0)

    head_row = got[0, :, CORNER_AT : WANTED_AT + piece_dev]
    wanted_here = head_row[:, WANTED_AT - CORNER_AT :]
    pair_len = atoms_dev * pairs
    pair_sum = jnp.sum(pair_rows_got, 0).reshape(-1, pairs)
    corner = head_row[:, : 2 * atoms_dev].reshape(grid_devs, 2, atoms_dev)
    corner = jnp.transpose(corner, (0, 2, 1)).reshape(-1, 2)
    box_depth = pair_functions.shape[1]
    box_cells = pair_functions.shape[2]
    atoms = pair_sum.shape[0]
    flat_functions = pair_functions.reshape(pairs * box_depth, box_cells)
    mask = wanted_here.reshape(atoms, box_depth)
    weights = (pair_sum[:, :, None] * mask[:, None, :]).reshape(atoms, pairs * box_depth)
    boxes = jnp.dot(weights, flat_functions, precision=THREE_PASS).reshape(atoms, BY, BX)
    col_ids = jnp.arange(NX, dtype=jnp.float32)
    row_ids = jnp.arange(NY, dtype=jnp.float32)
    box_cols = jnp.arange(BX, dtype=jnp.float32)
    box_rows = jnp.arange(BY, dtype=jnp.float32)
    col_place = (
        jnp.mod(corner[:, 1:2, None] + box_cols[None, :, None], NX) == col_ids[None, None, :]
    ).astype(jnp.float32)
    widened = jnp.einsum("aij,ajx->aix", boxes, col_place, precision=THREE_PASS)
    row_place = (
        jnp.mod(corner[:, 0:1, None] + box_rows[None, :, None], NY) == row_ids[None, None, :]
    ).astype(jnp.float32)
    augment = jnp.einsum("aiy,aix->yx", row_place, widened, precision=THREE_PASS)
    density = valence + augment
    return density.reshape(1, 1, NY, NX)


def solution(mesh):
    in_specs = (
        P("band", None, "grid", None),
        P("band"),
        P(),
        P(),
        P("band", None, None, "grid"),
        P(),
        P("grid", None),
        P("grid", None),
        P("grid"),
    )
    out_specs = P("grid", "band", None, None)
    return jax.shard_map(
        on_device, mesh=mesh, in_specs=in_specs, out_specs=out_specs, check_vma=False
    )
```

```python
import functools
import math

import jax
import jax.numpy as jnp
import numpy as np
from jax import lax
from jax.experimental import pallas as pl
from jax.experimental.pallas import tpu as pltpu
from jax.sharding import PartitionSpec as P

NX = 256
NY = 256
PLANE_SLOTS = 4
BY = 16
BX = 16


PRECISE = lax.Precision.HIGHEST
THREE_PASS = lax.Precision.HIGH


def phase_table(left, right, length):
    phase_int = left[:, None] * right[None, :] % length
    phases = phase_int.astype(jnp.float32) * (2.0 * math.pi / length)
    return jnp.cos(phases), jnp.sin(phases)


SMEM_SPEC = pl.BlockSpec(memory_space=pltpu.SMEM)
CORNER_AT = 32
CORNER_LANES = 32
WANTED_AT = 64
LANES = 128
VMEM_SPEC = pl.BlockSpec(memory_space=pltpu.VMEM)


def pack_kernel(
    counts_ref,
    occ_ref,
    coef_ref,
    proj_ref,
    owner_ref,
    slot_ref,
    pick_rows_ref,
    pick_cols_ref,
    factor_ref,
    corner_ref,
    send_ref,
    *,
    grid_devs,
    band_devs,
    plane_slots,
    z_length,
    scale,
):
    devices = grid_devs * band_devs
    occupied = occ_ref[0]
    dest = lax.broadcasted_iota(jnp.int32, (devices, 1), 0)
    dest_grid = dest % grid_devs
    dest_band = dest // grid_devs
    owner = owner_ref[...]
    count_d = jnp.zeros((devices, 1), jnp.int32)
    offset_d = jnp.zeros((devices, 1), jnp.int32)
    count_r = jnp.zeros(owner.shape, jnp.int32)
    for g in range(grid_devs):
        count = counts_ref[g]
        count_d = count_d + jnp.where(dest_grid == g, count, 0)
        offset_d = offset_d + jnp.where(dest_grid > g, count, 0)
        count_r = count_r + jnp.where(owner == g, count, 0)
    live = dest_band < count_d
    plane_z = jnp.where(live, offset_d + dest_band, 0)
    weight = jnp.where(live, jnp.sqrt(occupied) * scale, 0.0)
    freq = lax.broadcasted_iota(jnp.int32, (1, z_length), 1)
    phases = ((plane_z * freq) % z_length).astype(jnp.float32) * (2.0 * math.pi / z_length)
    coef = coef_ref[...]
    half = coef.shape[0] // 2
    swapped = jnp.concatenate([-coef[half:], coef[:half]], 0)
    contract_last = (((1,), (1,)), ((), ()))
    lines = lax.dot_general(
        jnp.cos(phases), coef, contract_last, precision=PRECISE, preferred_element_type=jnp.float32
    ) + lax.dot_general(
        jnp.sin(phases), swapped, contract_last, precision=PRECISE, preferred_element_type=jnp.float32
    )
    send_ref[...] = jnp.zeros(send_ref.shape, jnp.float32)
    lines = lines * weight
    corners = corner_ref[...].astype(jnp.float32)
    atoms_here = corners.shape[1]
    head = jnp.zeros((devices, LANES), jnp.float32)
    head = jnp.concatenate([lines, head[:, lines.shape[1] :]], 1)

    slot = slot_ref[...]
    for _ in range(plane_slots - 1):
        slot = jnp.where(slot >= count_r, slot - count_r, slot)
    target = owner * plane_slots + slot
    dest_plane = dest_grid * plane_slots + dest_band
    wanted = jnp.where(target == dest_plane, 1.0, 0.0)
    head = jnp.concatenate(
        [head[:, :CORNER_AT], jnp.broadcast_to(corners[0:1, :], (devices, atoms_here)),
         jnp.broadcast_to(corners[1:2, :], (devices, atoms_here)),
         head[:, CORNER_AT + 2 * atoms_here : WANTED_AT], wanted], 1)
    send_ref[:, 0:1, :] = head.reshape(devices, 1, LANES)

    atoms = proj_ref.shape[1]
    total = None
    for part in range(proj_ref.shape[0]):
        proj_t = proj_ref[part]
        left = jnp.dot(proj_t, pick_rows_ref[...], precision=PRECISE, preferred_element_type=jnp.float32)
        right = jnp.dot(proj_t, pick_cols_ref[...], precision=PRECISE, preferred_element_type=jnp.float32)
        total = left * right if total is None else total + left * right
    total = total * (factor_ref[...] * occupied)
    pairs = total.shape[1]
    send_ref[:, 1 : 1 + atoms, :] = jnp.broadcast_to(total[None, :, :LANES], (devices, atoms, LANES))
    tail = pairs - LANES
    per_row = LANES // tail
    for atom in range(atoms):
        row = 1 + atoms + atom // per_row
        start = (atom % per_row) * tail
        send_ref[:, row : row + 1, start : start + tail] = jnp.broadcast_to(
            total[None, atom : atom + 1, LANES:], (devices, 1, tail)
        )


def on_device(
    coefficients,
    occupations,
    stick_cols,
    plane_counts,
    projections,
    pair_functions,
    atom_offsets,
    piece_owner,
    piece_slot,
):
    grid_devs = lax.axis_size("grid")
    band_devs = lax.axis_size("band")
    devices = grid_devs * band_devs
    _, _, stick_local, z_length = coefficients.shape
    stick_count = stick_local * grid_devs
    plane_slots = PLANE_SLOTS

    nproj = projections.shape[2]
    pair_rows, pair_cols = np.triu_indices(nproj)
    pairs = pair_rows.shape[0]
    pick_rows = jnp.asarray((np.arange(nproj)[:, None] == pair_rows[None, :]).astype(np.float32))
    pick_cols = jnp.asarray((np.arange(nproj)[:, None] == pair_cols[None, :]).astype(np.float32))
    factor = jnp.asarray(np.where(pair_rows == pair_cols, 1.0, 2.0).astype(np.float32)[None, :])
    piece_dev = piece_owner.shape[0]
    atoms_dev = atom_offsets.shape[0]
    assert 2 * stick_local <= CORNER_AT and 2 * atoms_dev <= CORNER_LANES
    assert WANTED_AT + piece_dev == LANES and LANES < pairs < 2 * LANES
    tail = pairs - LANES
    per_row = LANES // tail
    slab_rows = 1 + atoms_dev + -(-atoms_dev // per_row)
    send = pl.pallas_call(
        functools.partial(
            pack_kernel,
            grid_devs=grid_devs,
            band_devs=band_devs,
            plane_slots=plane_slots,
            z_length=z_length,
            scale=(z_length * stick_count) ** -0.5,
        ),
        out_shape=jax.ShapeDtypeStruct((devices, slab_rows, LANES), jnp.float32),
        in_specs=[SMEM_SPEC, SMEM_SPEC] + [VMEM_SPEC] * 8,
        out_specs=VMEM_SPEC,
    )(
        plane_counts,
        occupations,
        coefficients.reshape(2 * stick_local, z_length),
        jnp.transpose(projections, (0, 1, 3, 2)).reshape(2, atoms_dev, nproj),
        piece_owner.reshape(1, piece_dev),
        piece_slot.reshape(1, piece_dev),
        pick_rows,
        pick_cols,
        factor,
        atom_offsets.T,
    )
    got = lax.all_to_all(send, ("band", "grid"), 0, 0, tiled=True)
    got = got.reshape(band_devs, grid_devs, slab_rows * LANES)
    pair_parts = []
    for atom in range(atoms_dev):
        head_at = (1 + atom) * LANES
        tail_at = (1 + atoms_dev + atom // per_row) * LANES + (atom % per_row) * tail
        pair_parts.append(
            jnp.concatenate(
                [got[:, :, head_at : head_at + LANES], got[:, :, tail_at : tail_at + tail]], 2
            )
        )
    pair_rows_got = jnp.stack(pair_parts, 2)

    lre = got[:, :, 0:stick_local].reshape(band_devs, stick_count)
    lim = got[:, :, stick_local : 2 * stick_local].reshape(band_devs, stick_count)
    row_of = stick_cols // NX
    col_of = stick_cols % NX
    y_cos, y_sin = phase_table(jnp.arange(NY, dtype=jnp.int32), row_of, NY)
    stick_live = jnp.where(stick_cols < NX * NY, 1.0, 0.0)[None, :]
    along_y = jnp.concatenate([y_cos * stick_live, y_sin * stick_live], 1)
    x_cos, x_sin = phase_table(col_of, jnp.arange(NX, dtype=jnp.int32), NX)
    rhs = jnp.concatenate(
        [jnp.concatenate([x_cos, x_sin], 1), jnp.concatenate([-x_sin, x_cos], 1)], 0
    )
    y_c = along_y[:, :stick_count]
    y_s = along_y[:, stick_count:]
    lhs = jnp.concatenate(
        [y_c[None] * lre[:, None, :] - y_s[None] * lim[:, None, :],
         y_c[None] * lim[:, None, :] + y_s[None] * lre[:, None, :]], 2
    )
    wave = jnp.einsum("byk,kx->byx", lhs, rhs, precision=THREE_PASS)
    valence = jnp.sum(wave[:, :, :NX] ** 2 + wave[:, :, NX:] ** 2, 0)

    head_row = got[0, :, CORNER_AT : WANTED_AT + piece_dev]
    wanted_here = head_row[:, WANTED_AT - CORNER_AT :]
    pair_len = atoms_dev * pairs
    pair_sum = jnp.sum(pair_rows_got, 0).reshape(-1, pairs)
    corner = head_row[:, : 2 * atoms_dev].reshape(grid_devs, 2, atoms_dev)
    corner = jnp.transpose(corner, (0, 2, 1)).reshape(-1, 2)
    box_depth = pair_functions.shape[1]
    box_cells = pair_functions.shape[2]
    atoms = pair_sum.shape[0]
    flat_functions = pair_functions.reshape(pairs * box_depth, box_cells)
    mask = wanted_here.reshape(atoms, box_depth)
    weights = (pair_sum[:, :, None] * mask[:, None, :]).reshape(atoms, pairs * box_depth)
    boxes = jnp.dot(weights, flat_functions, precision=THREE_PASS).reshape(atoms, BY, BX)
    col_ids = jnp.arange(NX, dtype=jnp.float32)
    row_ids = jnp.arange(NY, dtype=jnp.float32)
    box_cols = jnp.arange(BX, dtype=jnp.float32)
    box_rows = jnp.arange(BY, dtype=jnp.float32)
    col_place = (
        jnp.mod(corner[:, 1:2, None] + box_cols[None, :, None], NX) == col_ids[None, None, :]
    ).astype(jnp.float32)
    widened = jnp.einsum("aij,ajx->aix", boxes, col_place, precision=THREE_PASS)
    row_place = (
        jnp.mod(corner[:, 0:1, None] + box_rows[None, :, None], NY) == row_ids[None, None, :]
    ).astype(jnp.float32)
    augment = jnp.einsum("aiy,aix->yx", row_place, widened, precision=THREE_PASS)
    density = valence + augment
    return density.reshape(1, 1, NY, NX)


def solution(mesh):
    in_specs = (
        P("band", None, "grid", None),
        P("band"),
        P(),
        P(),
        P("band", None, None, "grid"),
        P(),
        P("grid", None),
        P("grid", None),
        P("grid"),
    )
    out_specs = P("grid", "band", None, None)
    return jax.shard_map(
        on_device, mesh=mesh, in_specs=in_specs, out_specs=out_specs, check_vma=False
    )
```
